256 devices in a mesh: nodes: 64 (over x, z, core), heads: 4 (over y).
Axes of the slice: x: 4, y: 4, z: 8, core: 2. Of those that a mesh axis runs over, the one named last changes fastest.
Arguments:
- feats: bfloat16 [65536, 512], P('nodes'), may hold values from -6 to 6
- w_query: bfloat16 [512, 512], P(None, 'heads'), may hold values from -0.25 to 0.25
- w_key: bfloat16 [512, 512], P(None, 'heads'), may hold values from -0.25 to 0.25
- w_value: bfloat16 [512, 512], P(None, 'heads'), may hold values from -0.25 to 0.25
- w_out: bfloat16 [512, 512], P('heads'), may hold values from -6 to 6
- head_scale: float32 [8], P('heads'), may hold values from 2 to 10
- nbr_owner: int32 [512, 4], P('nodes'), may hold values from 0 to 63, all different within a row; in each aligned block of 8 rows (0 to 7, 8 to 15, ...) at most 2 rows name the same one
- nbr_local: int32 [512, 4], P('nodes'), may hold values from 0 to 7
- slot_valid: int32 [512, 4], P('nodes'), may hold values 0 or 1
Outputs:
- mixed: bfloat16 [65536, 512], P('nodes', 'heads')
The draws below stay inside these ranges and needn't reach their ends.
Inputs may be any that keep to these rules, and one draw needn't show every extreme that they name: `nbr_owner`: the 4 owners listed for one query block are distinct. Among the query blocks of one index of nodes, no owner is listed more than 2 times, and 2 is reached.
All inputs are finite; a program needn't handle non-finite values. No bound on the sum of `slot_valid` on one device may be relied on, other than what follows from the above.
Results may differ from the reference program's by a relative error of at most 0.012.
Values may be sent and summed in bfloat16 or wider, within the bound.
No kernel may reach another device: no remote copies, remote signals or barrier semaphores. Data moves between devices by JAX's collectives and lax.ppermute only.
A program may use at most 128 MiB of HBM per device.

```python
import math
import jax
import jax.numpy as jnp
import numpy as np
from jax import lax

D = 512
H = 8
HD = 64
BLK = 128
NB = 4
BLK_DEV = 8
QBLOCKS = 512
NODES = 65536
CAP = 2
N_NODES = 64


def place_ends(result, stream_key, low, high):
    longest = result.shape.index(max(result.shape))
    spots = []
    for shift in (0, 1):
        where = [jax.random.randint(jax.random.fold_in(stream_key, axis), (), 0, length) for axis, length in enumerate(result.shape)]
        where[longest] = (where[longest] + shift) % result.shape[longest]
        spots.append(tuple(where))
    return result.at[spots[0]].set(low).at[spots[1]].set(high)


def shard_levels(rng, dims, cuts, smallest, top_value):
    gain, own = 1.0, jax.random.fold_in(rng, 6)
    for position, shards_of in cuts:
        heights = jnp.exp(jax.random.uniform(jax.random.fold_in(own, position), (shards_of,), jnp.float32, smallest / len(cuts), top_value / len(cuts)))
        gain = gain * jnp.repeat(heights, dims[position] // shards_of).reshape([-1 if axis == position else 1 for axis in range(len(dims))])
    return gain


def shared_out(rng, own, number, rows, number_of, top, most, lean):
    ranking = jax.random.permutation(rng, number_of)
    packed, common = portions_of(number_of, rows * top, most, lean, True), portions_of(number_of, rows * top, most, lean, False)
    places = jnp.arange(number_of)

    def named(sizes, rotation):
        used = int((sizes > 0).sum())
        fixed = max(1, used // 4)
        passed = fixed + (places - fixed + rotation * (used - fixed)) % max(1, number_of - fixed)
        return jnp.zeros((number_of,), jnp.int32).at[ranking[jnp.where(places < fixed, places, passed)]].set(jnp.asarray(sizes, jnp.int32))

    sizes = jnp.where(number % 4 == 0, named(packed, number // 4), named(common, number - number // 4 - 1))
    mixed = jax.random.permutation(jax.random.fold_in(own, 3), number_of)
    source_of, sink = mixed[0:number_of // 2 * 2:2], mixed[1:number_of // 2 * 2:2]
    room = jnp.minimum(sizes[source_of] - 1, most - sizes[sink]) // 2
    room = jnp.where((source_of == ranking[0]) | (sink == ranking[0]) | (sizes[sink] == 0), 0, jnp.maximum(room, 0))
    passed = jax.random.randint(jax.random.fold_in(own, 4), (number_of // 2,), 0, 1 << 20) % (room + 1)
    sizes = sizes.at[source_of].add(-passed).at[sink].add(passed)
    members = jnp.searchsorted(jnp.cumsum(sizes), jnp.arange(rows * top), side="right").astype(jnp.int32)
    grid = members.reshape(top, rows).T
    grid = grid[jax.random.permutation(jax.random.fold_in(own, 1), rows)]
    rotation = jax.random.randint(jax.random.fold_in(own, 2), (rows, 1), 0, top)
    return jnp.take_along_axis(grid, (jnp.arange(top)[None, :] + rotation) % top, axis=1)


def portions_of(number_of, total, most, lean, full):
    weights = [(1 << 20) // math.isqrt(rank ** lean) + 1 for rank in range(1, number_of + 1)]
    largest = most if full else min(most, max(-(-total // number_of), total * weights[0] // sum(weights)))
    least = 1 if total - largest >= number_of - 1 else 0
    given, spare = [largest] + [least] * (number_of - 1), total - largest - least * (number_of - 1)
    while spare > 0:
        candidates = [i for i in range(1, number_of) if given[i] < largest] or [i for i in range(1, number_of) if given[i] < most]
        pool, remaining = sum([weights[i] for i in candidates]), spare
        for i in candidates:
            addition = min(most - given[i], max(1, remaining * weights[i] // pool), spare)
            given[i] = given[i] + addition
            spare = spare - addition
    return np.array(given)


def scatter_about(stream_key, extent, scale, most, split=(), kind=jnp.bfloat16):
    array = scale * jax.random.normal(stream_key, extent, jnp.float32)
    if split:
        array = array * shard_levels(stream_key, extent, split, -0.22, 0.18)
    return jnp.clip(array, -most, most).astype(kind)


def setup_inputs(seed: int = 0) -> dict:
    splits = jax.random.split(jax.random.key(seed), 10)
    feats = scatter_about(splits[0], (NODES, D), 1.0, 6.0, ((0, 64),))
    w_query = scatter_about(splits[1], (D, D), D ** -0.5, 0.25, ((1, 4),))
    w_key = scatter_about(splits[2], (D, D), D ** -0.5, 0.25, ((1, 4),))
    w_value = scatter_about(splits[3], (D, D), D ** -0.5, 0.25, ((1, 4),))
    w_out = scatter_about(splits[4], (D, D), 1.0, 6.0, ((0, 4),))
    head_scale = jnp.clip(jnp.exp(math.log(10.0) - 1.609438 * jax.random.uniform(splits[5], (H,), jnp.float32) ** shard_levels(splits[5], (H,), ((0, 4),), -0.2, 0.2)), 2.0, 10.0)
    nbr_owner_keys = jax.random.split(jax.random.fold_in(splits[6], 1), QBLOCKS // BLK_DEV)
    nbr_owner_turns = jax.random.permutation(jax.random.fold_in(splits[6], 3), QBLOCKS // BLK_DEV)
    nbr_owner = jax.vmap(lambda own, number: shared_out(jax.random.fold_in(splits[6], 2), own, number, BLK_DEV, N_NODES, NB, CAP, 2))(nbr_owner_keys, nbr_owner_turns).reshape((QBLOCKS, NB))
    nbr_local = place_ends(jax.random.randint(splits[7], (QBLOCKS, NB), 0, BLK_DEV), jax.random.fold_in(splits[7], 1), 0, BLK_DEV - 1).astype(jnp.int32)
    slot_valid = place_ends((jax.random.randint(splits[8], (QBLOCKS, NB), 0, 4) < 3).astype(jnp.int32), jax.random.fold_in(splits[8], 1), 0, 1)
    return dict(feats=feats, w_query=w_query, w_key=w_key, w_value=w_value, w_out=w_out, head_scale=head_scale, nbr_owner=nbr_owner, nbr_local=nbr_local, slot_valid=slot_valid)


def unit_rows(values, count):
    shaped = values.reshape(values.shape[0], count, -1)
    total = lax.optimization_barrier(jnp.sum(shaped * shaped, axis=-1, keepdims=True))
    return (shaped * lax.rsqrt(total + 1e-06)).astype(jnp.bfloat16)

def rounded(values):
    return lax.optimization_barrier(values.astype(jnp.bfloat16)).astype(jnp.float32)

def reference(feats, w_query, w_key, w_value, w_out, head_scale, nbr_owner, nbr_local, slot_valid):
    query_n = unit_rows(jnp.dot(feats, w_query, preferred_element_type=jnp.float32), H)
    key_n = unit_rows(jnp.dot(feats, w_key, preferred_element_type=jnp.float32), H)
    value_b = jnp.dot(feats, w_value, preferred_element_type=jnp.float32).astype(jnp.bfloat16).reshape(NODES, H, HD)
    key_blocks = key_n.reshape(QBLOCKS, BLK, H, HD)
    value_blocks = value_b.reshape(QBLOCKS, BLK, H, HD)
    own_ids = jnp.arange(QBLOCKS, dtype=jnp.int32)[:, None]
    slot_ids = jnp.concatenate([own_ids, (nbr_owner * BLK_DEV + nbr_local).astype(jnp.int32)], axis=1)
    live = jnp.concatenate([jnp.ones((QBLOCKS, 1), jnp.float32), slot_valid.astype(jnp.float32)], axis=1)
    query_groups = query_n.reshape(N_NODES, BLK_DEV, BLK, H, HD)
    id_groups = slot_ids.reshape(N_NODES, BLK_DEV, NB + 1)
    live_groups = live.reshape(N_NODES, BLK_DEV, NB + 1)

    def group(items):
        queries, idents, alive = items
        keys = key_blocks[idents].astype(jnp.float32)
        values = value_blocks[idents].astype(jnp.float32)
        scores = jnp.einsum('gqhd,gskhd->gshqk', queries.astype(jnp.float32), keys)
        weight = jnp.exp(head_scale[None, None, :, None, None] * (scores - 1.0)) * alive[:, :, None, None, None]
        denom = lax.optimization_barrier(jnp.sum(rounded(lax.optimization_barrier(jnp.sum(weight, axis=-1))), axis=1))
        numer = jnp.einsum('gshqk,gskhd->gsqhd', rounded(weight), values)
        numer = lax.optimization_barrier(jnp.sum(rounded(numer), axis=1))
        return (numer / jnp.transpose(denom, (0, 2, 1))[..., None]).astype(jnp.bfloat16)
    attn = lax.map(group, (query_groups, id_groups, live_groups)).reshape(NODES, D)
    return jnp.dot(attn, w_out, preferred_element_type=jnp.float32).astype(jnp.bfloat16)
```

```python
import functools

import jax
import jax.numpy as jnp
from jax import lax
from jax.experimental import pallas as pl
from jax.experimental.pallas import tpu as pltpu
from jax.sharding import PartitionSpec as P


def unit_rows(values, count):
    shaped = values.reshape(values.shape[0], count, -1)
    total = jnp.sum(shaped * shaped, axis=-1, keepdims=True)
    return (shaped * lax.rsqrt(total + 1e-06)).astype(jnp.bfloat16).reshape(values.shape)


def tile_kernel(pick_ref, live_ref, scale_ref, q_ref, kv_ref, num_ref, den_ref, *, count):
    t = pl.program_id(0)
    feat = q_ref.shape[-1]
    hd = feat // count

    @pl.when(live_ref[t] > 0)
    def _():
        q = q_ref[0]
        kv = kv_ref[0]
        for h in range(count):
            qh = q[:, h * hd:(h + 1) * hd]
            kh = kv[:, h * hd:(h + 1) * hd]
            vh = kv[:, feat + h * hd:feat + (h + 1) * hd]
            s = lax.dot_general(
                qh, kh, (((1,), (1,)), ((), ())), preferred_element_type=jnp.float32
            )
            w = jnp.exp(scale_ref[h] * (s - 1.0))
            den_ref[0, :, h:h + 1] = jnp.sum(w, axis=1, keepdims=True)
            num = jnp.dot(w.astype(jnp.bfloat16), vh, preferred_element_type=jnp.float32)
            num_ref[0, :, h * hd:(h + 1) * hd] = num.astype(jnp.bfloat16)

    @pl.when(live_ref[t] == 0)
    def _():
        num_ref[...] = jnp.zeros(num_ref.shape, num_ref.dtype)
        den_ref[...] = jnp.zeros(den_ref.shape, den_ref.dtype)


def run_tiles(query_tiles, block_pairs, pick, live, scales):
    tiles, width, feat = query_tiles.shape
    count = scales.shape[0]
    grid_spec = pltpu.PrefetchScalarGridSpec(
        num_scalar_prefetch=2,
        grid=(tiles,),
        in_specs=[
            pl.BlockSpec(memory_space=pltpu.SMEM),
            pl.BlockSpec((1, width, feat), lambda t, pick, live: (t, 0, 0)),
            pl.BlockSpec((1, width, 2 * feat), lambda t, pick, live: (pick[t], 0, 0)),
        ],
        out_specs=[
            pl.BlockSpec((1, width, feat), lambda t, pick, live: (t, 0, 0)),
            pl.BlockSpec((1, width, count), lambda t, pick, live: (t, 0, 0)),
        ],
    )
    numer, denom = pl.pallas_call(
        functools.partial(tile_kernel, count=count),
        grid_spec=grid_spec,
        out_shape=[
            jax.ShapeDtypeStruct((tiles, width, feat), jnp.bfloat16),
            jax.ShapeDtypeStruct((tiles, width, count), jnp.float32),
        ],
    )(pick, live, scales, query_tiles, block_pairs)
    return numer, denom.astype(jnp.bfloat16)


def body(feats, w_query, w_key, w_value, w_out, head_scale, nbr_owner, nbr_local, slot_valid):
    rows = feats.shape[0]
    feat = w_query.shape[1]
    count = head_scale.shape[0]
    nblocks, slots = nbr_owner.shape
    width = rows // nblocks
    devices = lax.axis_size("nodes")
    capacity = max(2, min(nblocks // 2, 3 * nblocks * slots // (2 * devices)))
    tile_count = devices * capacity
    query_n = unit_rows(jnp.dot(feats, w_query, preferred_element_type=jnp.float32), count)
    key_n = unit_rows(jnp.dot(feats, w_key, preferred_element_type=jnp.float32), count)
    value_b = jnp.dot(feats, w_value, preferred_element_type=jnp.float32).astype(jnp.bfloat16)
    query_block_rows = query_n.reshape(nblocks, width, feat)
    block_pair_list = jnp.concatenate([key_n, value_b], axis=1).reshape(nblocks, width, 2 * feat)
    owners = nbr_owner.reshape(-1)
    pairs = owners.shape[0]
    pair_block = jnp.arange(pairs, dtype=jnp.int32) // slots
    owner_hot = (owners[:, None] == jnp.arange(devices, dtype=jnp.int32)[None, :]).astype(jnp.int32)
    rank = jnp.sum(jnp.cumsum(owner_hot, axis=0) * owner_hot, axis=1) - 1
    target = owners * capacity + rank
    place = (target[:, None] == jnp.arange(tile_count, dtype=jnp.int32)[None, :]).astype(jnp.int32)
    wanted = jnp.where(slot_valid.reshape(-1) > 0, nbr_local.reshape(-1), -1)
    request = jnp.sum(place * (wanted[:, None] + 1), axis=0) - 1
    block_hot = (pair_block[:, None] == jnp.arange(nblocks, dtype=jnp.int32)[None, :]).astype(
        jnp.float32
    )
    selector_onehot = jnp.dot(place.T.astype(jnp.float32), block_hot).astype(jnp.bfloat16)
    query_outgoing = jnp.dot(
        selector_onehot,
        query_block_rows.reshape(nblocks, width * feat),
        preferred_element_type=jnp.float32,
    ).astype(jnp.bfloat16)
    asked = lax.all_to_all(
        request.reshape(devices, capacity), "nodes", split_axis=0, concat_axis=0, tiled=True
    ).reshape(-1)
    query_in = lax.all_to_all(
        query_outgoing.reshape(devices, capacity * width, feat),
        "nodes",
        split_axis=0,
        concat_axis=0,
        tiled=True,
    )
    self_numer, self_denom = run_tiles(
        query_block_rows,
        block_pair_list,
        jnp.arange(nblocks, dtype=jnp.int32),
        jnp.ones((nblocks,), jnp.int32),
        head_scale,
    )
    live_in = (asked >= 0).astype(jnp.int32)
    pick_in = jnp.clip(asked, 0, nblocks - 1)
    numer, denom = run_tiles(
        query_in.reshape(tile_count, width, feat), block_pair_list, pick_in, live_in, head_scale
    )
    numer = lax.all_to_all(
        numer.reshape(devices, capacity * width, feat),
        "nodes",
        split_axis=0,
        concat_axis=0,
        tiled=True,
    )
    denom = lax.all_to_all(
        denom.reshape(devices, capacity * width, count),
        "nodes",
        split_axis=0,
        concat_axis=0,
        tiled=True,
    )
    numer_total = self_numer.astype(jnp.float32).reshape(nblocks, width * feat) + jnp.dot(
        selector_onehot.T,
        numer.reshape(tile_count, width * feat),
        preferred_element_type=jnp.float32,
    )
    denominator_overall = self_denom.astype(jnp.float32).reshape(nblocks, width * count) + jnp.dot(
        selector_onehot.T,
        denom.reshape(tile_count, width * count),
        preferred_element_type=jnp.float32,
    )
    attn = numer_total.reshape(rows, count, feat // count) / denominator_overall.reshape(
        rows, count, 1
    )
    attn = attn.astype(jnp.bfloat16).reshape(rows, feat)
    attn_all = lax.all_gather(attn, "heads", axis=1, tiled=True)
    w_out_all = lax.all_gather(w_out, "heads", axis=0, tiled=True)
    cols = w_out.shape[0]
    w_cols = lax.dynamic_slice_in_dim(w_out_all, lax.axis_index("heads") * cols, cols, axis=1)
    return jnp.dot(attn_all, w_cols, preferred_element_type=jnp.float32).astype(jnp.bfloat16)


def solution(mesh):
    placed = (
        P("nodes", None),
        P(None, "heads"),
        P(None, "heads"),
        P(None, "heads"),
        P("heads", None),
        P("heads"),
        P("nodes", None),
        P("nodes", None),
        P("nodes", None),
    )
    return jax.shard_map(
        body, mesh=mesh, in_specs=placed, out_specs=P("nodes", "heads"), check_vma=False
    )
```

```python
import functools

import jax
import jax.numpy as jnp
from jax import lax
from jax.experimental import pallas as pl
from jax.experimental.pallas import tpu as pltpu
from jax.sharding import PartitionSpec as P


def unit_rows(values, count):
    shaped = values.reshape(values.shape[0], count, -1)
    total = jnp.sum(shaped * shaped, axis=-1, keepdims=True)
    return (shaped * lax.rsqrt(total + 1e-06)).astype(jnp.bfloat16).reshape(values.shape)


def tile_kernel(pick_ref, live_ref, scale_ref, q_ref, kv_ref, num_ref, den_ref, *, count, group):
    g = pl.program_id(0)
    width, feat = q_ref.shape[1], q_ref.shape[2]
    hd = feat // count
    ones = jnp.ones((8, width), jnp.bfloat16)
    nt = (((1,), (1,)), ((), ()))
    for i in range(group):
        t = g * group + i

        @pl.when(live_ref[t] > 0)
        def _():
            q = q_ref[i]
            kv = kv_ref[pick_ref[t]]
            for h in range(count):
                qh = q[:, h * hd:(h + 1) * hd]
                kh = kv[:, h * hd:(h + 1) * hd]
                vh = kv[:, feat + h * hd:feat + (h + 1) * hd]
                s = lax.dot_general(qh, kh, nt, preferred_element_type=jnp.float32)
                w = jnp.exp(scale_ref[h] * (s - 1.0))
                w_hi = w.astype(jnp.bfloat16)
                w_lo = (w - w_hi.astype(jnp.float32)).astype(jnp.bfloat16)
                den = lax.dot_general(ones, w_hi, nt, preferred_element_type=jnp.float32)
                den = den + lax.dot_general(ones, w_lo, nt, preferred_element_type=jnp.float32)
                den_ref[i:i + 1, h * width:(h + 1) * width] = den[0:1]
                num = jnp.dot(w_hi, vh, preferred_element_type=jnp.float32)
                num_ref[i, :, h * hd:(h + 1) * hd] = num.astype(jnp.bfloat16)

        @pl.when(live_ref[t] == 0)
        def _():
            num_ref[i] = jnp.zeros((width, feat), num_ref.dtype)
            den_ref[i:i + 1, :] = jnp.zeros((1, count * width), den_ref.dtype)


def run_tiles(query_tiles, block_pairs, pick, live, scales):
    tiles, width, feat = query_tiles.shape
    count = scales.shape[0]
    group = 8
    nblocks = block_pairs.shape[0]
    grid_spec = pltpu.PrefetchScalarGridSpec(
        num_scalar_prefetch=2,
        grid=(tiles // group,),
        in_specs=[
            pl.BlockSpec(memory_space=pltpu.SMEM),
            pl.BlockSpec((group, width, feat), lambda g, pick, live: (g, 0, 0)),
            pl.BlockSpec((nblocks, width, 2 * feat), lambda g, pick, live: (0, 0, 0)),
        ],
        out_specs=[
            pl.BlockSpec((group, width, feat), lambda g, pick, live: (g, 0, 0)),
            pl.BlockSpec((group, count * width), lambda g, pick, live: (g, 0)),
        ],
    )
    numer, denom = pl.pallas_call(
        functools.partial(tile_kernel, count=count, group=group),
        grid_spec=grid_spec,
        out_shape=[
            jax.ShapeDtypeStruct((tiles, width, feat), jnp.bfloat16),
            jax.ShapeDtypeStruct((tiles, count * width), jnp.float32),
        ],
    )(pick, live, scales, query_tiles, block_pairs)
    return numer, denom.astype(jnp.bfloat16)


def body(feats, w_query, w_key, w_value, w_out, head_scale, nbr_owner, nbr_local, slot_valid):
    rows = feats.shape[0]
    feat = w_query.shape[1]
    count = head_scale.shape[0]
    nblocks, slots = nbr_owner.shape
    width = rows // nblocks
    devices = lax.axis_size("nodes")
    capacity = max(2, min(nblocks // 2, 3 * nblocks * slots // (2 * devices)))
    tile_count = devices * capacity
    query_n = unit_rows(jnp.dot(feats, w_query, preferred_element_type=jnp.float32), count)
    key_n = unit_rows(jnp.dot(feats, w_key, preferred_element_type=jnp.float32), count)
    value_b = jnp.dot(feats, w_value, preferred_element_type=jnp.float32).astype(jnp.bfloat16)
    query_block_rows = query_n.reshape(nblocks, width, feat)
    block_pair_list = jnp.concatenate([key_n, value_b], axis=1).reshape(nblocks, width, 2 * feat)
    owners = nbr_owner.reshape(-1)
    pairs = owners.shape[0]
    pair_block = jnp.arange(pairs, dtype=jnp.int32) // slots
    owner_hot = (owners[:, None] == jnp.arange(devices, dtype=jnp.int32)[None, :]).astype(jnp.int32)
    rank = jnp.sum(jnp.cumsum(owner_hot, axis=0) * owner_hot, axis=1) - 1
    target = owners * capacity + rank
    place = (target[:, None] == jnp.arange(tile_count, dtype=jnp.int32)[None, :]).astype(jnp.int32)
    wanted = jnp.where(slot_valid.reshape(-1) > 0, nbr_local.reshape(-1), -1)
    request = jnp.sum(place * (wanted[:, None] + 1), axis=0) - 1
    block_hot = (pair_block[:, None] == jnp.arange(nblocks, dtype=jnp.int32)[None, :]).astype(
        jnp.float32
    )
    selector_onehot = jnp.dot(place.T.astype(jnp.float32), block_hot).astype(jnp.bfloat16)
    query_outgoing = jnp.einsum(
        "cm,mqk->cqk", selector_onehot, query_block_rows, preferred_element_type=jnp.float32
    ).astype(jnp.bfloat16)
    asked = lax.all_to_all(
        request.reshape(devices, capacity), "nodes", split_axis=0, concat_axis=0, tiled=True
    ).reshape(-1)
    query_in = lax.all_to_all(
        query_outgoing.reshape(devices, capacity * width, feat),
        "nodes",
        split_axis=0,
        concat_axis=0,
        tiled=True,
    )
    self_numer, self_denom = run_tiles(
        query_block_rows,
        block_pair_list,
        jnp.arange(nblocks, dtype=jnp.int32),
        jnp.ones((nblocks,), jnp.int32),
        head_scale,
    )
    live_in = (asked >= 0).astype(jnp.int32)
    pick_in = jnp.clip(asked, 0, nblocks - 1)
    numer, denom = run_tiles(
        query_in.reshape(tile_count, width, feat), block_pair_list, pick_in, live_in, head_scale
    )
    numer = lax.all_to_all(
        numer.reshape(devices, capacity * width, feat),
        "nodes",
        split_axis=0,
        concat_axis=0,
        tiled=True,
    )
    denom = lax.all_to_all(
        denom.reshape(devices, capacity * count * width),
        "nodes",
        split_axis=0,
        concat_axis=0,
        tiled=True,
    )
    numer_total = self_numer.astype(jnp.float32) + jnp.einsum(
        "uq,upl->qpl",
        selector_onehot,
        numer.reshape(tile_count, width, feat),
        preferred_element_type=jnp.float32,
    )
    denominator_overall = self_denom.astype(jnp.float32) + jnp.einsum(
        "uq,ul->ql",
        selector_onehot,
        denom.reshape(tile_count, count * width),
        preferred_element_type=jnp.float32,
    )
    den_rows = jnp.transpose(denominator_overall.reshape(nblocks, count, width), (0, 2, 1))
    attn = numer_total.reshape(nblocks, width, count, feat // count) / den_rows[..., None]
    attn = attn.astype(jnp.bfloat16).reshape(rows, feat)
    attn_all = lax.all_gather(attn, "heads", axis=1, tiled=True)
    cols = w_out.shape[0]
    w_out_t = lax.all_gather(w_out.T, "heads", axis=1, tiled=True)
    w_cols = lax.dynamic_slice_in_dim(w_out_t, lax.axis_index("heads") * cols, cols, axis=0).T
    return jnp.dot(attn_all, w_cols, preferred_element_type=jnp.float32).astype(jnp.bfloat16)


def solution(mesh):
    placed = (
        P("nodes", None),
        P(None, "heads"),
        P(None, "heads"),
        P(None, "heads"),
        P("heads", None),
        P("heads"),
        P("nodes", None),
        P("nodes", None),
        P("nodes", None),
    )
    return jax.shard_map(
        body, mesh=mesh, in_specs=placed, out_specs=P("nodes", "heads"), check_vma=False
    )
```

```python
import functools

import jax
import jax.numpy as jnp
from jax import lax
from jax.experimental import pallas as pl
from jax.experimental.pallas import tpu as pltpu
from jax.sharding import PartitionSpec as P


def unit_rows(values, count):
    shaped = values.reshape(values.shape[0], count, -1)
    total = jnp.sum(shaped * shaped, axis=-1, keepdims=True)
    return (shaped * lax.rsqrt(total + 1e-06)).astype(jnp.bfloat16).reshape(values.shape)


def tile_kernel(pick_ref, live_ref, scale_ref, q_ref, kv_ref, out_ref, den_scr, *, count, capacity):
    g = pl.program_id(0)
    width, feat = q_ref.shape[1], q_ref.shape[2]
    group = q_ref.shape[0]
    hd = feat // count
    ones = jnp.ones((8, width), jnp.bfloat16)
    nt = (((1,), (1,)), ((), ()))
    for i in range(group):
        t = g * group + i
        dest, slot = i // capacity, i % capacity

        @pl.when(live_ref[t] > 0)
        def _():
            q = q_ref[i]
            kv = kv_ref[pick_ref[t]]
            for h in range(count):
                qh = q[:, h * hd:(h + 1) * hd]
                kh = kv[:, h * hd:(h + 1) * hd]
                vh = kv[:, feat + h * hd:feat + (h + 1) * hd]
                s = lax.dot_general(qh, kh, nt, preferred_element_type=jnp.float32)
                w = jnp.exp(scale_ref[h] * (s - 1.0))
                w_hi = w.astype(jnp.bfloat16)
                w_lo = (w - w_hi.astype(jnp.float32)).astype(jnp.bfloat16)
                den = lax.dot_general(ones, w_hi, nt, preferred_element_type=jnp.float32)
                den = den + lax.dot_general(ones, w_lo, nt, preferred_element_type=jnp.float32)
                den_scr[i * count + h:i * count + h + 1, :] = den[0:1]
                num = jnp.dot(w_hi, vh, preferred_element_type=jnp.float32)
                out_ref[dest, slot * width:(slot + 1) * width, h * hd:(h + 1) * hd] = num.astype(
                    jnp.bfloat16
                )

        @pl.when(live_ref[t] == 0)
        def _():
            out_ref[dest, slot * width:(slot + 1) * width, :] = jnp.zeros((width, feat), out_ref.dtype)
            den_scr[i * count:(i + 1) * count, :] = jnp.zeros((count, width), den_scr.dtype)

    per = capacity * count
    extra = out_ref.shape[1] - capacity * width
    for d in range(group // capacity):
        rows = den_scr[d * per:(d + 1) * per, :]
        block = jnp.concatenate([rows, jnp.zeros((extra - per, width), rows.dtype)], axis=0)
        out_ref[d, capacity * width:, :] = block.astype(out_ref.dtype)


def run_tiles(query_tiles, block_pairs, pick, live, scales, capacity):
    tiles, width, feat = query_tiles.shape
    count = scales.shape[0]
    group = 8
    nblocks = block_pairs.shape[0]
    extra = 16
    rows_out = capacity * width + extra
    grid_spec = pltpu.PrefetchScalarGridSpec(
        num_scalar_prefetch=2,
        grid=(tiles // group,),
        in_specs=[
            pl.BlockSpec(memory_space=pltpu.SMEM),
            pl.BlockSpec((group, width, feat), lambda g, pick, live: (g, 0, 0)),
            pl.BlockSpec((nblocks, width, 2 * feat), lambda g, pick, live: (0, 0, 0)),
        ],
        out_specs=pl.BlockSpec((group // capacity, rows_out, feat), lambda g, pick, live: (g, 0, 0)),
        scratch_shapes=[pltpu.VMEM((group * count, width), jnp.float32)],
    )
    return pl.pallas_call(
        functools.partial(tile_kernel, count=count, capacity=capacity),
        grid_spec=grid_spec,
        out_shape=jax.ShapeDtypeStruct((tiles // capacity, rows_out, feat), jnp.bfloat16),
    )(pick, live, scales, query_tiles, block_pairs)


def split_result(result, capacity, width, count):
    dests, _, feat = result.shape
    numer = result[:, :capacity * width, :].reshape(dests * capacity, width, feat)
    denom = result[:, capacity * width:capacity * width + capacity * count, :]
    return numer, denom.reshape(dests * capacity, count * width)


def body(feats, w_query, w_key, w_value, w_out, head_scale, nbr_owner, nbr_local, slot_valid):
    rows = feats.shape[0]
    feat = w_query.shape[1]
    count = head_scale.shape[0]
    nblocks, slots = nbr_owner.shape
    width = rows // nblocks
    devices = lax.axis_size("nodes")
    capacity = max(2, min(nblocks // 2, 3 * nblocks * slots // (2 * devices)))
    tile_count = devices * capacity
    query_n = unit_rows(jnp.dot(feats, w_query, preferred_element_type=jnp.float32), count)
    key_n = unit_rows(jnp.dot(feats, w_key, preferred_element_type=jnp.float32), count)
    value_b = jnp.dot(feats, w_value, preferred_element_type=jnp.float32).astype(jnp.bfloat16)
    query_block_rows = query_n.reshape(nblocks, width, feat)
    block_pair_list = jnp.concatenate([key_n, value_b], axis=1).reshape(nblocks, width, 2 * feat)
    owners = nbr_owner.reshape(-1)
    pairs = owners.shape[0]
    pair_block = jnp.arange(pairs, dtype=jnp.int32) // slots
    owner_hot = (owners[:, None] == jnp.arange(devices, dtype=jnp.int32)[None, :]).astype(jnp.int32)
    rank = jnp.sum(jnp.cumsum(owner_hot, axis=0) * owner_hot, axis=1) - 1
    target = owners * capacity + rank
    place = (target[:, None] == jnp.arange(tile_count, dtype=jnp.int32)[None, :]).astype(jnp.int32)
    wanted = jnp.where(slot_valid.reshape(-1) > 0, nbr_local.reshape(-1), -1)
    request = jnp.sum(place * (wanted[:, None] + 1), axis=0) - 1
    block_hot = (pair_block[:, None] == jnp.arange(nblocks, dtype=jnp.int32)[None, :]).astype(
        jnp.float32
    )
    selector_onehot = jnp.dot(place.T.astype(jnp.float32), block_hot).astype(jnp.bfloat16)
    query_outgoing = jnp.einsum(
        "cm,mqk->cqk", selector_onehot, query_block_rows, preferred_element_type=jnp.float32
    ).astype(jnp.bfloat16)
    asked = lax.all_to_all(
        request.reshape(devices, capacity), "nodes", split_axis=0, concat_axis=0, tiled=True
    ).reshape(-1)
    query_in = lax.all_to_all(
        query_outgoing.reshape(devices, capacity * width, feat),
        "nodes",
        split_axis=0,
        concat_axis=0,
        tiled=True,
    )
    self_numer, self_denom = split_result(
        run_tiles(
            query_block_rows,
            block_pair_list,
            jnp.arange(nblocks, dtype=jnp.int32),
            jnp.ones((nblocks,), jnp.int32),
            head_scale,
            capacity,
        ),
        capacity,
        width,
        count,
    )
    live_in = (asked >= 0).astype(jnp.int32)
    pick_in = jnp.clip(asked, 0, nblocks - 1)
    result = run_tiles(
        query_in.reshape(tile_count, width, feat),
        block_pair_list,
        pick_in,
        live_in,
        head_scale,
        capacity,
    )
    result = lax.all_to_all(result, "nodes", split_axis=0, concat_axis=0, tiled=True)
    numer, denom = split_result(result, capacity, width, count)
    numer_total = self_numer.astype(jnp.float32) + jnp.einsum(
        "uq,upl->qpl", selector_onehot, numer, preferred_element_type=jnp.float32
    )
    denominator_overall = self_denom.astype(jnp.float32) + jnp.einsum(
        "uq,ul->ql", selector_onehot, denom, preferred_element_type=jnp.float32
    )
    den_rows = jnp.transpose(denominator_overall.reshape(nblocks, count, width), (0, 2, 1))
    attn = numer_total.reshape(nblocks, width, count, feat // count) / den_rows[..., None]
    attn = attn.astype(jnp.bfloat16).reshape(rows, feat)
    cols = w_out.shape[0]
    gathered = lax.all_gather(
        jnp.concatenate([attn, w_out.T], axis=0), "heads", axis=1, tiled=True
    )
    attn_all = gathered[:rows]
    w_rows = lax.dynamic_slice_in_dim(gathered[rows:], lax.axis_index("heads") * cols, cols, axis=0)
    return lax.dot_general(
        attn_all, w_rows, (((1,), (1,)), ((), ())), preferred_element_type=jnp.float32
    ).astype(jnp.bfloat16)


def solution(mesh):
    placed = (
        P("nodes", None),
        P(None, "heads"),
        P(None, "heads"),
        P(None, "heads"),
        P("heads", None),
        P("heads"),
        P("nodes", None),
        P("nodes", None),
        P("nodes", None),
    )
    return jax.shard_map(
        body, mesh=mesh, in_specs=placed, out_specs=P("nodes", "heads"), check_vma=False
    )
```

```python
import functools

import jax
import jax.numpy as jnp
from jax import lax
from jax.experimental import pallas as pl
from jax.experimental.pallas import tpu as pltpu
from jax.sharding import PartitionSpec as P


def unit_rows(values, count):
    shaped = values.reshape(values.shape[0], count, -1)
    total = jnp.sum(shaped * shaped, axis=-1, keepdims=True)
    return (shaped * lax.rsqrt(total + 1e-06)).astype(jnp.bfloat16).reshape(values.shape)


def tile_kernel(pick_ref, live_ref, scale_ref, q_ref, km_ref, vt_ref, out_ref, den_scr, *, count, capacity):
    g = pl.program_id(0)
    group, feat, width = q_ref.shape
    lane_rows = lax.broadcasted_iota(jnp.int32, (count * width, 1), 0)
    scale_col = jnp.zeros((count * width, 1), jnp.float32)
    for h in range(count):
        inside = (lane_rows >= h * width) & (lane_rows < (h + 1) * width)
        scale_col = jnp.where(inside, scale_ref[h], scale_col)
    for i in range(group):
        t = g * group + i
        dest, slot = i // capacity, i % capacity

        @pl.when(live_ref[t] > 0)
        def _():
            s = jnp.dot(km_ref[pick_ref[t]], q_ref[i], preferred_element_type=jnp.float32)
            w = jnp.exp(scale_col * (s - 1.0))
            for h in range(count):
                den_scr[i * count + h:i * count + h + 1, :] = jnp.sum(
                    w[h * width:(h + 1) * width], axis=0, keepdims=True
                )
            num = jnp.dot(
                vt_ref[pick_ref[t]], w.astype(jnp.bfloat16), preferred_element_type=jnp.float32
            )
            out_ref[dest, slot * feat:(slot + 1) * feat, :] = num.astype(out_ref.dtype)

        @pl.when(live_ref[t] == 0)
        def _():
            out_ref[dest, slot * feat:(slot + 1) * feat, :] = jnp.zeros((feat, width), out_ref.dtype)
            den_scr[i * count:(i + 1) * count, :] = jnp.zeros((count, width), den_scr.dtype)

    per = capacity * count
    extra = out_ref.shape[1] - capacity * feat
    for d in range(group // capacity):
        rows = den_scr[d * per:(d + 1) * per, :]
        block = jnp.concatenate([rows, jnp.zeros((extra - per, width), rows.dtype)], axis=0)
        out_ref[d, capacity * feat:, :] = block.astype(out_ref.dtype)


def run_tiles(query_t, key_stack, value_t, pick, live, scales, capacity):
    tiles, feat, width = query_t.shape
    count = scales.shape[0]
    group = 8
    nblocks = key_stack.shape[0]
    extra = 16
    rows_out = capacity * feat + extra
    grid_spec = pltpu.PrefetchScalarGridSpec(
        num_scalar_prefetch=2,
        grid=(tiles // group,),
        in_specs=[
            pl.BlockSpec(memory_space=pltpu.SMEM),
            pl.BlockSpec((group, feat, width), lambda g, pick, live: (g, 0, 0)),
            pl.BlockSpec((nblocks, count * width, feat), lambda g, pick, live: (0, 0, 0)),
            pl.BlockSpec((nblocks, feat, count * width), lambda g, pick, live: (0, 0, 0)),
        ],
        out_specs=pl.BlockSpec((group // capacity, rows_out, width), lambda g, pick, live: (g, 0, 0)),
        scratch_shapes=[pltpu.VMEM((group * count, width), jnp.float32)],
    )
    return pl.pallas_call(
        functools.partial(tile_kernel, count=count, capacity=capacity),
        grid_spec=grid_spec,
        out_shape=jax.ShapeDtypeStruct((tiles // capacity, rows_out, width), jnp.bfloat16),
    )(pick, live, scales, query_t, key_stack, value_t)


def split_result(result, capacity, width, count):
    dests, rows_out, lanes = result.shape
    feat = (rows_out - 16) // capacity
    numer = result[:, :capacity * feat, :].reshape(dests * capacity, feat, lanes)
    denom = result[:, capacity * feat:capacity * feat + capacity * count, :]
    return numer, denom.reshape(dests * capacity, count * width)


def body(feats, w_query, w_key, w_value, w_out, head_scale, nbr_owner, nbr_local, slot_valid):
    rows = feats.shape[0]
    feat = w_query.shape[1]
    count = head_scale.shape[0]
    nblocks, slots = nbr_owner.shape
    width = rows // nblocks
    devices = lax.axis_size("nodes")
    capacity = max(2, min(nblocks // 2, 3 * nblocks * slots // (2 * devices)))
    tile_count = devices * capacity
    query_n = unit_rows(jnp.dot(feats, w_query, preferred_element_type=jnp.float32), count)
    key_n = unit_rows(jnp.dot(feats, w_key, preferred_element_type=jnp.float32), count)
    value_b = jnp.dot(feats, w_value, preferred_element_type=jnp.float32).astype(jnp.bfloat16)
    hd = feat // count
    query_t = jnp.swapaxes(query_n.reshape(nblocks, width, feat), 1, 2)
    key_blocks = key_n.reshape(nblocks, width, feat)
    value_t = jnp.swapaxes(value_b.reshape(nblocks, width, feat), 1, 2)
    head_of = jnp.arange(feat, dtype=jnp.int32) // hd
    key_stack = jnp.stack(
        [jnp.where(head_of[None, None, :] == h, key_blocks, 0) for h in range(count)], axis=1
    ).reshape(nblocks, count * width, feat)
    value_stack = jnp.stack(
        [jnp.where(head_of[None, :, None] == h, value_t, 0) for h in range(count)], axis=2
    ).reshape(nblocks, feat, count * width)
    owners = nbr_owner.reshape(-1)
    pairs = owners.shape[0]
    pair_block = jnp.arange(pairs, dtype=jnp.int32) // slots
    owner_hot = (owners[:, None] == jnp.arange(devices, dtype=jnp.int32)[None, :]).astype(jnp.int32)
    rank = jnp.sum(jnp.cumsum(owner_hot, axis=0) * owner_hot, axis=1) - 1
    target = owners * capacity + rank
    place = (target[:, None] == jnp.arange(tile_count, dtype=jnp.int32)[None, :]).astype(jnp.int32)
    wanted = jnp.where(slot_valid.reshape(-1) > 0, nbr_local.reshape(-1), -1)
    request = jnp.sum(place * (wanted[:, None] + 1), axis=0) - 1
    block_hot = (pair_block[:, None] == jnp.arange(nblocks, dtype=jnp.int32)[None, :]).astype(
        jnp.float32
    )
    selector_onehot = jnp.dot(place.T.astype(jnp.float32), block_hot).astype(jnp.bfloat16)
    query_outgoing = jnp.einsum(
        "cm,mfq->cfq", selector_onehot, query_t, preferred_element_type=jnp.float32
    ).astype(jnp.bfloat16)
    asked = lax.all_to_all(
        request.reshape(devices, capacity), "nodes", split_axis=0, concat_axis=0, tiled=True
    ).reshape(-1)
    query_in = lax.all_to_all(
        query_outgoing.reshape(devices, capacity * feat, width),
        "nodes",
        split_axis=0,
        concat_axis=0,
        tiled=True,
    )
    self_numer, self_denom = split_result(
        run_tiles(
            query_t,
            key_stack,
            value_stack,
            jnp.arange(nblocks, dtype=jnp.int32),
            jnp.ones((nblocks,), jnp.int32),
            head_scale,
            capacity,
        ),
        capacity,
        width,
        count,
    )
    live_in = (asked >= 0).astype(jnp.int32)
    pick_in = jnp.clip(asked, 0, nblocks - 1)
    result = run_tiles(
        query_in.reshape(tile_count, feat, width),
        key_stack,
        value_stack,
        pick_in,
        live_in,
        head_scale,
        capacity,
    )
    result = lax.all_to_all(result, "nodes", split_axis=0, concat_axis=0, tiled=True)
    numer, denom = split_result(result, capacity, width, count)
    numer_total = self_numer.astype(jnp.float32) + jnp.einsum(
        "ub,ufq->bfq", selector_onehot, numer, preferred_element_type=jnp.float32
    )
    numer_total = jnp.swapaxes(numer_total, 1, 2)
    denominator_overall = self_denom.astype(jnp.float32) + jnp.einsum(
        "uq,ul->ql", selector_onehot, denom, preferred_element_type=jnp.float32
    )
    den_rows = jnp.transpose(denominator_overall.reshape(nblocks, count, width), (0, 2, 1))
    attn = numer_total.reshape(nblocks, width, count, feat // count) / den_rows[..., None]
    attn = attn.astype(jnp.bfloat16).reshape(rows, feat)
    attn_all = lax.all_gather(attn, "heads", axis=1, tiled=True)
    w_cols = lax.dynamic_slice_in_dim(w_out, lax.axis_index("heads") * feat, feat, axis=1)
    return jnp.dot(attn_all, w_cols, preferred_element_type=jnp.float32).astype(jnp.bfloat16)


def solution(mesh):
    placed = (
        P("nodes", None),
        P(None, "heads"),
        P(None, "heads"),
        P(None, "heads"),
        P(None, None),
        P("heads"),
        P("nodes", None),
        P("nodes", None),
        P("nodes", None),
    )
    return jax.shard_map(
        body, mesh=mesh, in_specs=placed, out_specs=P("nodes", "heads"), check_vma=False
    )
```

```python
import functools

import jax
import jax.numpy as jnp
from jax import lax
from jax.experimental import pallas as pl
from jax.experimental.pallas import tpu as pltpu
from jax.sharding import PartitionSpec as P


def unit_rows(values, count):
    shaped = values.reshape(values.shape[0], count, -1)
    total = jnp.sum(shaped * shaped, axis=-1, keepdims=True)
    return (shaped * lax.rsqrt(total + 1e-06)).astype(jnp.bfloat16).reshape(values.shape)


def attend_kernel(
    slot_ref, live_ref, scale_ref, q_ref, own_ref, recv_ref, out_ref, num_scr, den_scr, *, count, slots
):
    b = pl.program_id(0)
    feat, width = q_ref.shape[1], q_ref.shape[2]
    hd = feat // count
    q_t = q_ref[0]
    lane_head = lax.broadcasted_iota(jnp.int32, (width, feat), 1) // hd
    row_head = lax.broadcasted_iota(jnp.int32, (feat, width), 0) // hd
    stack_rows = lax.broadcasted_iota(jnp.int32, (count * width, 1), 0)
    scale_col = jnp.zeros((count * width, 1), jnp.float32)
    for h in range(count):
        inside = (stack_rows >= h * width) & (stack_rows < (h + 1) * width)
        scale_col = jnp.where(inside, scale_ref[h], scale_col)

    def tile(kv):
        keys = kv[:width]
        values_t = kv[width:]
        key_stack = jnp.concatenate(
            [jnp.where(lane_head == h, keys, jnp.zeros_like(keys)) for h in range(count)], axis=0
        )
        value_stack = jnp.concatenate(
            [jnp.where(row_head == h, values_t, jnp.zeros_like(values_t)) for h in range(count)],
            axis=1,
        )
        s = jnp.dot(key_stack, q_t, preferred_element_type=jnp.float32)
        w = jnp.exp(scale_col * (s - 1.0))
        dens = [
            jnp.sum(w[h * width:(h + 1) * width], axis=0, keepdims=True)
            .astype(jnp.bfloat16)
            .astype(jnp.float32)
            for h in range(count)
        ]
        num = jnp.dot(value_stack, w.astype(jnp.bfloat16), preferred_element_type=jnp.float32)
        return num.astype(jnp.bfloat16).astype(jnp.float32), jnp.concatenate(dens, axis=0)

    num, den = tile(own_ref[b])
    num_scr[...] = num
    den_scr[...] = den
    for s in range(slots):
        p = b * slots + s

        @pl.when(live_ref[p] > 0)
        def _():
            num_s, den_s = tile(recv_ref[slot_ref[p]])
            num_scr[...] += num_s
            den_scr[...] += den_s

    den_full = jnp.zeros((feat, width), jnp.float32)
    for h in range(count):
        den_full = jnp.where(row_head == h, den_scr[h:h + 1, :], den_full)
    out_ref[0] = (num_scr[...] / den_full).astype(out_ref.dtype)


def attend(query_t, own_kv, recv_kv, slot_of, live, scales):
    nblocks, feat, width = query_t.shape
    count = scales.shape[0]
    slots = slot_of.shape[0] // nblocks
    tiles = recv_kv.shape[0]
    grid_spec = pltpu.PrefetchScalarGridSpec(
        num_scalar_prefetch=2,
        grid=(nblocks,),
        in_specs=[
            pl.BlockSpec(memory_space=pltpu.SMEM),
            pl.BlockSpec((1, feat, width), lambda b, slot_of, live: (b, 0, 0)),
            pl.BlockSpec((nblocks, 2 * width, feat), lambda b, slot_of, live: (0, 0, 0)),
            pl.BlockSpec((tiles, 2 * width, feat), lambda b, slot_of, live: (0, 0, 0)),
        ],
        out_specs=pl.BlockSpec((1, feat, width), lambda b, slot_of, live: (b, 0, 0)),
        scratch_shapes=[
            pltpu.VMEM((feat, width), jnp.float32),
            pltpu.VMEM((count, width), jnp.float32),
        ],
    )
    return pl.pallas_call(
        functools.partial(attend_kernel, count=count, slots=slots),
        grid_spec=grid_spec,
        out_shape=jax.ShapeDtypeStruct((nblocks, feat, width), jnp.bfloat16),
        compiler_params=pltpu.CompilerParams(vmem_limit_bytes=48 * 1024 * 1024),
    )(slot_of, live, scales, query_t, own_kv, recv_kv)


def body(feats, w_query, w_key, w_value, w_out, head_scale, nbr_owner, nbr_local, slot_valid):
    w_out, feats = lax.optimization_barrier((w_out, feats))
    rows = feats.shape[0]
    feat = w_query.shape[1]
    count = head_scale.shape[0]
    nblocks, slots = nbr_owner.shape
    width = rows // nblocks
    devices = lax.axis_size("nodes")
    capacity = max(2, min(nblocks // 2, 3 * nblocks * slots // (2 * devices)))
    tile_count = devices * capacity
    query_n = unit_rows(jnp.dot(feats, w_query, preferred_element_type=jnp.float32), count)
    key_n = unit_rows(jnp.dot(feats, w_key, preferred_element_type=jnp.float32), count)
    value_b = jnp.dot(feats, w_value, preferred_element_type=jnp.float32).astype(jnp.bfloat16)
    query_t = jnp.swapaxes(query_n.reshape(nblocks, width, feat), 1, 2)
    own_kv = jnp.concatenate(
        [key_n.reshape(nblocks, width, feat), jnp.swapaxes(value_b.reshape(nblocks, width, feat), 1, 2)],
        axis=1,
    )
    owners = nbr_owner.reshape(-1)
    owner_hot = (owners[:, None] == jnp.arange(devices, dtype=jnp.int32)[None, :]).astype(jnp.int32)
    rank = jnp.sum(jnp.cumsum(owner_hot, axis=0) * owner_hot, axis=1) - 1
    target = owners * capacity + rank
    place = (target[:, None] == jnp.arange(tile_count, dtype=jnp.int32)[None, :]).astype(jnp.int32)
    valid = (slot_valid.reshape(-1) > 0).astype(jnp.int32)
    wanted = jnp.where(valid > 0, nbr_local.reshape(-1), -1)
    request = jnp.sum(place * (wanted[:, None] + 1), axis=0) - 1
    asked = lax.all_to_all(
        request.reshape(devices, capacity), "nodes", split_axis=0, concat_axis=0, tiled=True
    ).reshape(-1)
    ask_hot = (asked[:, None] == jnp.arange(nblocks, dtype=jnp.int32)[None, :]).astype(jnp.bfloat16)
    payload = jnp.einsum(
        "cm,mrl->crl", ask_hot, own_kv, preferred_element_type=jnp.float32
    ).astype(jnp.bfloat16)
    recv_kv = lax.all_to_all(
        payload.reshape(devices, capacity * 2 * width, feat),
        "nodes",
        split_axis=0,
        concat_axis=0,
        tiled=True,
    ).reshape(tile_count, 2 * width, feat)
    slot_of = jnp.clip(target, 0, tile_count - 1).astype(jnp.int32)
    attn_t = attend(query_t, own_kv, recv_kv, slot_of, valid, head_scale)
    attn = jnp.swapaxes(attn_t, 1, 2).reshape(rows, feat)
    attn_all = lax.all_gather(attn, "heads", axis=1, tiled=True)
    w_cols = lax.dynamic_slice_in_dim(w_out, lax.axis_index("heads") * feat, feat, axis=1)
    return jnp.dot(attn_all, w_cols, preferred_element_type=jnp.float32).astype(jnp.bfloat16)


def solution(mesh):
    placed = (
        P("nodes", None),
        P(None, "heads"),
        P(None, "heads"),
        P(None, "heads"),
        P(None, None),
        P("heads"),
        P("nodes", None),
        P("nodes", None),
        P("nodes", None),
    )
    return jax.shard_map(
        body, mesh=mesh, in_specs=placed, out_specs=P("nodes", "heads"), check_vma=False
    )
```

```python
import functools

import jax
import jax.numpy as jnp
from jax import lax
from jax.experimental import pallas as pl
from jax.experimental.pallas import tpu as pltpu
from jax.sharding import PartitionSpec as P


def unit_rows(values, count):
    shaped = values.reshape(values.shape[0], count, -1)
    total = jnp.sum(shaped * shaped, axis=-1, keepdims=True)
    return (shaped * lax.rsqrt(total + 1e-06)).astype(jnp.bfloat16).reshape(values.shape)


def attend_kernel(
    slot_ref, live_ref, scale_ref, q_ref, own_ref, recv_ref, out_ref, num_scr, den_scr, *, count, slots
):
    b = pl.program_id(0)
    feat, lanes = q_ref.shape[1], q_ref.shape[2]
    width = lanes // count
    hd = feat // count
    q_stack = q_ref[0]
    row_head = lax.broadcasted_iota(jnp.int32, (feat, width), 0) // hd
    lane_pos = lax.broadcasted_iota(jnp.int32, (1, lanes), 1)
    scale_row = jnp.zeros((1, lanes), jnp.float32)
    for h in range(count):
        inside = (lane_pos >= h * width) & (lane_pos < (h + 1) * width)
        scale_row = jnp.where(inside, scale_ref[h], scale_row)

    def tile(kv):
        keys = kv[:width]
        values_t = kv[width:]
        s = jnp.dot(keys, q_stack, preferred_element_type=jnp.float32)
        w = jnp.exp(scale_row * (s - 1.0))
        den = jnp.sum(w, axis=0, keepdims=True).astype(jnp.bfloat16).astype(jnp.float32)
        w_b = w.astype(jnp.bfloat16)
        num = jnp.zeros((feat, width), jnp.float32)
        for h in range(count):
            part = jnp.dot(values_t, w_b[:, h * width:(h + 1) * width], preferred_element_type=jnp.float32)
            num = jnp.where(row_head == h, part, num)
        return num.astype(jnp.bfloat16).astype(jnp.float32), den

    num, den = tile(own_ref[b])
    num_scr[...] = num
    den_scr[...] = den
    for s in range(slots):
        p = b * slots + s

        @pl.when(live_ref[p] > 0)
        def _():
            num_s, den_s = tile(recv_ref[slot_ref[p]])
            num_scr[...] += num_s
            den_scr[...] += den_s

    den_full = jnp.zeros((feat, width), jnp.float32)
    for h in range(count):
        den_full = jnp.where(row_head == h, den_scr[:, h * width:(h + 1) * width], den_full)
    out_ref[0] = (num_scr[...] / den_full).astype(out_ref.dtype)


def attend(query_stack, own_kv, recv_kv, slot_of, live, scales):
    nblocks, feat, lanes = query_stack.shape
    count = scales.shape[0]
    width = lanes // count
    slots = slot_of.shape[0] // nblocks
    tiles = recv_kv.shape[0]
    grid_spec = pltpu.PrefetchScalarGridSpec(
        num_scalar_prefetch=2,
        grid=(nblocks,),
        in_specs=[
            pl.BlockSpec(memory_space=pltpu.SMEM),
            pl.BlockSpec((1, feat, lanes), lambda b, slot_of, live: (b, 0, 0)),
            pl.BlockSpec((nblocks, 2 * width, feat), lambda b, slot_of, live: (0, 0, 0)),
            pl.BlockSpec((tiles, 2 * width, feat), lambda b, slot_of, live: (0, 0, 0)),
        ],
        out_specs=pl.BlockSpec((1, feat, width), lambda b, slot_of, live: (b, 0, 0)),
        scratch_shapes=[
            pltpu.VMEM((feat, width), jnp.float32),
            pltpu.VMEM((1, lanes), jnp.float32),
        ],
    )
    return pl.pallas_call(
        functools.partial(attend_kernel, count=count, slots=slots),
        grid_spec=grid_spec,
        out_shape=jax.ShapeDtypeStruct((nblocks, feat, width), jnp.bfloat16),
        compiler_params=pltpu.CompilerParams(vmem_limit_bytes=48 * 1024 * 1024),
    )(slot_of, live, scales, query_stack, own_kv, recv_kv)


def gather_kernel(pick_ref, src_ref, out_ref):
    g = pl.program_id(0)
    group = out_ref.shape[0]
    for i in range(group):
        out_ref[i] = src_ref[pick_ref[g * group + i]]


def gather_blocks(blocks, pick):
    nblocks, r, l = blocks.shape
    tiles = pick.shape[0]
    group = 32
    grid_spec = pltpu.PrefetchScalarGridSpec(
        num_scalar_prefetch=1,
        grid=(tiles // group,),
        in_specs=[pl.BlockSpec((nblocks, r, l), lambda g, pick: (0, 0, 0))],
        out_specs=pl.BlockSpec((group, r, l), lambda g, pick: (g, 0, 0)),
    )
    return pl.pallas_call(
        gather_kernel,
        grid_spec=grid_spec,
        out_shape=jax.ShapeDtypeStruct((tiles, r, l), blocks.dtype),
    )(pick, blocks)


def body(feats, w_query, w_key, w_value, w_out, head_scale, nbr_owner, nbr_local, slot_valid):
    rows = feats.shape[0]
    feat = w_query.shape[1]
    count = head_scale.shape[0]
    nblocks, slots = nbr_owner.shape
    width = rows // nblocks
    devices = lax.axis_size("nodes")
    capacity = max(2, min(nblocks // 2, 3 * nblocks * slots // (2 * devices)))
    tile_count = devices * capacity
    query_n = unit_rows(jnp.dot(feats, w_query, preferred_element_type=jnp.float32), count)
    key_n = unit_rows(jnp.dot(feats, w_key, preferred_element_type=jnp.float32), count)
    value_b = jnp.dot(feats, w_value, preferred_element_type=jnp.float32).astype(jnp.bfloat16)
    query_t = jnp.swapaxes(query_n.reshape(nblocks, width, feat), 1, 2)
    head_of = jnp.arange(feat, dtype=jnp.int32) // (feat // count)
    query_stack = jnp.concatenate(
        [jnp.where(head_of[None, :, None] == h, query_t, 0) for h in range(count)], axis=2
    )
    own_kv = jnp.concatenate(
        [key_n.reshape(nblocks, width, feat), jnp.swapaxes(value_b.reshape(nblocks, width, feat), 1, 2)],
        axis=1,
    )
    owners = nbr_owner.reshape(-1)
    owner_hot = (owners[:, None] == jnp.arange(devices, dtype=jnp.int32)[None, :]).astype(jnp.int32)
    rank = jnp.sum(jnp.cumsum(owner_hot, axis=0) * owner_hot, axis=1) - 1
    target = owners * capacity + rank
    place = (target[:, None] == jnp.arange(tile_count, dtype=jnp.int32)[None, :]).astype(jnp.int32)
    valid = (slot_valid.reshape(-1) > 0).astype(jnp.int32)
    wanted = jnp.where(valid > 0, nbr_local.reshape(-1), -1)
    request = jnp.sum(place * (wanted[:, None] + 1), axis=0) - 1
    asked = lax.all_to_all(
        request.reshape(devices, capacity), "nodes", split_axis=0, concat_axis=0, tiled=True
    ).reshape(-1)
    payload = gather_blocks(own_kv, jnp.clip(asked, 0, nblocks - 1).astype(jnp.int32))
    w_out, payload = lax.optimization_barrier((w_out, payload))
    recv_kv = lax.all_to_all(
        payload.reshape(devices, capacity * 2 * width, feat),
        "nodes",
        split_axis=0,
        concat_axis=0,
        tiled=True,
    ).reshape(tile_count, 2 * width, feat)
    slot_of = jnp.clip(target, 0, tile_count - 1).astype(jnp.int32)
    attn_t = attend(query_stack, own_kv, recv_kv, slot_of, valid, head_scale)
    attn = jnp.swapaxes(attn_t, 1, 2).reshape(rows, feat)
    attn_all = lax.all_gather(attn, "heads", axis=1, tiled=True)
    w_cols = lax.dynamic_slice_in_dim(w_out, lax.axis_index("heads") * feat, feat, axis=1)
    return jnp.dot(attn_all, w_cols, preferred_element_type=jnp.float32).astype(jnp.bfloat16)


def solution(mesh):
    placed = (
        P("nodes", None),
        P(None, "heads"),
        P(None, "heads"),
        P(None, "heads"),
        P(None, None),
        P("heads"),
        P("nodes", None),
        P("nodes", None),
        P("nodes", None),
    )
    return jax.shard_map(
        body, mesh=mesh, in_specs=placed, out_specs=P("nodes", "heads"), check_vma=False
    )
```

```python
import functools

import jax
import jax.numpy as jnp
from jax import lax
from jax.experimental import pallas as pl
from jax.experimental.pallas import tpu as pltpu
from jax.sharding import PartitionSpec as P


def unit_rows(values, count):
    shaped = values.reshape(values.shape[0], count, -1)
    total = jnp.sum(shaped * shaped, axis=-1, keepdims=True)
    return (shaped * lax.rsqrt(total + 1e-06)).astype(jnp.bfloat16).reshape(values.shape)


def attend_kernel(
    slot_ref,
    live_ref,
    scale_ref,
    q_ref,
    own_ref,
    recv_ref,
    out_ref,
    num_scr,
    den_scr,
    buf,
    sems,
    *,
    count,
    slots,
):
    b = pl.program_id(0)
    pairs = buf.shape[0]

    def pair_copy(p):
        return pltpu.make_async_copy(recv_ref.at[slot_ref[p]], buf.at[p], sems.at[p])

    @pl.when(b == 0)
    def _():
        for p in range(pairs):

            @pl.when(live_ref[p] > 0)
            def _():
                pair_copy(p).start()

    feat, lanes = q_ref.shape[1], q_ref.shape[2]
    width = lanes // count
    hd = feat // count
    q_stack = q_ref[0]
    row_head = lax.broadcasted_iota(jnp.int32, (feat, width), 0) // hd
    lane_pos = lax.broadcasted_iota(jnp.int32, (1, lanes), 1)
    scale_row = jnp.zeros((1, lanes), jnp.float32)
    for h in range(count):
        inside = (lane_pos >= h * width) & (lane_pos < (h + 1) * width)
        scale_row = jnp.where(inside, scale_ref[h], scale_row)

    def tile(kv):
        keys = kv[:width]
        values_t = kv[width:]
        s = jnp.dot(keys, q_stack, preferred_element_type=jnp.float32)
        w = jnp.exp(scale_row * (s - 1.0))
        den = jnp.sum(w, axis=0, keepdims=True).astype(jnp.bfloat16).astype(jnp.float32)
        w_b = w.astype(jnp.bfloat16)
        num = jnp.zeros((feat, width), jnp.float32)
        for h in range(count):
            part = jnp.dot(values_t, w_b[:, h * width:(h + 1) * width], preferred_element_type=jnp.float32)
            num = jnp.where(row_head == h, part, num)
        return num.astype(jnp.bfloat16).astype(jnp.float32), den

    num, den = tile(own_ref[b])
    num_scr[...] = num
    den_scr[...] = den
    for s in range(slots):
        p = b * slots + s

        @pl.when(live_ref[p] > 0)
        def _():
            pair_copy(p).wait()
            num_s, den_s = tile(buf[p])
            num_scr[...] += num_s
            den_scr[...] += den_s

    den_full = jnp.zeros((feat, width), jnp.float32)
    for h in range(count):
        den_full = jnp.where(row_head == h, den_scr[:, h * width:(h + 1) * width], den_full)
    out_ref[0] = (num_scr[...] / den_full).astype(out_ref.dtype)


def attend(query_stack, own_kv, recv_kv, slot_of, live, scales):
    nblocks, feat, lanes = query_stack.shape
    count = scales.shape[0]
    width = lanes // count
    slots = slot_of.shape[0] // nblocks
    grid_spec = pltpu.PrefetchScalarGridSpec(
        num_scalar_prefetch=2,
        grid=(nblocks,),
        in_specs=[
            pl.BlockSpec(memory_space=pltpu.SMEM),
            pl.BlockSpec((1, feat, lanes), lambda b, slot_of, live: (b, 0, 0)),
            pl.BlockSpec((nblocks, 2 * width, feat), lambda b, slot_of, live: (0, 0, 0)),
            pl.BlockSpec(memory_space=pl.ANY),
        ],
        out_specs=pl.BlockSpec((1, feat, width), lambda b, slot_of, live: (b, 0, 0)),
        scratch_shapes=[
            pltpu.VMEM((feat, width), jnp.float32),
            pltpu.VMEM((1, lanes), jnp.float32),
            pltpu.VMEM((nblocks * slots, 2 * width, feat), recv_kv.dtype),
            pltpu.SemaphoreType.DMA((nblocks * slots,)),
        ],
    )
    return pl.pallas_call(
        functools.partial(attend_kernel, count=count, slots=slots),
        grid_spec=grid_spec,
        out_shape=jax.ShapeDtypeStruct((nblocks, feat, width), jnp.bfloat16),
        compiler_params=pltpu.CompilerParams(vmem_limit_bytes=48 * 1024 * 1024),
    )(slot_of, live, scales, query_stack, own_kv, recv_kv)


def gather_kernel(pick_ref, src_ref, out_ref):
    g = pl.program_id(0)
    group = out_ref.shape[0]
    for i in range(group):
        out_ref[i] = src_ref[pick_ref[g * group + i]]


def gather_blocks(blocks, pick):
    nblocks, r, l = blocks.shape
    tiles = pick.shape[0]
    group = 32
    grid_spec = pltpu.PrefetchScalarGridSpec(
        num_scalar_prefetch=1,
        grid=(tiles // group,),
        in_specs=[pl.BlockSpec((nblocks, r, l), lambda g, pick: (0, 0, 0))],
        out_specs=pl.BlockSpec((group, r, l), lambda g, pick: (g, 0, 0)),
    )
    return pl.pallas_call(
        gather_kernel,
        grid_spec=grid_spec,
        out_shape=jax.ShapeDtypeStruct((tiles, r, l), blocks.dtype),
    )(pick, blocks)


def body(feats, w_query, w_key, w_value, w_out, head_scale, nbr_owner, nbr_local, slot_valid):
    rows = feats.shape[0]
    feat = w_query.shape[1]
    count = head_scale.shape[0]
    nblocks, slots = nbr_owner.shape
    width = rows // nblocks
    devices = lax.axis_size("nodes")
    capacity = max(2, min(nblocks // 2, 3 * nblocks * slots // (2 * devices)))
    tile_count = devices * capacity
    query_n = unit_rows(jnp.dot(feats, w_query, preferred_element_type=jnp.float32), count)
    key_n = unit_rows(jnp.dot(feats, w_key, preferred_element_type=jnp.float32), count)
    value_b = jnp.dot(feats, w_value, preferred_element_type=jnp.float32).astype(jnp.bfloat16)
    query_t = jnp.swapaxes(query_n.reshape(nblocks, width, feat), 1, 2)
    head_of = jnp.arange(feat, dtype=jnp.int32) // (feat // count)
    query_stack = jnp.concatenate(
        [jnp.where(head_of[None, :, None] == h, query_t, 0) for h in range(count)], axis=2
    )
    own_kv = jnp.concatenate(
        [key_n.reshape(nblocks, width, feat), jnp.swapaxes(value_b.reshape(nblocks, width, feat), 1, 2)],
        axis=1,
    )
    owners = nbr_owner.reshape(-1)
    owner_hot = (owners[:, None] == jnp.arange(devices, dtype=jnp.int32)[None, :]).astype(jnp.int32)
    rank = jnp.sum(jnp.cumsum(owner_hot, axis=0) * owner_hot, axis=1) - 1
    target = owners * capacity + rank
    place = (target[:, None] == jnp.arange(tile_count, dtype=jnp.int32)[None, :]).astype(jnp.int32)
    valid = (slot_valid.reshape(-1) > 0).astype(jnp.int32)
    wanted = jnp.where(valid > 0, nbr_local.reshape(-1), -1)
    request = jnp.sum(place * (wanted[:, None] + 1), axis=0) - 1
    asked = lax.all_to_all(
        request.reshape(devices, capacity), "nodes", split_axis=0, concat_axis=0, tiled=True
    ).reshape(-1)
    payload = gather_blocks(own_kv, jnp.clip(asked, 0, nblocks - 1).astype(jnp.int32))
    w_out, payload = lax.optimization_barrier((w_out, payload))
    w_out_t = lax.all_gather(w_out.T, "heads", axis=1, tiled=True)
    recv_kv = lax.all_to_all(
        payload.reshape(devices, capacity * 2 * width, feat),
        "nodes",
        split_axis=0,
        concat_axis=0,
        tiled=True,
    ).reshape(tile_count, 2 * width, feat)
    recv_kv, w_out_t = lax.optimization_barrier((recv_kv, w_out_t))
    slot_of = jnp.clip(target, 0, tile_count - 1).astype(jnp.int32)
    attn_t = attend(query_stack, own_kv, recv_kv, slot_of, valid, head_scale)
    attn = jnp.swapaxes(attn_t, 1, 2).reshape(rows, feat)
    attn_all = lax.all_gather(attn, "heads", axis=1, tiled=True)
    w_rows = lax.dynamic_slice_in_dim(w_out_t, lax.axis_index("heads") * feat, feat, axis=0)
    return lax.dot_general(
        attn_all, w_rows, (((1,), (1,)), ((), ())), preferred_element_type=jnp.float32
    ).astype(jnp.bfloat16)


def solution(mesh):
    placed = (
        P("nodes", None),
        P(None, "heads"),
        P(None, "heads"),
        P(None, "heads"),
        P("heads", None),
        P("heads"),
        P("nodes", None),
        P("nodes", None),
        P("nodes", None),
    )
    return jax.shard_map(
        body, mesh=mesh, in_specs=placed, out_specs=P("nodes", "heads"), check_vma=False
    )
```

```python
import functools

import jax
import jax.numpy as jnp
from jax import lax
from jax.experimental import pallas as pl
from jax.experimental.pallas import tpu as pltpu
from jax.sharding import PartitionSpec as P


def unit_rows(values, count):
    shaped = values.reshape(values.shape[0], count, -1)
    total = jnp.sum(shaped * shaped, axis=-1, keepdims=True)
    return (shaped * lax.rsqrt(total + 1e-06)).astype(jnp.bfloat16).reshape(values.shape)


def attend_kernel(slot_ref, live_ref, scale_ref, q_ref, own_ref, recv_ref, out_ref, buf, sems, *, count, slots):
    b = pl.program_id(0)
    pairs = buf.shape[0]
    feat, lanes = q_ref.shape[1], q_ref.shape[2]
    width = lanes // count
    hd = feat // count

    def pair_copy(p):
        return pltpu.make_async_copy(recv_ref.at[slot_ref[p]], buf.at[p], sems.at[p])

    @pl.when(b == 0)
    def _():
        for p in range(pairs):
            pair_copy(p).start()

    for s in range(slots):
        pair_copy(b * slots + s).wait()
    q_stack = q_ref[0]
    row_head = lax.broadcasted_iota(jnp.int32, (feat, width), 0) // hd
    lane_pos = lax.broadcasted_iota(jnp.int32, (1, lanes), 1)
    scale_row = jnp.zeros((1, lanes), jnp.float32)
    for h in range(count):
        inside = (lane_pos >= h * width) & (lane_pos < (h + 1) * width)
        scale_row = jnp.where(inside, scale_ref[h], scale_row)
    key_rows = lax.broadcasted_iota(jnp.int32, ((slots + 1) * width, 1), 0)
    live_col = jnp.ones(((slots + 1) * width, 1), jnp.float32)
    for s in range(slots):
        inside = (key_rows >= (s + 1) * width) & (key_rows < (s + 2) * width)
        live_col = jnp.where(inside, live_ref[b * slots + s].astype(jnp.float32), live_col)
    blocks = [own_ref[b]] + [buf[b * slots + s] for s in range(slots)]
    keys = jnp.concatenate([blk[:width] for blk in blocks], axis=0)
    values_t = jnp.concatenate([blk[width:] for blk in blocks], axis=1)
    s_all = jnp.dot(keys, q_stack, preferred_element_type=jnp.float32)
    w = jnp.exp(scale_row * (s_all - 1.0)) * live_col
    den = jnp.sum(w, axis=0, keepdims=True)
    w_b = w.astype(jnp.bfloat16)
    num = jnp.zeros((feat, width), jnp.float32)
    den_full = jnp.zeros((feat, width), jnp.float32)
    for h in range(count):
        part = jnp.dot(values_t, w_b[:, h * width:(h + 1) * width], preferred_element_type=jnp.float32)
        num = jnp.where(row_head == h, part, num)
        den_full = jnp.where(row_head == h, den[:, h * width:(h + 1) * width], den_full)
    out_ref[0] = (num / den_full).astype(out_ref.dtype)


def attend(query_stack, own_kv, recv_kv, slot_of, live, scales):
    nblocks, feat, lanes = query_stack.shape
    count = scales.shape[0]
    width = lanes // count
    slots = slot_of.shape[0] // nblocks
    grid_spec = pltpu.PrefetchScalarGridSpec(
        num_scalar_prefetch=2,
        grid=(nblocks,),
        in_specs=[
            pl.BlockSpec(memory_space=pltpu.SMEM),
            pl.BlockSpec((1, feat, lanes), lambda b, slot_of, live: (b, 0, 0)),
            pl.BlockSpec((nblocks, 2 * width, feat), lambda b, slot_of, live: (0, 0, 0)),
            pl.BlockSpec(memory_space=pl.ANY),
        ],
        out_specs=pl.BlockSpec((1, feat, width), lambda b, slot_of, live: (b, 0, 0)),
        scratch_shapes=[
            pltpu.VMEM((nblocks * slots, 2 * width, feat), recv_kv.dtype),
            pltpu.SemaphoreType.DMA((nblocks * slots,)),
        ],
    )
    return pl.pallas_call(
        functools.partial(attend_kernel, count=count, slots=slots),
        grid_spec=grid_spec,
        out_shape=jax.ShapeDtypeStruct((nblocks, feat, width), jnp.bfloat16),
        compiler_params=pltpu.CompilerParams(vmem_limit_bytes=48 * 1024 * 1024),
    )(slot_of, live, scales, query_stack, own_kv, recv_kv)


def gather_kernel(pick_ref, src_ref, out_ref):
    g = pl.program_id(0)
    group = out_ref.shape[0]
    for i in range(group):
        out_ref[i] = src_ref[pick_ref[g * group + i]]


def gather_blocks(blocks, pick):
    nblocks, r, l = blocks.shape
    tiles = pick.shape[0]
    group = 32
    grid_spec = pltpu.PrefetchScalarGridSpec(
        num_scalar_prefetch=1,
        grid=(tiles // group,),
        in_specs=[pl.BlockSpec((nblocks, r, l), lambda g, pick: (0, 0, 0))],
        out_specs=pl.BlockSpec((group, r, l), lambda g, pick: (g, 0, 0)),
    )
    return pl.pallas_call(
        gather_kernel,
        grid_spec=grid_spec,
        out_shape=jax.ShapeDtypeStruct((tiles, r, l), blocks.dtype),
    )(pick, blocks)


def body(feats, w_query, w_key, w_value, w_out, head_scale, nbr_owner, nbr_local, slot_valid):
    rows = feats.shape[0]
    feat = w_query.shape[1]
    count = head_scale.shape[0]
    nblocks, slots = nbr_owner.shape
    width = rows // nblocks
    devices = lax.axis_size("nodes")
    capacity = max(2, min(nblocks // 2, 3 * nblocks * slots // (2 * devices)))
    tile_count = devices * capacity
    query_n = unit_rows(jnp.dot(feats, w_query, preferred_element_type=jnp.float32), count)
    key_n = unit_rows(jnp.dot(feats, w_key, preferred_element_type=jnp.float32), count)
    value_b = jnp.dot(feats, w_value, preferred_element_type=jnp.float32).astype(jnp.bfloat16)
    query_t = jnp.swapaxes(query_n.reshape(nblocks, width, feat), 1, 2)
    head_of = jnp.arange(feat, dtype=jnp.int32) // (feat // count)
    query_stack = jnp.concatenate(
        [jnp.where(head_of[None, :, None] == h, query_t, 0) for h in range(count)], axis=2
    )
    own_kv = jnp.concatenate(
        [key_n.reshape(nblocks, width, feat), jnp.swapaxes(value_b.reshape(nblocks, width, feat), 1, 2)],
        axis=1,
    )
    owners = nbr_owner.reshape(-1)
    owner_hot = (owners[:, None] == jnp.arange(devices, dtype=jnp.int32)[None, :]).astype(jnp.int32)
    rank = jnp.sum(jnp.cumsum(owner_hot, axis=0) * owner_hot, axis=1) - 1
    target = owners * capacity + rank
    place = (target[:, None] == jnp.arange(tile_count, dtype=jnp.int32)[None, :]).astype(jnp.int32)
    valid = (slot_valid.reshape(-1) > 0).astype(jnp.int32)
    wanted = jnp.where(valid > 0, nbr_local.reshape(-1), -1)
    request = jnp.sum(place * (wanted[:, None] + 1), axis=0) - 1
    asked = lax.all_to_all(
        request.reshape(devices, capacity), "nodes", split_axis=0, concat_axis=0, tiled=True
    ).reshape(-1)
    payload = gather_blocks(own_kv, jnp.clip(asked, 0, nblocks - 1).astype(jnp.int32))
    w_out, payload = lax.optimization_barrier((w_out, payload))
    w_out_t = lax.all_gather(w_out.T, "heads", axis=1, tiled=True)
    recv_kv = lax.all_to_all(
        payload.reshape(devices, capacity * 2 * width, feat),
        "nodes",
        split_axis=0,
        concat_axis=0,
        tiled=True,
    ).reshape(tile_count, 2 * width, feat)
    recv_kv, w_out_t = lax.optimization_barrier((recv_kv, w_out_t))
    slot_of = jnp.clip(target, 0, tile_count - 1).astype(jnp.int32)
    attn_t = attend(query_stack, own_kv, recv_kv, slot_of, valid, head_scale)
    attn = jnp.swapaxes(attn_t, 1, 2).reshape(rows, feat)
    heads = lax.axis_size("heads")
    me = lax.axis_index("heads")

    def out_part(piece, source):
        w_part = lax.dynamic_slice(w_out_t, (me * feat, source * feat), (feat, feat))
        return lax.dot_general(
            piece, w_part, (((1,), (1,)), ((), ())), preferred_element_type=jnp.float32
        )

    mixed = out_part(attn, me)
    for k in range(1, heads):
        piece = lax.ppermute(attn, "heads", [(j, (j + k) % heads) for j in range(heads)])
        mixed = mixed + out_part(piece, (me - k) % heads)
    return mixed.astype(jnp.bfloat16)


def solution(mesh):
    placed = (
        P("nodes", None),
        P(None, "heads"),
        P(None, "heads"),
        P(None, "heads"),
        P("heads", None),
        P("heads"),
        P("nodes", None),
        P("nodes", None),
        P("nodes", None),
    )
    return jax.shard_map(
        body, mesh=mesh, in_specs=placed, out_specs=P("nodes", "heads"), check_vma=False
    )
```

```python
import functools

import jax
import jax.numpy as jnp
from jax import lax
from jax.experimental import pallas as pl
from jax.experimental.pallas import tpu as pltpu
from jax.sharding import PartitionSpec as P


def unit_rows(values, count):
    shaped = values.reshape(values.shape[0], count, -1)
    total = jnp.sum(shaped * shaped, axis=-1, keepdims=True)
    return (shaped * lax.rsqrt(total + 1e-06)).astype(jnp.bfloat16).reshape(values.shape)


def attend_kernel(slot_ref, live_ref, scale_ref, q_ref, own_ref, recv_ref, out_ref, buf, sems, *, count, slots):
    b = pl.program_id(0)
    pairs = buf.shape[0]
    feat, lanes = q_ref.shape[1], q_ref.shape[2]
    width = lanes // count
    hd = feat // count

    def pair_copy(p):
        return pltpu.make_async_copy(recv_ref.at[slot_ref[p]], buf.at[p], sems.at[p])

    @pl.when(b == 0)
    def _():
        for p in range(pairs):

            @pl.when(live_ref[p] > 0)
            def _():
                pair_copy(p).start()

            @pl.when(live_ref[p] == 0)
            def _():
                buf[p] = jnp.zeros(buf.shape[1:], buf.dtype)

    for s in range(slots):

        @pl.when(live_ref[b * slots + s] > 0)
        def _():
            pair_copy(b * slots + s).wait()
    q_stack = q_ref[0]
    row_head = lax.broadcasted_iota(jnp.int32, (feat, width), 0) // hd
    lane_pos = lax.broadcasted_iota(jnp.int32, (1, lanes), 1)
    scale_row = jnp.zeros((1, lanes), jnp.float32)
    for h in range(count):
        inside = (lane_pos >= h * width) & (lane_pos < (h + 1) * width)
        scale_row = jnp.where(inside, scale_ref[h], scale_row)
    key_rows = lax.broadcasted_iota(jnp.int32, ((slots + 1) * width, 1), 0)
    live_col = jnp.ones(((slots + 1) * width, 1), jnp.float32)
    for s in range(slots):
        inside = (key_rows >= (s + 1) * width) & (key_rows < (s + 2) * width)
        live_col = jnp.where(inside, live_ref[b * slots + s].astype(jnp.float32), live_col)
    blocks = [own_ref[b]] + [buf[b * slots + s] for s in range(slots)]
    keys = jnp.concatenate([blk[:width] for blk in blocks], axis=0)
    values_t = jnp.concatenate([blk[width:] for blk in blocks], axis=1)
    s_all = jnp.dot(keys, q_stack, preferred_element_type=jnp.float32)
    w = jnp.exp(scale_row * (s_all - 1.0)) * live_col
    den = jnp.sum(w, axis=0, keepdims=True)
    w_b = w.astype(jnp.bfloat16)
    num = jnp.zeros((feat, width), jnp.float32)
    den_full = jnp.zeros((feat, width), jnp.float32)
    for h in range(count):
        part = jnp.dot(values_t, w_b[:, h * width:(h + 1) * width], preferred_element_type=jnp.float32)
        num = jnp.where(row_head == h, part, num)
        den_full = jnp.where(row_head == h, den[:, h * width:(h + 1) * width], den_full)
    out_ref[0] = (num / den_full).astype(out_ref.dtype)


def attend(query_stack, own_kv, recv_kv, slot_of, live, scales):
    nblocks, feat, lanes = query_stack.shape
    count = scales.shape[0]
    width = lanes // count
    slots = slot_of.shape[0] // nblocks
    grid_spec = pltpu.PrefetchScalarGridSpec(
        num_scalar_prefetch=2,
        grid=(nblocks,),
        in_specs=[
            pl.BlockSpec(memory_space=pltpu.SMEM),
            pl.BlockSpec((1, feat, lanes), lambda b, slot_of, live: (b, 0, 0)),
            pl.BlockSpec((nblocks, 2 * width, feat), lambda b, slot_of, live: (0, 0, 0)),
            pl.BlockSpec(memory_space=pl.ANY),
        ],
        out_specs=pl.BlockSpec((1, feat, width), lambda b, slot_of, live: (b, 0, 0)),
        scratch_shapes=[
            pltpu.VMEM((nblocks * slots, 2 * width, feat), recv_kv.dtype),
            pltpu.SemaphoreType.DMA((nblocks * slots,)),
        ],
    )
    return pl.pallas_call(
        functools.partial(attend_kernel, count=count, slots=slots),
        grid_spec=grid_spec,
        out_shape=jax.ShapeDtypeStruct((nblocks, feat, width), jnp.bfloat16),
        compiler_params=pltpu.CompilerParams(vmem_limit_bytes=48 * 1024 * 1024),
    )(slot_of, live, scales, query_stack, own_kv, recv_kv)


def gather_kernel(pick_ref, src_ref, out_ref, sems):
    tiles = out_ref.shape[0]

    def slot_copy(c):
        return pltpu.make_async_copy(src_ref.at[pick_ref[c]], out_ref.at[c], sems.at[c])

    for c in range(tiles):

        @pl.when(pick_ref[c] >= 0)
        def _():
            slot_copy(c).start()

    for c in range(tiles):

        @pl.when(pick_ref[c] >= 0)
        def _():
            slot_copy(c).wait()


def gather_blocks(blocks, pick):
    tiles = pick.shape[0]
    grid_spec = pltpu.PrefetchScalarGridSpec(
        num_scalar_prefetch=1,
        grid=(1,),
        in_specs=[pl.BlockSpec(memory_space=pl.ANY)],
        out_specs=pl.BlockSpec(memory_space=pl.ANY),
        scratch_shapes=[pltpu.SemaphoreType.DMA((tiles,))],
    )
    return pl.pallas_call(
        gather_kernel,
        grid_spec=grid_spec,
        out_shape=jax.ShapeDtypeStruct((tiles,) + blocks.shape[1:], blocks.dtype),
    )(pick, blocks)


def body(feats, w_query, w_key, w_value, w_out, head_scale, nbr_owner, nbr_local, slot_valid):
    rows = feats.shape[0]
    feat = w_query.shape[1]
    count = head_scale.shape[0]
    nblocks, slots = nbr_owner.shape
    width = rows // nblocks
    devices = lax.axis_size("nodes")
    capacity = max(2, min(nblocks // 2, 3 * nblocks * slots // (2 * devices)))
    tile_count = devices * capacity
    query_n = unit_rows(jnp.dot(feats, w_query, preferred_element_type=jnp.float32), count)
    key_n = unit_rows(jnp.dot(feats, w_key, preferred_element_type=jnp.float32), count)
    value_b = jnp.dot(feats, w_value, preferred_element_type=jnp.float32).astype(jnp.bfloat16)
    query_t = jnp.swapaxes(query_n.reshape(nblocks, width, feat), 1, 2)
    head_of = jnp.arange(feat, dtype=jnp.int32) // (feat // count)
    query_stack = jnp.concatenate(
        [jnp.where(head_of[None, :, None] == h, query_t, 0) for h in range(count)], axis=2
    )
    own_kv = jnp.concatenate(
        [key_n.reshape(nblocks, width, feat), jnp.swapaxes(value_b.reshape(nblocks, width, feat), 1, 2)],
        axis=1,
    )
    owners = nbr_owner.reshape(-1)
    owner_hot = (owners[:, None] == jnp.arange(devices, dtype=jnp.int32)[None, :]).astype(jnp.int32)
    rank = jnp.sum(jnp.cumsum(owner_hot, axis=0) * owner_hot, axis=1) - 1
    target = owners * capacity + rank
    place = (target[:, None] == jnp.arange(tile_count, dtype=jnp.int32)[None, :]).astype(jnp.int32)
    valid = (slot_valid.reshape(-1) > 0).astype(jnp.int32)
    wanted = jnp.where(valid > 0, nbr_local.reshape(-1), -1)
    request = jnp.sum(place * (wanted[:, None] + 1), axis=0) - 1
    asked = lax.all_to_all(
        request.reshape(devices, capacity), "nodes", split_axis=0, concat_axis=0, tiled=True
    ).reshape(-1)
    payload = gather_blocks(own_kv, jnp.clip(asked, -1, nblocks - 1).astype(jnp.int32))
    w_out, payload = lax.optimization_barrier((w_out, payload))
    w_out_t = lax.all_gather(w_out.T, "heads", axis=1, tiled=True)
    recv_kv = lax.all_to_all(
        payload.reshape(devices, capacity * 2 * width, feat),
        "nodes",
        split_axis=0,
        concat_axis=0,
        tiled=True,
    ).reshape(tile_count, 2 * width, feat)
    recv_kv, w_out_t = lax.optimization_barrier((recv_kv, w_out_t))
    slot_of = jnp.clip(target, 0, tile_count - 1).astype(jnp.int32)
    attn_t = attend(query_stack, own_kv, recv_kv, slot_of, valid, head_scale)
    attn = jnp.swapaxes(attn_t, 1, 2).reshape(rows, feat)
    heads = lax.axis_size("heads")
    me = lax.axis_index("heads")

    def out_part(piece, source):
        w_part = lax.dynamic_slice(w_out_t, (me * feat, source * feat), (feat, feat))
        return lax.dot_general(
            piece, w_part, (((1,), (1,)), ((), ())), preferred_element_type=jnp.float32
        )

    pieces = lax.all_to_all(
        jnp.broadcast_to(attn[None], (heads,) + attn.shape), "heads", 0, 0, tiled=False
    )
    mixed = out_part(pieces[0], 0)
    for k in range(1, heads):
        mixed = mixed + out_part(pieces[k], k)
    return mixed.astype(jnp.bfloat16)


def solution(mesh):
    placed = (
        P("nodes", None),
        P(None, "heads"),
        P(None, "heads"),
        P(None, "heads"),
        P("heads", None),
        P("heads"),
        P("nodes", None),
        P("nodes", None),
        P("nodes", None),
    )
    return jax.shard_map(
        body, mesh=mesh, in_specs=placed, out_specs=P("nodes", "heads"), check_vma=False
    )
```

```python
import functools

import jax
import jax.numpy as jnp
from jax import lax
from jax.experimental import pallas as pl
from jax.experimental.pallas import tpu as pltpu
from jax.sharding import PartitionSpec as P


def unit_rows(values, count):
    shaped = values.reshape(values.shape[0], count, -1)
    total = jnp.sum(shaped * shaped, axis=-1, keepdims=True)
    return (shaped * lax.rsqrt(total + 1e-06)).astype(jnp.bfloat16).reshape(values.shape)


def attend_kernel(slot_ref, live_ref, scale_ref, q_ref, own_ref, recv_ref, out_ref, buf, sems, *, count, slots):
    b = pl.program_id(0)
    pairs = buf.shape[0]
    feat, lanes = q_ref.shape[1], q_ref.shape[2]
    width = lanes // count
    hd = feat // count

    def pair_copy(p):
        return pltpu.make_async_copy(recv_ref.at[slot_ref[p]], buf.at[p], sems.at[p])

    @pl.when(b == 0)
    def _():
        for p in range(pairs):
            pair_copy(p).start()

    for s in range(slots):
        pair_copy(b * slots + s).wait()
    q_stack = q_ref[0]
    row_head = lax.broadcasted_iota(jnp.int32, (feat, width), 0) // hd
    lane_pos = lax.broadcasted_iota(jnp.int32, (1, lanes), 1)
    scale_row = jnp.zeros((1, lanes), jnp.float32)
    for h in range(count):
        inside = (lane_pos >= h * width) & (lane_pos < (h + 1) * width)
        scale_row = jnp.where(inside, scale_ref[h], scale_row)
    key_rows = lax.broadcasted_iota(jnp.int32, ((slots + 1) * width, 1), 0)
    live_col = jnp.ones(((slots + 1) * width, 1), jnp.float32)
    for s in range(slots):
        inside = (key_rows >= (s + 1) * width) & (key_rows < (s + 2) * width)
        live_col = jnp.where(inside, live_ref[b * slots + s].astype(jnp.float32), live_col)
    blocks = [own_ref[b]] + [buf[b * slots + s] for s in range(slots)]
    keys = jnp.concatenate([blk[:width] for blk in blocks], axis=0)
    values_t = jnp.concatenate([blk[width:] for blk in blocks], axis=1)
    s_all = jnp.dot(keys, q_stack, preferred_element_type=jnp.float32)
    w = jnp.exp(scale_row * (s_all - 1.0)) * live_col
    den = jnp.sum(w, axis=0, keepdims=True)
    w_b = w.astype(jnp.bfloat16)
    num = jnp.zeros((feat, width), jnp.float32)
    den_full = jnp.zeros((feat, width), jnp.float32)
    for h in range(count):
        part = jnp.dot(values_t, w_b[:, h * width:(h + 1) * width], preferred_element_type=jnp.float32)
        num = jnp.where(row_head == h, part, num)
        den_full = jnp.where(row_head == h, den[:, h * width:(h + 1) * width], den_full)
    out_ref[0] = (num / den_full).astype(out_ref.dtype)


def attend(query_stack, own_kv, recv_kv, slot_of, live, scales):
    nblocks, feat, lanes = query_stack.shape
    count = scales.shape[0]
    width = lanes // count
    slots = slot_of.shape[0] // nblocks
    grid_spec = pltpu.PrefetchScalarGridSpec(
        num_scalar_prefetch=2,
        grid=(nblocks,),
        in_specs=[
            pl.BlockSpec(memory_space=pltpu.SMEM),
            pl.BlockSpec((1, feat, lanes), lambda b, slot_of, live: (b, 0, 0)),
            pl.BlockSpec((nblocks, 2 * width, feat), lambda b, slot_of, live: (0, 0, 0)),
            pl.BlockSpec(memory_space=pl.ANY),
        ],
        out_specs=pl.BlockSpec((1, feat, width), lambda b, slot_of, live: (b, 0, 0)),
        scratch_shapes=[
            pltpu.VMEM((nblocks * slots, 2 * width, feat), recv_kv.dtype),
            pltpu.SemaphoreType.DMA((nblocks * slots,)),
        ],
    )
    return pl.pallas_call(
        functools.partial(attend_kernel, count=count, slots=slots),
        grid_spec=grid_spec,
        out_shape=jax.ShapeDtypeStruct((nblocks, feat, width), jnp.bfloat16),
        compiler_params=pltpu.CompilerParams(vmem_limit_bytes=48 * 1024 * 1024),
    )(slot_of, live, scales, query_stack, own_kv, recv_kv)


def gather_kernel(pick_ref, src_ref, out_ref):
    g = pl.program_id(0)
    group = out_ref.shape[0]
    for i in range(group):
        out_ref[i] = src_ref[pick_ref[g * group + i]]


def gather_blocks(blocks, pick):
    nblocks, r, l = blocks.shape
    tiles = pick.shape[0]
    group = 32
    grid_spec = pltpu.PrefetchScalarGridSpec(
        num_scalar_prefetch=1,
        grid=(tiles // group,),
        in_specs=[pl.BlockSpec((nblocks, r, l), lambda g, pick: (0, 0, 0))],
        out_specs=pl.BlockSpec((group, r, l), lambda g, pick: (g, 0, 0)),
    )
    return pl.pallas_call(
        gather_kernel,
        grid_spec=grid_spec,
        out_shape=jax.ShapeDtypeStruct((tiles, r, l), blocks.dtype),
    )(pick, blocks)


def body(feats, w_query, w_key, w_value, w_out, head_scale, nbr_owner, nbr_local, slot_valid):
    rows = feats.shape[0]
    feat = w_query.shape[1]
    count = head_scale.shape[0]
    nblocks, slots = nbr_owner.shape
    width = rows // nblocks
    devices = lax.axis_size("nodes")
    capacity = max(2, min(nblocks // 2, 3 * nblocks * slots // (2 * devices)))
    tile_count = devices * capacity
    query_n = unit_rows(jnp.dot(feats, w_query, preferred_element_type=jnp.float32), count)
    key_n = unit_rows(jnp.dot(feats, w_key, preferred_element_type=jnp.float32), count)
    value_b = jnp.dot(feats, w_value, preferred_element_type=jnp.float32).astype(jnp.bfloat16)
    query_t = jnp.swapaxes(query_n.reshape(nblocks, width, feat), 1, 2)
    head_of = jnp.arange(feat, dtype=jnp.int32) // (feat // count)
    query_stack = jnp.concatenate(
        [jnp.where(head_of[None, :, None] == h, query_t, 0) for h in range(count)], axis=2
    )
    own_kv = jnp.concatenate(
        [key_n.reshape(nblocks, width, feat), jnp.swapaxes(value_b.reshape(nblocks, width, feat), 1, 2)],
        axis=1,
    )
    me = lax.axis_index("nodes")
    owners = nbr_owner.reshape(-1)
    valid = (slot_valid.reshape(-1) > 0).astype(jnp.int32)
    owner_hot = (
        (owners[:, None] == jnp.arange(devices, dtype=jnp.int32)[None, :]) & (valid[:, None] > 0)
    ).astype(jnp.int32)
    rank = jnp.sum(jnp.cumsum(owner_hot, axis=0) * owner_hot, axis=1) - 1
    target = jnp.where(valid > 0, owners * capacity + rank, 0)
    code = jnp.where(slot_valid > 0, nbr_owner * nblocks + nbr_local, -1)
    every = lax.all_gather(code.reshape(1, nblocks * slots), "nodes", axis=0, tiled=True)
    mine = ((every >= 0) & (every // nblocks == me)).astype(jnp.int32)
    their_rank = jnp.cumsum(mine, axis=1) - 1
    local_plus = every - me * nblocks + 1
    asked = jnp.stack(
        [jnp.sum(mine * (their_rank == r) * local_plus, axis=1) - 1 for r in range(capacity)],
        axis=1,
    ).reshape(-1)
    payload = gather_blocks(own_kv, jnp.clip(asked, 0, nblocks - 1).astype(jnp.int32))
    w_out, payload = lax.optimization_barrier((w_out, payload))
    w_out_t = lax.all_gather(w_out.T, "heads", axis=1, tiled=True)
    recv_kv = lax.all_to_all(
        payload.reshape(devices, capacity * 2 * width, feat),
        "nodes",
        split_axis=0,
        concat_axis=0,
        tiled=True,
    ).reshape(tile_count, 2 * width, feat)
    recv_kv, w_out_t = lax.optimization_barrier((recv_kv, w_out_t))
    slot_of = jnp.clip(target, 0, tile_count - 1).astype(jnp.int32)
    attn_t = attend(query_stack, own_kv, recv_kv, slot_of, valid, head_scale)
    attn = jnp.swapaxes(attn_t, 1, 2).reshape(rows, feat)
    heads = lax.axis_size("heads")
    me = lax.axis_index("heads")

    def out_part(piece, source):
        w_part = lax.dynamic_slice(w_out_t, (me * feat, source * feat), (feat, feat))
        return lax.dot_general(
            piece, w_part, (((1,), (1,)), ((), ())), preferred_element_type=jnp.float32
        )

    mixed = out_part(attn, me)
    for k in range(1, heads):
        piece = lax.ppermute(attn, "heads", [(j, (j + k) % heads) for j in range(heads)])
        mixed = mixed + out_part(piece, (me - k) % heads)
    return mixed.astype(jnp.bfloat16)


def solution(mesh):
    placed = (
        P("nodes", None),
        P(None, "heads"),
        P(None, "heads"),
        P(None, "heads"),
        P("heads", None),
        P("heads"),
        P("nodes", None),
        P("nodes", None),
        P("nodes", None),
    )
    return jax.shard_map(
        body, mesh=mesh, in_specs=placed, out_specs=P("nodes", "heads"), check_vma=False
    )
```

```python
import functools

import jax
import jax.numpy as jnp
from jax import lax
from jax.experimental import pallas as pl
from jax.experimental.pallas import tpu as pltpu
from jax.sharding import PartitionSpec as P


def unit_rows(values, count):
    shaped = values.reshape(values.shape[0], count, -1)
    total = jnp.sum(shaped * shaped, axis=-1, keepdims=True)
    return (shaped * lax.rsqrt(total + 1e-06)).astype(jnp.bfloat16).reshape(values.shape)


def attend_kernel(slot_ref, live_ref, scale_ref, q_ref, own_ref, recv_ref, out_ref, buf, sems, *, count, slots):
    pairs = buf.shape[0]
    nblocks, feat, lanes = q_ref.shape
    width = lanes // count
    hd = feat // count

    def pair_copy(p):
        return pltpu.make_async_copy(recv_ref.at[slot_ref[p]], buf.at[p], sems.at[p])

    for p in range(pairs):
        pair_copy(p).start()

    row_head = lax.broadcasted_iota(jnp.int32, (feat, width), 0) // hd
    lane_pos = lax.broadcasted_iota(jnp.int32, (1, lanes), 1)
    scale_row = jnp.zeros((1, lanes), jnp.float32)
    for h in range(count):
        inside = (lane_pos >= h * width) & (lane_pos < (h + 1) * width)
        scale_row = jnp.where(inside, scale_ref[h], scale_row)
    key_rows = lax.broadcasted_iota(jnp.int32, ((slots + 1) * width, 1), 0)

    def block(b, carry):
        for s in range(slots):
            pair_copy(b * slots + s).wait()
        live_col = jnp.ones(((slots + 1) * width, 1), jnp.float32)
        for s in range(slots):
            inside = (key_rows >= (s + 1) * width) & (key_rows < (s + 2) * width)
            live_col = jnp.where(inside, live_ref[b * slots + s].astype(jnp.float32), live_col)
        blocks = [own_ref[b]] + [buf[b * slots + s] for s in range(slots)]
        keys = jnp.concatenate([blk[:width] for blk in blocks], axis=0)
        values_t = jnp.concatenate([blk[width:] for blk in blocks], axis=1)
        s_all = jnp.dot(keys, q_ref[b], preferred_element_type=jnp.float32)
        w = jnp.exp(scale_row * (s_all - 1.0)) * live_col
        den = jnp.sum(w, axis=0, keepdims=True)
        w_b = w.astype(jnp.bfloat16)
        num = jnp.zeros((feat, width), jnp.float32)
        den_full = jnp.zeros((feat, width), jnp.float32)
        for h in range(count):
            part = jnp.dot(values_t, w_b[:, h * width:(h + 1) * width], preferred_element_type=jnp.float32)
            num = jnp.where(row_head == h, part, num)
            den_full = jnp.where(row_head == h, den[:, h * width:(h + 1) * width], den_full)
        out_ref[b] = (num / den_full).astype(out_ref.dtype)
        return carry

    lax.fori_loop(0, nblocks, block, 0)


def attend(query_stack, own_kv, recv_kv, slot_of, live, scales):
    nblocks, feat, lanes = query_stack.shape
    count = scales.shape[0]
    width = lanes // count
    slots = slot_of.shape[0] // nblocks
    grid_spec = pltpu.PrefetchScalarGridSpec(
        num_scalar_prefetch=2,
        grid=(1,),
        in_specs=[
            pl.BlockSpec(memory_space=pltpu.SMEM),
            pl.BlockSpec((nblocks, feat, lanes), lambda i, slot_of, live: (0, 0, 0)),
            pl.BlockSpec((nblocks, 2 * width, feat), lambda i, slot_of, live: (0, 0, 0)),
            pl.BlockSpec(memory_space=pl.ANY),
        ],
        out_specs=pl.BlockSpec((nblocks, feat, width), lambda i, slot_of, live: (0, 0, 0)),
        scratch_shapes=[
            pltpu.VMEM((nblocks * slots, 2 * width, feat), recv_kv.dtype),
            pltpu.SemaphoreType.DMA((nblocks * slots,)),
        ],
    )
    return pl.pallas_call(
        functools.partial(attend_kernel, count=count, slots=slots),
        grid_spec=grid_spec,
        out_shape=jax.ShapeDtypeStruct((nblocks, feat, width), jnp.bfloat16),
        compiler_params=pltpu.CompilerParams(vmem_limit_bytes=48 * 1024 * 1024),
    )(slot_of, live, scales, query_stack, own_kv, recv_kv)


def gather_kernel(pick_ref, src_ref, out_ref):
    g = pl.program_id(0)
    group = out_ref.shape[0]
    for i in range(group):
        out_ref[i] = src_ref[pick_ref[g * group + i]]


def gather_blocks(blocks, pick):
    nblocks, r, l = blocks.shape
    tiles = pick.shape[0]
    group = 32
    grid_spec = pltpu.PrefetchScalarGridSpec(
        num_scalar_prefetch=1,
        grid=(tiles // group,),
        in_specs=[pl.BlockSpec((nblocks, r, l), lambda g, pick: (0, 0, 0))],
        out_specs=pl.BlockSpec((group, r, l), lambda g, pick: (g, 0, 0)),
    )
    return pl.pallas_call(
        gather_kernel,
        grid_spec=grid_spec,
        out_shape=jax.ShapeDtypeStruct((tiles, r, l), blocks.dtype),
    )(pick, blocks)


def body(feats, w_query, w_key, w_value, w_out, head_scale, nbr_owner, nbr_local, slot_valid):
    rows = feats.shape[0]
    feat = w_query.shape[1]
    count = head_scale.shape[0]
    nblocks, slots = nbr_owner.shape
    width = rows // nblocks
    devices = lax.axis_size("nodes")
    capacity = max(2, min(nblocks // 2, 3 * nblocks * slots // (2 * devices)))
    tile_count = devices * capacity
    query_n = unit_rows(jnp.dot(feats, w_query, preferred_element_type=jnp.float32), count)
    key_n = unit_rows(jnp.dot(feats, w_key, preferred_element_type=jnp.float32), count)
    value_b = jnp.dot(feats, w_value, preferred_element_type=jnp.float32).astype(jnp.bfloat16)
    query_t = jnp.swapaxes(query_n.reshape(nblocks, width, feat), 1, 2)
    head_of = jnp.arange(feat, dtype=jnp.int32) // (feat // count)
    query_stack = jnp.concatenate(
        [jnp.where(head_of[None, :, None] == h, query_t, 0) for h in range(count)], axis=2
    )
    own_kv = jnp.concatenate(
        [key_n.reshape(nblocks, width, feat), jnp.swapaxes(value_b.reshape(nblocks, width, feat), 1, 2)],
        axis=1,
    )
    owners = nbr_owner.reshape(-1)
    owner_hot = (owners[:, None] == jnp.arange(devices, dtype=jnp.int32)[None, :]).astype(jnp.int32)
    rank = jnp.sum(jnp.cumsum(owner_hot, axis=0) * owner_hot, axis=1) - 1
    target = owners * capacity + rank
    place = (target[:, None] == jnp.arange(tile_count, dtype=jnp.int32)[None, :]).astype(jnp.int32)
    valid = (slot_valid.reshape(-1) > 0).astype(jnp.int32)
    wanted = jnp.where(valid > 0, nbr_local.reshape(-1), -1)
    request = jnp.sum(place * (wanted[:, None] + 1), axis=0) - 1
    asked = lax.all_to_all(
        request.reshape(devices, capacity), "nodes", split_axis=0, concat_axis=0, tiled=True
    ).reshape(-1)
    payload = gather_blocks(own_kv, jnp.clip(asked, 0, nblocks - 1).astype(jnp.int32))
    w_out, payload = lax.optimization_barrier((w_out, payload))
    w_out_t = lax.all_gather(w_out.T, "heads", axis=1, tiled=True)
    recv_kv = lax.all_to_all(
        payload.reshape(devices, capacity * 2 * width, feat),
        "nodes",
        split_axis=0,
        concat_axis=0,
        tiled=True,
    ).reshape(tile_count, 2 * width, feat)
    recv_kv, w_out_t = lax.optimization_barrier((recv_kv, w_out_t))
    slot_of = jnp.clip(target, 0, tile_count - 1).astype(jnp.int32)
    attn_t = attend(query_stack, own_kv, recv_kv, slot_of, valid, head_scale)
    attn = jnp.swapaxes(attn_t, 1, 2).reshape(rows, feat)
    heads = lax.axis_size("heads")
    me = lax.axis_index("heads")

    def out_part(piece, source):
        w_part = lax.dynamic_slice(w_out_t, (me * feat, source * feat), (feat, feat))
        return lax.dot_general(
            piece, w_part, (((1,), (1,)), ((), ())), preferred_element_type=jnp.float32
        )

    mixed = out_part(attn, me)
    for k in range(1, heads):
        piece = lax.ppermute(attn, "heads", [(j, (j + k) % heads) for j in range(heads)])
        mixed = mixed + out_part(piece, (me - k) % heads)
    return mixed.astype(jnp.bfloat16)


def solution(mesh):
    placed = (
        P("nodes", None),
        P(None, "heads"),
        P(None, "heads"),
        P(None, "heads"),
        P("heads", None),
        P("heads"),
        P("nodes", None),
        P("nodes", None),
        P("nodes", None),
    )
    return jax.shard_map(
        body, mesh=mesh, in_specs=placed, out_specs=P("nodes", "heads"), check_vma=False
    )
```

```python
import functools

import jax
import jax.numpy as jnp
from jax import lax
from jax.experimental import pallas as pl
from jax.experimental.pallas import tpu as pltpu
from jax.sharding import PartitionSpec as P


def unit_rows(values, count):
    shaped = values.reshape(values.shape[0], count, -1)
    total = jnp.sum(shaped * shaped, axis=-1, keepdims=True)
    return (shaped * lax.rsqrt(total + 1e-06)).astype(jnp.bfloat16).reshape(values.shape)


def attend_kernel(slot_ref, live_ref, scale_ref, q_ref, own_ref, recv_ref, out_ref, buf, sems, *, count, slots):
    b = pl.program_id(0)
    pairs = buf.shape[0]
    feat, lanes = q_ref.shape[1], q_ref.shape[2]
    width = lanes // count
    hd = feat // count

    def pair_copy(p):
        return pltpu.make_async_copy(recv_ref.at[slot_ref[p]], buf.at[p], sems.at[p])

    @pl.when(b == 0)
    def _():
        for p in range(pairs):
            pair_copy(p).start()

    for s in range(slots):
        pair_copy(b * slots + s).wait()
    q_stack = q_ref[0]
    row_head = lax.broadcasted_iota(jnp.int32, (feat, width), 0) // hd
    lane_pos = lax.broadcasted_iota(jnp.int32, (1, lanes), 1)
    scale_row = jnp.zeros((1, lanes), jnp.float32)
    for h in range(count):
        inside = (lane_pos >= h * width) & (lane_pos < (h + 1) * width)
        scale_row = jnp.where(inside, scale_ref[h], scale_row)
    key_rows = lax.broadcasted_iota(jnp.int32, ((slots + 1) * width, 1), 0)
    live_col = jnp.ones(((slots + 1) * width, 1), jnp.float32)
    for s in range(slots):
        inside = (key_rows >= (s + 1) * width) & (key_rows < (s + 2) * width)
        live_col = jnp.where(inside, live_ref[b * slots + s].astype(jnp.float32), live_col)
    blocks = [own_ref[b]] + [buf[b * slots + s] for s in range(slots)]
    keys = jnp.concatenate([blk[:width] for blk in blocks], axis=0)
    values_t = jnp.concatenate([blk[width:] for blk in blocks], axis=1)
    s_all = jnp.dot(keys, q_stack, preferred_element_type=jnp.float32)
    w = jnp.exp(scale_row * (s_all - 1.0)) * live_col
    den = jnp.sum(w, axis=0, keepdims=True)
    w_b = w.astype(jnp.bfloat16)
    num = jnp.zeros((feat, width), jnp.float32)
    den_full = jnp.zeros((feat, width), jnp.float32)
    for h in range(count):
        part = jnp.dot(values_t, w_b[:, h * width:(h + 1) * width], preferred_element_type=jnp.float32)
        num = jnp.where(row_head == h, part, num)
        den_full = jnp.where(row_head == h, den[:, h * width:(h + 1) * width], den_full)
    out_ref[0] = (num / den_full).astype(out_ref.dtype)


def attend(query_stack, own_kv, recv_kv, slot_of, live, scales):
    nblocks, feat, lanes = query_stack.shape
    count = scales.shape[0]
    width = lanes // count
    slots = slot_of.shape[0] // nblocks
    grid_spec = pltpu.PrefetchScalarGridSpec(
        num_scalar_prefetch=2,
        grid=(nblocks,),
        in_specs=[
            pl.BlockSpec(memory_space=pltpu.SMEM),
            pl.BlockSpec((1, feat, lanes), lambda b, slot_of, live: (b, 0, 0)),
            pl.BlockSpec((nblocks, 2 * width, feat), lambda b, slot_of, live: (0, 0, 0)),
            pl.BlockSpec(memory_space=pl.ANY),
        ],
        out_specs=pl.BlockSpec((1, feat, width), lambda b, slot_of, live: (b, 0, 0)),
        scratch_shapes=[
            pltpu.VMEM((nblocks * slots, 2 * width, feat), recv_kv.dtype),
            pltpu.SemaphoreType.DMA((nblocks * slots,)),
        ],
    )
    return pl.pallas_call(
        functools.partial(attend_kernel, count=count, slots=slots),
        grid_spec=grid_spec,
        out_shape=jax.ShapeDtypeStruct((nblocks, feat, width), jnp.bfloat16),
        compiler_params=pltpu.CompilerParams(vmem_limit_bytes=48 * 1024 * 1024),
    )(slot_of, live, scales, query_stack, own_kv, recv_kv)


def gather_kernel(pick_ref, src_ref, out_ref):
    g = pl.program_id(0)
    group = out_ref.shape[0]
    for i in range(group):
        out_ref[i] = src_ref[pick_ref[g * group + i]]


def gather_blocks(blocks, pick):
    nblocks, r, l = blocks.shape
    tiles = pick.shape[0]
    group = 32
    grid_spec = pltpu.PrefetchScalarGridSpec(
        num_scalar_prefetch=1,
        grid=(tiles // group,),
        in_specs=[pl.BlockSpec((nblocks, r, l), lambda g, pick: (0, 0, 0))],
        out_specs=pl.BlockSpec((group, r, l), lambda g, pick: (g, 0, 0)),
    )
    return pl.pallas_call(
        gather_kernel,
        grid_spec=grid_spec,
        out_shape=jax.ShapeDtypeStruct((tiles, r, l), blocks.dtype),
    )(pick, blocks)


def body(feats, w_query, w_key, w_value, w_out, head_scale, nbr_owner, nbr_local, slot_valid):
    rows = feats.shape[0]
    feat = w_query.shape[1]
    count = head_scale.shape[0]
    nblocks, slots = nbr_owner.shape
    width = rows // nblocks
    devices = lax.axis_size("nodes")
    capacity = max(2, min(nblocks // 2, 3 * nblocks * slots // (2 * devices)))
    tile_count = devices * capacity
    query_n = unit_rows(jnp.dot(feats, w_query, preferred_element_type=jnp.float32), count)
    key_n = unit_rows(jnp.dot(feats, w_key, preferred_element_type=jnp.float32), count)
    value_b = jnp.dot(feats, w_value, preferred_element_type=jnp.float32).astype(jnp.bfloat16)
    query_t = jnp.swapaxes(query_n.reshape(nblocks, width, feat), 1, 2)
    head_of = jnp.arange(feat, dtype=jnp.int32) // (feat // count)
    query_stack = jnp.concatenate(
        [jnp.where(head_of[None, :, None] == h, query_t, 0) for h in range(count)], axis=2
    )
    own_kv = jnp.concatenate(
        [key_n.reshape(nblocks, width, feat), jnp.swapaxes(value_b.reshape(nblocks, width, feat), 1, 2)],
        axis=1,
    )
    owners = nbr_owner.reshape(-1)
    owner_hot = (owners[:, None] == jnp.arange(devices, dtype=jnp.int32)[None, :]).astype(jnp.int32)
    rank = jnp.sum(jnp.cumsum(owner_hot, axis=0) * owner_hot, axis=1) - 1
    target = owners * capacity + rank
    place = (target[:, None] == jnp.arange(tile_count, dtype=jnp.int32)[None, :]).astype(jnp.int32)
    valid = (slot_valid.reshape(-1) > 0).astype(jnp.int32)
    wanted = jnp.where(valid > 0, nbr_local.reshape(-1), -1)
    request = jnp.sum(place * (wanted[:, None] + 1), axis=0) - 1
    asked = lax.all_to_all(
        request.reshape(devices, capacity), "nodes", split_axis=0, concat_axis=0, tiled=True
    ).reshape(-1)
    heads = lax.axis_size("heads")
    me = lax.axis_index("heads")
    quarter = width // heads
    model = feats.shape[1]
    feats_parts = feats.reshape(nblocks * heads, quarter, model)
    pick = jnp.clip(asked, 0, nblocks - 1).astype(jnp.int32) * heads + me
    payload = gather_blocks(feats_parts, pick)
    w_out, payload = lax.optimization_barrier((w_out, payload))
    w_out_t = lax.all_gather(w_out.T, "heads", axis=1, tiled=True)
    recv = lax.all_to_all(
        payload.reshape(devices, capacity * quarter, model),
        "nodes",
        split_axis=0,
        concat_axis=0,
        tiled=True,
    ).reshape(tile_count, quarter, model)
    recv, w_out_t = lax.optimization_barrier((recv, w_out_t))
    slot_of = jnp.clip(target, 0, tile_count - 1).astype(jnp.int32)
    piece = gather_blocks(recv, slot_of)
    pair_rows = lax.all_gather(piece, "heads", axis=1, tiled=True)
    pairs = pair_rows.shape[0]
    pair_k = unit_rows(
        jnp.dot(pair_rows.reshape(-1, model), w_key, preferred_element_type=jnp.float32), count
    )
    pair_v = jnp.dot(
        pair_rows.reshape(-1, model), w_value, preferred_element_type=jnp.float32
    ).astype(jnp.bfloat16)
    pair_kv = jnp.concatenate(
        [
            pair_k.reshape(pairs, width, feat),
            jnp.swapaxes(pair_v.reshape(pairs, width, feat), 1, 2),
        ],
        axis=1,
    )
    pair_ids = jnp.arange(pairs, dtype=jnp.int32)
    attn_t = attend(query_stack, own_kv, pair_kv, pair_ids, valid, head_scale)
    attn = jnp.swapaxes(attn_t, 1, 2).reshape(rows, feat)
    heads = lax.axis_size("heads")
    me = lax.axis_index("heads")

    def out_part(piece, source):
        w_part = lax.dynamic_slice(w_out_t, (me * feat, source * feat), (feat, feat))
        return lax.dot_general(
            piece, w_part, (((1,), (1,)), ((), ())), preferred_element_type=jnp.float32
        )

    mixed = out_part(attn, me)
    for k in range(1, heads):
        piece = lax.ppermute(attn, "heads", [(j, (j + k) % heads) for j in range(heads)])
        mixed = mixed + out_part(piece, (me - k) % heads)
    return mixed.astype(jnp.bfloat16)


def solution(mesh):
    placed = (
        P("nodes", None),
        P(None, "heads"),
        P(None, "heads"),
        P(None, "heads"),
        P("heads", None),
        P("heads"),
        P("nodes", None),
        P("nodes", None),
        P("nodes", None),
    )
    return jax.shard_map(
        body, mesh=mesh, in_specs=placed, out_specs=P("nodes", "heads"), check_vma=False
    )
```

```python
import functools

import jax
import jax.numpy as jnp
from jax import lax
from jax.experimental import pallas as pl
from jax.experimental.pallas import tpu as pltpu
from jax.sharding import PartitionSpec as P


def unit_rows(values, count):
    shaped = values.reshape(values.shape[0], count, -1)
    total = jnp.sum(shaped * shaped, axis=-1, keepdims=True)
    return (shaped * lax.rsqrt(total + 1e-06)).astype(jnp.bfloat16).reshape(values.shape)


def attend_kernel(slot_ref, live_ref, scale_ref, q_ref, own_ref, recv_ref, out_ref, buf, sems, *, count, slots):
    b = pl.program_id(0)
    pairs = buf.shape[0]
    feat, lanes = q_ref.shape[1], q_ref.shape[2]
    width = lanes // count
    hd = feat // count

    def pair_copy(p):
        return pltpu.make_async_copy(recv_ref.at[slot_ref[p]], buf.at[p], sems.at[p])

    @pl.when(b == 0)
    def _():
        for p in range(pairs):
            pair_copy(p).start()

    for s in range(slots):
        pair_copy(b * slots + s).wait()
    q_stack = q_ref[0]
    row_head = lax.broadcasted_iota(jnp.int32, (feat, width), 0) // hd
    lane_pos = lax.broadcasted_iota(jnp.int32, (1, lanes), 1)
    scale_row = jnp.zeros((1, lanes), jnp.float32)
    for h in range(count):
        inside = (lane_pos >= h * width) & (lane_pos < (h + 1) * width)
        scale_row = jnp.where(inside, scale_ref[h], scale_row)
    key_rows = lax.broadcasted_iota(jnp.int32, ((slots + 1) * width, 1), 0)
    live_col = jnp.ones(((slots + 1) * width, 1), jnp.float32)
    for s in range(slots):
        inside = (key_rows >= (s + 1) * width) & (key_rows < (s + 2) * width)
        live_col = jnp.where(inside, live_ref[b * slots + s].astype(jnp.float32), live_col)
    blocks = [own_ref[b]] + [buf[b * slots + s] for s in range(slots)]
    keys = jnp.concatenate([blk[:width] for blk in blocks], axis=0)
    values_t = jnp.concatenate([blk[width:] for blk in blocks], axis=1)
    s_all = jnp.dot(keys, q_stack, preferred_element_type=jnp.float32)
    w = jnp.exp(scale_row * (s_all - 1.0)) * live_col
    den = jnp.sum(w, axis=0, keepdims=True)
    w_b = w.astype(jnp.bfloat16)
    num = jnp.zeros((feat, width), jnp.float32)
    den_full = jnp.zeros((feat, width), jnp.float32)
    for h in range(count):
        part = jnp.dot(values_t, w_b[:, h * width:(h + 1) * width], preferred_element_type=jnp.float32)
        num = jnp.where(row_head == h, part, num)
        den_full = jnp.where(row_head == h, den[:, h * width:(h + 1) * width], den_full)
    out_ref[0] = (num / den_full).astype(out_ref.dtype)


def attend(query_stack, own_kv, recv_kv, slot_of, live, scales):
    nblocks, feat, lanes = query_stack.shape
    count = scales.shape[0]
    width = lanes // count
    slots = slot_of.shape[0] // nblocks
    grid_spec = pltpu.PrefetchScalarGridSpec(
        num_scalar_prefetch=2,
        grid=(nblocks,),
        in_specs=[
            pl.BlockSpec(memory_space=pltpu.SMEM),
            pl.BlockSpec((1, feat, lanes), lambda b, slot_of, live: (b, 0, 0)),
            pl.BlockSpec((nblocks, 2 * width, feat), lambda b, slot_of, live: (0, 0, 0)),
            pl.BlockSpec(memory_space=pl.ANY),
        ],
        out_specs=pl.BlockSpec((1, feat, width), lambda b, slot_of, live: (b, 0, 0)),
        scratch_shapes=[
            pltpu.VMEM((nblocks * slots, 2 * width, feat), recv_kv.dtype),
            pltpu.SemaphoreType.DMA((nblocks * slots,)),
        ],
    )
    return pl.pallas_call(
        functools.partial(attend_kernel, count=count, slots=slots),
        grid_spec=grid_spec,
        out_shape=jax.ShapeDtypeStruct((nblocks, feat, width), jnp.bfloat16),
        compiler_params=pltpu.CompilerParams(vmem_limit_bytes=48 * 1024 * 1024),
    )(slot_of, live, scales, query_stack, own_kv, recv_kv)


def gather_kernel(pick_ref, src_ref, out_ref):
    g = pl.program_id(0)
    group = out_ref.shape[0]
    for i in range(group):
        out_ref[i] = src_ref[pick_ref[g * group + i]]


def gather_blocks(blocks, pick):
    nblocks, r, l = blocks.shape
    tiles = pick.shape[0]
    group = 32
    grid_spec = pltpu.PrefetchScalarGridSpec(
        num_scalar_prefetch=1,
        grid=(tiles // group,),
        in_specs=[pl.BlockSpec((nblocks, r, l), lambda g, pick: (0, 0, 0))],
        out_specs=pl.BlockSpec((group, r, l), lambda g, pick: (g, 0, 0)),
    )
    return pl.pallas_call(
        gather_kernel,
        grid_spec=grid_spec,
        out_shape=jax.ShapeDtypeStruct((tiles, r, l), blocks.dtype),
    )(pick, blocks)


def body(feats, w_query, w_key, w_value, w_out, head_scale, nbr_owner, nbr_local, slot_valid):
    rows = feats.shape[0]
    feat = w_query.shape[1]
    count = head_scale.shape[0]
    nblocks, slots = nbr_owner.shape
    width = rows // nblocks
    devices = lax.axis_size("nodes")
    capacity = max(2, min(nblocks // 2, 3 * nblocks * slots // (2 * devices)))
    tile_count = devices * capacity
    query_n = unit_rows(jnp.dot(feats, w_query, preferred_element_type=jnp.float32), count)
    key_n = unit_rows(jnp.dot(feats, w_key, preferred_element_type=jnp.float32), count)
    value_b = jnp.dot(feats, w_value, preferred_element_type=jnp.float32).astype(jnp.bfloat16)
    query_t = jnp.swapaxes(query_n.reshape(nblocks, width, feat), 1, 2)
    head_of = jnp.arange(feat, dtype=jnp.int32) // (feat // count)
    query_stack = jnp.concatenate(
        [jnp.where(head_of[None, :, None] == h, query_t, 0) for h in range(count)], axis=2
    )
    own_kv = jnp.concatenate(
        [key_n.reshape(nblocks, width, feat), jnp.swapaxes(value_b.reshape(nblocks, width, feat), 1, 2)],
        axis=1,
    )
    owners = nbr_owner.reshape(-1)
    owner_hot = (owners[:, None] == jnp.arange(devices, dtype=jnp.int32)[None, :]).astype(jnp.int32)
    rank = jnp.sum(jnp.cumsum(owner_hot, axis=0) * owner_hot, axis=1) - 1
    target = owners * capacity + rank
    place = (target[:, None] == jnp.arange(tile_count, dtype=jnp.int32)[None, :]).astype(jnp.int32)
    valid = (slot_valid.reshape(-1) > 0).astype(jnp.int32)
    wanted = jnp.where(valid > 0, nbr_local.reshape(-1), -1)
    request = jnp.sum(place * (wanted[:, None] + 1), axis=0) - 1
    asked = lax.all_to_all(
        request.reshape(devices, capacity), "nodes", split_axis=0, concat_axis=0, tiled=True
    ).reshape(-1)
    heads = lax.axis_size("heads")
    me = lax.axis_index("heads")
    quarter = width // heads
    model = feats.shape[1]
    feats_parts = feats.reshape(nblocks * heads, quarter, model)
    pick = jnp.clip(asked, 0, nblocks - 1).astype(jnp.int32) * heads + me
    payload = gather_blocks(feats_parts, pick)
    w_out, w_key_b, w_value_b, payload = lax.optimization_barrier((w_out, w_key, w_value, payload))
    w_out_t = lax.all_gather(w_out.T, "heads", axis=1, tiled=True)
    w_key_all = lax.all_gather(w_key_b, "heads", axis=1, tiled=True).reshape(model, heads, feat)
    w_value_all = lax.all_gather(w_value_b, "heads", axis=1, tiled=True).reshape(model, heads, feat)
    w_kv_all = jnp.stack([w_key_all, w_value_all], axis=2).reshape(model, heads * 2 * feat)
    recv = lax.all_to_all(
        payload.reshape(devices, capacity * quarter, model),
        "nodes",
        split_axis=0,
        concat_axis=0,
        tiled=True,
    ).reshape(tile_count, quarter, model)
    recv, w_out_t, w_kv_all = lax.optimization_barrier((recv, w_out_t, w_kv_all))
    slot_of = jnp.clip(target, 0, tile_count - 1).astype(jnp.int32)
    piece = gather_blocks(recv, slot_of)
    pairs = piece.shape[0]
    kv_all = jnp.dot(
        piece.reshape(pairs * quarter, model), w_kv_all, preferred_element_type=jnp.float32
    ).reshape(pairs * quarter, heads, 2, feat)
    k_all = unit_rows(kv_all[:, :, 0, :].reshape(pairs * quarter, heads * feat), heads * count)
    v_all = kv_all[:, :, 1, :].astype(jnp.bfloat16)
    send = jnp.concatenate(
        [k_all.reshape(pairs * quarter, heads, feat), v_all], axis=2
    ).reshape(pairs, quarter, heads, 2 * feat)
    send = jnp.transpose(send, (2, 0, 1, 3))
    got = lax.all_to_all(send, "heads", 0, 0, tiled=True)
    got = jnp.transpose(got, (1, 0, 2, 3)).reshape(pairs, width, 2 * feat)
    pair_kv = jnp.concatenate([got[:, :, :feat], jnp.swapaxes(got[:, :, feat:], 1, 2)], axis=1)
    pair_ids = jnp.arange(pairs, dtype=jnp.int32)
    attn_t = attend(query_stack, own_kv, pair_kv, pair_ids, valid, head_scale)
    attn = jnp.swapaxes(attn_t, 1, 2).reshape(rows, feat)
    heads = lax.axis_size("heads")
    me = lax.axis_index("heads")

    def out_part(piece, source):
        w_part = lax.dynamic_slice(w_out_t, (me * feat, source * feat), (feat, feat))
        return lax.dot_general(
            piece, w_part, (((1,), (1,)), ((), ())), preferred_element_type=jnp.float32
        )

    mixed = out_part(attn, me)
    for k in range(1, heads):
        piece = lax.ppermute(attn, "heads", [(j, (j + k) % heads) for j in range(heads)])
        mixed = mixed + out_part(piece, (me - k) % heads)
    return mixed.astype(jnp.bfloat16)


def solution(mesh):
    placed = (
        P("nodes", None),
        P(None, "heads"),
        P(None, "heads"),
        P(None, "heads"),
        P("heads", None),
        P("heads"),
        P("nodes", None),
        P("nodes", None),
        P("nodes", None),
    )
    return jax.shard_map(
        body, mesh=mesh, in_specs=placed, out_specs=P("nodes", "heads"), check_vma=False
    )
```

```python
import functools

import jax
import jax.numpy as jnp
from jax import lax
from jax.experimental import pallas as pl
from jax.experimental.pallas import tpu as pltpu
from jax.sharding import PartitionSpec as P


def unit_rows(values, count):
    shaped = values.reshape(values.shape[0], count, -1)
    total = jnp.sum(shaped * shaped, axis=-1, keepdims=True)
    return (shaped * lax.rsqrt(total + 1e-06)).astype(jnp.bfloat16).reshape(values.shape)


def attend_kernel(slot_ref, live_ref, scale_ref, q_ref, own_ref, recv_ref, out_ref, buf, sems, *, count, slots):
    b = pl.program_id(0)
    pairs = buf.shape[0]
    feat, lanes = q_ref.shape[1], q_ref.shape[2]
    width = lanes // count
    hd = feat // count

    def pair_copy(p):
        return pltpu.make_async_copy(recv_ref.at[slot_ref[p]], buf.at[p], sems.at[p])

    @pl.when(b == 0)
    def _():
        for p in range(pairs):
            pair_copy(p).start()

    for s in range(slots):
        pair_copy(b * slots + s).wait()
    q_stack = q_ref[0]
    row_head = lax.broadcasted_iota(jnp.int32, (feat, width), 0) // hd
    lane_pos = lax.broadcasted_iota(jnp.int32, (1, lanes), 1)
    scale_row = jnp.zeros((1, lanes), jnp.float32)
    for h in range(count):
        inside = (lane_pos >= h * width) & (lane_pos < (h + 1) * width)
        scale_row = jnp.where(inside, scale_ref[h], scale_row)
    key_rows = lax.broadcasted_iota(jnp.int32, ((slots + 1) * width, 1), 0)
    live_col = jnp.ones(((slots + 1) * width, 1), jnp.float32)
    for s in range(slots):
        inside = (key_rows >= (s + 1) * width) & (key_rows < (s + 2) * width)
        live_col = jnp.where(inside, live_ref[b * slots + s].astype(jnp.float32), live_col)
    blocks = [own_ref[b]] + [buf[b * slots + s] for s in range(slots)]
    keys = jnp.concatenate([blk[:width] for blk in blocks], axis=0)
    values_t = jnp.concatenate([blk[width:] for blk in blocks], axis=1)
    s_all = jnp.dot(keys, q_stack, preferred_element_type=jnp.float32)
    w = jnp.exp(scale_row * (s_all - 1.0)) * live_col
    den = jnp.sum(w, axis=0, keepdims=True)
    w_b = w.astype(jnp.bfloat16)
    num = jnp.zeros((feat, width), jnp.float32)
    den_full = jnp.zeros((feat, width), jnp.float32)
    for h in range(count):
        part = jnp.dot(values_t, w_b[:, h * width:(h + 1) * width], preferred_element_type=jnp.float32)
        num = jnp.where(row_head == h, part, num)
        den_full = jnp.where(row_head == h, den[:, h * width:(h + 1) * width], den_full)
    out_ref[0] = (num / den_full).astype(out_ref.dtype)


def attend(query_stack, own_kv, recv_kv, slot_of, live, scales):
    nblocks, feat, lanes = query_stack.shape
    count = scales.shape[0]
    width = lanes // count
    slots = slot_of.shape[0] // nblocks
    grid_spec = pltpu.PrefetchScalarGridSpec(
        num_scalar_prefetch=2,
        grid=(nblocks,),
        in_specs=[
            pl.BlockSpec(memory_space=pltpu.SMEM),
            pl.BlockSpec((1, feat, lanes), lambda b, slot_of, live: (b, 0, 0)),
            pl.BlockSpec((nblocks, 2 * width, feat), lambda b, slot_of, live: (0, 0, 0)),
            pl.BlockSpec(memory_space=pl.ANY),
        ],
        out_specs=pl.BlockSpec((1, feat, width), lambda b, slot_of, live: (b, 0, 0)),
        scratch_shapes=[
            pltpu.VMEM((nblocks * slots, 2 * width, feat), recv_kv.dtype),
            pltpu.SemaphoreType.DMA((nblocks * slots,)),
        ],
    )
    return pl.pallas_call(
        functools.partial(attend_kernel, count=count, slots=slots),
        grid_spec=grid_spec,
        out_shape=jax.ShapeDtypeStruct((nblocks, feat, width), jnp.bfloat16),
        compiler_params=pltpu.CompilerParams(vmem_limit_bytes=48 * 1024 * 1024),
    )(slot_of, live, scales, query_stack, own_kv, recv_kv)


def gather_kernel(pick_ref, src_ref, out_ref):
    g = pl.program_id(0)
    group = out_ref.shape[0]
    for i in range(group):
        out_ref[i] = src_ref[pick_ref[g * group + i]]


def gather_blocks(blocks, pick):
    nblocks, r, l = blocks.shape
    tiles = pick.shape[0]
    group = 32
    grid_spec = pltpu.PrefetchScalarGridSpec(
        num_scalar_prefetch=1,
        grid=(tiles // group,),
        in_specs=[pl.BlockSpec((nblocks, r, l), lambda g, pick: (0, 0, 0))],
        out_specs=pl.BlockSpec((group, r, l), lambda g, pick: (g, 0, 0)),
    )
    return pl.pallas_call(
        gather_kernel,
        grid_spec=grid_spec,
        out_shape=jax.ShapeDtypeStruct((tiles, r, l), blocks.dtype),
    )(pick, blocks)


def project_kernel(x_ref, w_ref, out_ref, *, hd):
    kv = jnp.dot(x_ref[...], w_ref[...], preferred_element_type=jnp.float32)
    feat = kv.shape[1] // 2
    keys = kv[:, :feat]
    lane = lax.broadcasted_iota(jnp.int32, (1, feat), 1)
    sq = keys * keys
    scale = jnp.zeros(keys.shape, jnp.float32)
    for h in range(feat // hd):
        inside = (lane >= h * hd) & (lane < (h + 1) * hd)
        total = jnp.sum(jnp.where(inside, sq, 0.0), axis=1, keepdims=True)
        scale = jnp.where(inside, lax.rsqrt(total + 1e-06), scale)
    out_ref[0, :, :feat] = (keys * scale).astype(out_ref.dtype)
    out_ref[0, :, feat:] = kv[:, feat:].astype(out_ref.dtype)


def project_all(rows, w_kv, heads, hd):
    n, model = rows.shape
    cols = w_kv.shape[1] // heads
    return pl.pallas_call(
        functools.partial(project_kernel, hd=hd),
        grid=(heads,),
        in_specs=[
            pl.BlockSpec((n, model), lambda y: (0, 0)),
            pl.BlockSpec((model, cols), lambda y: (0, y)),
        ],
        out_specs=pl.BlockSpec((1, n, cols), lambda y: (y, 0, 0)),
        out_shape=jax.ShapeDtypeStruct((heads, n, cols), jnp.bfloat16),
    )(rows, w_kv)


def body(feats, w_query, w_key, w_value, w_out, head_scale, nbr_owner, nbr_local, slot_valid):
    rows = feats.shape[0]
    feat = w_query.shape[1]
    count = head_scale.shape[0]
    nblocks, slots = nbr_owner.shape
    width = rows // nblocks
    devices = lax.axis_size("nodes")
    capacity = max(2, min(nblocks // 2, 3 * nblocks * slots // (2 * devices)))
    tile_count = devices * capacity
    query_n = unit_rows(jnp.dot(feats, w_query, preferred_element_type=jnp.float32), count)
    key_n = unit_rows(jnp.dot(feats, w_key, preferred_element_type=jnp.float32), count)
    value_b = jnp.dot(feats, w_value, preferred_element_type=jnp.float32).astype(jnp.bfloat16)
    query_t = jnp.swapaxes(query_n.reshape(nblocks, width, feat), 1, 2)
    head_of = jnp.arange(feat, dtype=jnp.int32) // (feat // count)
    query_stack = jnp.concatenate(
        [jnp.where(head_of[None, :, None] == h, query_t, 0) for h in range(count)], axis=2
    )
    own_kv = jnp.concatenate(
        [key_n.reshape(nblocks, width, feat), jnp.swapaxes(value_b.reshape(nblocks, width, feat), 1, 2)],
        axis=1,
    )
    owners = nbr_owner.reshape(-1)
    owner_hot = (owners[:, None] == jnp.arange(devices, dtype=jnp.int32)[None, :]).astype(jnp.int32)
    rank = jnp.sum(jnp.cumsum(owner_hot, axis=0) * owner_hot, axis=1) - 1
    target = owners * capacity + rank
    place = (target[:, None] == jnp.arange(tile_count, dtype=jnp.int32)[None, :]).astype(jnp.int32)
    valid = (slot_valid.reshape(-1) > 0).astype(jnp.int32)
    wanted = jnp.where(valid > 0, nbr_local.reshape(-1), -1)
    request = jnp.sum(place * (wanted[:, None] + 1), axis=0) - 1
    asked = lax.all_to_all(
        request.reshape(devices, capacity), "nodes", split_axis=0, concat_axis=0, tiled=True
    ).reshape(-1)
    heads = lax.axis_size("heads")
    me = lax.axis_index("heads")
    quarter = width // heads
    model = feats.shape[1]
    feats_parts = feats.reshape(nblocks * heads, quarter, model)
    pick = jnp.clip(asked, 0, nblocks - 1).astype(jnp.int32) * heads + me
    payload = gather_blocks(feats_parts, pick)
    w_out, w_key_b, w_value_b, payload = lax.optimization_barrier((w_out, w_key, w_value, payload))
    w_out_t = lax.all_gather(w_out.T, "heads", axis=1, tiled=True)
    w_key_all = lax.all_gather(w_key_b, "heads", axis=1, tiled=True).reshape(model, heads, feat)
    w_value_all = lax.all_gather(w_value_b, "heads", axis=1, tiled=True).reshape(model, heads, feat)
    w_kv_all = jnp.stack([w_key_all, w_value_all], axis=2).reshape(model, heads * 2 * feat)
    recv = lax.all_to_all(
        payload.reshape(devices, capacity * quarter, model),
        "nodes",
        split_axis=0,
        concat_axis=0,
        tiled=True,
    ).reshape(tile_count, quarter, model)
    recv, w_out_t, w_kv_all = lax.optimization_barrier((recv, w_out_t, w_kv_all))
    slot_of = jnp.clip(target, 0, tile_count - 1).astype(jnp.int32)
    piece = gather_blocks(recv, slot_of)
    pairs = piece.shape[0]
    send = project_all(piece.reshape(pairs * quarter, model), w_kv_all, heads, feat // count).reshape(
        heads, pairs, quarter, 2 * feat
    )
    got = lax.all_to_all(send, "heads", 0, 0, tiled=True)
    got = jnp.transpose(got, (1, 0, 2, 3)).reshape(pairs, width, 2 * feat)
    pair_kv = jnp.concatenate([got[:, :, :feat], jnp.swapaxes(got[:, :, feat:], 1, 2)], axis=1)
    pair_ids = jnp.arange(pairs, dtype=jnp.int32)
    attn_t = attend(query_stack, own_kv, pair_kv, pair_ids, valid, head_scale)
    attn = jnp.swapaxes(attn_t, 1, 2).reshape(rows, feat)
    heads = lax.axis_size("heads")
    me = lax.axis_index("heads")

    def out_part(piece, source):
        w_part = lax.dynamic_slice(w_out_t, (me * feat, source * feat), (feat, feat))
        return lax.dot_general(
            piece, w_part, (((1,), (1,)), ((), ())), preferred_element_type=jnp.float32
        )

    mixed = out_part(attn, me)
    for k in range(1, heads):
        piece = lax.ppermute(attn, "heads", [(j, (j + k) % heads) for j in range(heads)])
        mixed = mixed + out_part(piece, (me - k) % heads)
    return mixed.astype(jnp.bfloat16)


def solution(mesh):
    placed = (
        P("nodes", None),
        P(None, "heads"),
        P(None, "heads"),
        P(None, "heads"),
        P("heads", None),
        P("heads"),
        P("nodes", None),
        P("nodes", None),
        P("nodes", None),
    )
    return jax.shard_map(
        body, mesh=mesh, in_specs=placed, out_specs=P("nodes", "heads"), check_vma=False
    )
```

```python
import functools

import jax
import jax.numpy as jnp
from jax import lax
from jax.experimental import pallas as pl
from jax.experimental.pallas import tpu as pltpu
from jax.sharding import PartitionSpec as P


def unit_rows(values, count):
    shaped = values.reshape(values.shape[0], count, -1)
    total = jnp.sum(shaped * shaped, axis=-1, keepdims=True)
    return (shaped * lax.rsqrt(total + 1e-06)).astype(jnp.bfloat16).reshape(values.shape)


def attend_kernel(slot_ref, live_ref, scale_ref, q_ref, own_ref, recv_ref, out_ref, buf, sems, *, count, slots):
    b = pl.program_id(0)
    pairs = buf.shape[0]
    stacked, feat = q_ref.shape[1], q_ref.shape[2]
    width = stacked // count
    hd = feat // count

    def pair_copy(p):
        return pltpu.make_async_copy(recv_ref.at[slot_ref[p]], buf.at[p], sems.at[p])

    @pl.when(b == 0)
    def _():
        for p in range(pairs):
            pair_copy(p).start()

    for s in range(slots):
        pair_copy(b * slots + s).wait()
    lane_head = lax.broadcasted_iota(jnp.int32, (width, feat), 1) // hd
    stack_rows = lax.broadcasted_iota(jnp.int32, (stacked, 1), 0)
    scale_col = jnp.zeros((stacked, 1), jnp.float32)
    for h in range(count):
        inside = (stack_rows >= h * width) & (stack_rows < (h + 1) * width)
        scale_col = jnp.where(inside, scale_ref[h], scale_col)
    key_lanes = lax.broadcasted_iota(jnp.int32, (1, (slots + 1) * width), 1)
    live_row = jnp.ones((1, (slots + 1) * width), jnp.float32)
    for s in range(slots):
        inside = (key_lanes >= (s + 1) * width) & (key_lanes < (s + 2) * width)
        live_row = jnp.where(inside, live_ref[b * slots + s].astype(jnp.float32), live_row)
    blocks = [own_ref[b]] + [buf[b * slots + s] for s in range(slots)]
    keys = jnp.concatenate([blk[:, :feat] for blk in blocks], axis=0)
    values = jnp.concatenate([blk[:, feat:] for blk in blocks], axis=0)
    s_all = lax.dot_general(
        q_ref[0], keys, (((1,), (1,)), ((), ())), preferred_element_type=jnp.float32
    )
    w = jnp.exp(scale_col * (s_all - 1.0)) * live_row
    den = jnp.sum(w, axis=1, keepdims=True)
    w_b = w.astype(jnp.bfloat16)
    num = jnp.zeros((width, feat), jnp.float32)
    den_full = jnp.zeros((width, feat), jnp.float32)
    for h in range(count):
        part = jnp.dot(w_b[h * width:(h + 1) * width], values, preferred_element_type=jnp.float32)
        num = jnp.where(lane_head == h, part, num)
        den_full = jnp.where(lane_head == h, den[h * width:(h + 1) * width], den_full)
    out_ref[0] = (num / den_full).astype(out_ref.dtype)


def attend(query_stack, own_kv, recv_kv, slot_of, live, scales):
    nblocks, stacked, feat = query_stack.shape
    count = scales.shape[0]
    width = stacked // count
    slots = slot_of.shape[0] // nblocks
    grid_spec = pltpu.PrefetchScalarGridSpec(
        num_scalar_prefetch=2,
        grid=(nblocks,),
        in_specs=[
            pl.BlockSpec(memory_space=pltpu.SMEM),
            pl.BlockSpec((1, stacked, feat), lambda b, slot_of, live: (b, 0, 0)),
            pl.BlockSpec((nblocks, width, 2 * feat), lambda b, slot_of, live: (0, 0, 0)),
            pl.BlockSpec(memory_space=pl.ANY),
        ],
        out_specs=pl.BlockSpec((1, width, feat), lambda b, slot_of, live: (b, 0, 0)),
        scratch_shapes=[
            pltpu.VMEM((nblocks * slots, width, 2 * feat), recv_kv.dtype),
            pltpu.SemaphoreType.DMA((nblocks * slots,)),
        ],
    )
    return pl.pallas_call(
        functools.partial(attend_kernel, count=count, slots=slots),
        grid_spec=grid_spec,
        out_shape=jax.ShapeDtypeStruct((nblocks, width, feat), jnp.bfloat16),
        compiler_params=pltpu.CompilerParams(vmem_limit_bytes=48 * 1024 * 1024),
    )(slot_of, live, scales, query_stack, own_kv, recv_kv)


def gather_kernel(pick_ref, src_ref, out_ref):
    g = pl.program_id(0)
    group = out_ref.shape[0]
    for i in range(group):
        out_ref[i] = src_ref[pick_ref[g * group + i]]


def gather_blocks(blocks, pick):
    nblocks, r, l = blocks.shape
    tiles = pick.shape[0]
    group = 32
    grid_spec = pltpu.PrefetchScalarGridSpec(
        num_scalar_prefetch=1,
        grid=(tiles // group,),
        in_specs=[pl.BlockSpec((nblocks, r, l), lambda g, pick: (0, 0, 0))],
        out_specs=pl.BlockSpec((group, r, l), lambda g, pick: (g, 0, 0)),
    )
    return pl.pallas_call(
        gather_kernel,
        grid_spec=grid_spec,
        out_shape=jax.ShapeDtypeStruct((tiles, r, l), blocks.dtype),
    )(pick, blocks)


def project_kernel(x_ref, w_ref, out_ref, *, hd):
    kv = jnp.dot(x_ref[...], w_ref[...], preferred_element_type=jnp.float32)
    feat = kv.shape[1] // 2
    keys = kv[:, :feat]
    lane = lax.broadcasted_iota(jnp.int32, (1, feat), 1)
    sq = keys * keys
    scale = jnp.zeros(keys.shape, jnp.float32)
    for h in range(feat // hd):
        inside = (lane >= h * hd) & (lane < (h + 1) * hd)
        total = jnp.sum(jnp.where(inside, sq, 0.0), axis=1, keepdims=True)
        scale = jnp.where(inside, lax.rsqrt(total + 1e-06), scale)
    out_ref[0, :, :feat] = (keys * scale).astype(out_ref.dtype)
    out_ref[0, :, feat:] = kv[:, feat:].astype(out_ref.dtype)


def project_all(rows, w_kv, heads, hd):
    n, model = rows.shape
    cols = w_kv.shape[1] // heads
    return pl.pallas_call(
        functools.partial(project_kernel, hd=hd),
        grid=(heads,),
        in_specs=[
            pl.BlockSpec((n, model), lambda y: (0, 0)),
            pl.BlockSpec((model, cols), lambda y: (0, y)),
        ],
        out_specs=pl.BlockSpec((1, n, cols), lambda y: (y, 0, 0)),
        out_shape=jax.ShapeDtypeStruct((heads, n, cols), jnp.bfloat16),
    )(rows, w_kv)


def body(feats, w_query, w_key, w_value, w_out, head_scale, nbr_owner, nbr_local, slot_valid):
    rows = feats.shape[0]
    feat = w_query.shape[1]
    count = head_scale.shape[0]
    nblocks, slots = nbr_owner.shape
    width = rows // nblocks
    devices = lax.axis_size("nodes")
    capacity = max(2, min(nblocks // 2, 3 * nblocks * slots // (2 * devices)))
    tile_count = devices * capacity
    query_n = unit_rows(jnp.dot(feats, w_query, preferred_element_type=jnp.float32), count)
    key_n = unit_rows(jnp.dot(feats, w_key, preferred_element_type=jnp.float32), count)
    value_b = jnp.dot(feats, w_value, preferred_element_type=jnp.float32).astype(jnp.bfloat16)
    query_blocks = query_n.reshape(nblocks, width, feat)
    head_of = jnp.arange(feat, dtype=jnp.int32) // (feat // count)
    query_stack = jnp.concatenate(
        [jnp.where(head_of[None, None, :] == h, query_blocks, 0) for h in range(count)], axis=1
    )
    own_kv = jnp.concatenate([key_n, value_b], axis=1).reshape(nblocks, width, 2 * feat)
    owners = nbr_owner.reshape(-1)
    owner_hot = (owners[:, None] == jnp.arange(devices, dtype=jnp.int32)[None, :]).astype(jnp.int32)
    rank = jnp.sum(jnp.cumsum(owner_hot, axis=0) * owner_hot, axis=1) - 1
    target = owners * capacity + rank
    place = (target[:, None] == jnp.arange(tile_count, dtype=jnp.int32)[None, :]).astype(jnp.int32)
    valid = (slot_valid.reshape(-1) > 0).astype(jnp.int32)
    wanted = jnp.where(valid > 0, nbr_local.reshape(-1), -1)
    request = jnp.sum(place * (wanted[:, None] + 1), axis=0) - 1
    asked = lax.all_to_all(
        request.reshape(devices, capacity), "nodes", split_axis=0, concat_axis=0, tiled=True
    ).reshape(-1)
    heads = lax.axis_size("heads")
    me = lax.axis_index("heads")
    quarter = width // heads
    model = feats.shape[1]
    feats_parts = feats.reshape(nblocks * heads, quarter, model)
    pick = jnp.clip(asked, 0, nblocks - 1).astype(jnp.int32) * heads + me
    payload = gather_blocks(feats_parts, pick)
    w_out, w_key_b, w_value_b, payload = lax.optimization_barrier((w_out, w_key, w_value, payload))
    w_out_t = lax.all_gather(w_out.T, "heads", axis=1, tiled=True)
    w_key_all = lax.all_gather(w_key_b, "heads", axis=1, tiled=True).reshape(model, heads, feat)
    w_value_all = lax.all_gather(w_value_b, "heads", axis=1, tiled=True).reshape(model, heads, feat)
    w_kv_all = jnp.stack([w_key_all, w_value_all], axis=2).reshape(model, heads * 2 * feat)
    recv = lax.all_to_all(
        payload.reshape(devices, capacity * quarter, model),
        "nodes",
        split_axis=0,
        concat_axis=0,
        tiled=True,
    ).reshape(tile_count, quarter, model)
    recv, w_out_t, w_kv_all = lax.optimization_barrier((recv, w_out_t, w_kv_all))
    slot_of = jnp.clip(target, 0, tile_count - 1).astype(jnp.int32)
    piece = gather_blocks(recv, slot_of)
    pairs = piece.shape[0]
    send = project_all(piece.reshape(pairs * quarter, model), w_kv_all, heads, feat // count).reshape(
        heads, pairs, quarter, 2 * feat
    )
    got = lax.all_to_all(send, "heads", 0, 0, tiled=True)
    pair_kv = jnp.transpose(got, (1, 0, 2, 3)).reshape(pairs, width, 2 * feat)
    pair_ids = jnp.arange(pairs, dtype=jnp.int32)
    attn_t = attend(query_stack, own_kv, pair_kv, pair_ids, valid, head_scale)
    attn = attn_t.reshape(rows, feat)
    heads = lax.axis_size("heads")
    me = lax.axis_index("heads")

    def out_part(piece, source):
        w_part = lax.dynamic_slice(w_out_t, (me * feat, source * feat), (feat, feat))
        return lax.dot_general(
            piece, w_part, (((1,), (1,)), ((), ())), preferred_element_type=jnp.float32
        )

    mixed = out_part(attn, me)
    for k in range(1, heads):
        piece = lax.ppermute(attn, "heads", [(j, (j + k) % heads) for j in range(heads)])
        mixed = mixed + out_part(piece, (me - k) % heads)
    return mixed.astype(jnp.bfloat16)


def solution(mesh):
    placed = (
        P("nodes", None),
        P(None, "heads"),
        P(None, "heads"),
        P(None, "heads"),
        P("heads", None),
        P("heads"),
        P("nodes", None),
        P("nodes", None),
        P("nodes", None),
    )
    return jax.shard_map(
        body, mesh=mesh, in_specs=placed, out_specs=P("nodes", "heads"), check_vma=False
    )
```

```python
import functools

import jax
import jax.numpy as jnp
from jax import lax
from jax.experimental import pallas as pl
from jax.experimental.pallas import tpu as pltpu
from jax.sharding import PartitionSpec as P


def unit_rows(values, count):
    shaped = values.reshape(values.shape[0], count, -1)
    total = jnp.sum(shaped * shaped, axis=-1, keepdims=True)
    return (shaped * lax.rsqrt(total + 1e-06)).astype(jnp.bfloat16).reshape(values.shape)


def attend_kernel(slot_ref, live_ref, scale_ref, q_ref, own_ref, recv_ref, out_ref, buf, sems, *, count, slots):
    b = pl.program_id(0)
    pairs = buf.shape[0]
    stacked, feat = q_ref.shape[1], q_ref.shape[2]
    width = stacked // count
    hd = feat // count

    def pair_copy(p):
        return pltpu.make_async_copy(recv_ref.at[slot_ref[p]], buf.at[p], sems.at[p])

    @pl.when(b == 0)
    def _():
        for p in range(pairs):
            pair_copy(p).start()

    for s in range(slots):
        pair_copy(b * slots + s).wait()
    lane_head = lax.broadcasted_iota(jnp.int32, (width, feat), 1) // hd
    stack_rows = lax.broadcasted_iota(jnp.int32, (stacked, 1), 0)
    scale_col = jnp.zeros((stacked, 1), jnp.float32)
    for h in range(count):
        inside = (stack_rows >= h * width) & (stack_rows < (h + 1) * width)
        scale_col = jnp.where(inside, scale_ref[h], scale_col)
    key_lanes = lax.broadcasted_iota(jnp.int32, (1, (slots + 1) * width), 1)
    live_row = jnp.ones((1, (slots + 1) * width), jnp.float32)
    for s in range(slots):
        inside = (key_lanes >= (s + 1) * width) & (key_lanes < (s + 2) * width)
        live_row = jnp.where(inside, live_ref[b * slots + s].astype(jnp.float32), live_row)
    blocks = [own_ref[b]] + [buf[b * slots + s] for s in range(slots)]
    keys = jnp.concatenate([blk[:, :feat] for blk in blocks], axis=0)
    values = jnp.concatenate([blk[:, feat:] for blk in blocks], axis=0)
    s_all = lax.dot_general(
        q_ref[0], keys, (((1,), (1,)), ((), ())), preferred_element_type=jnp.float32
    )
    w = jnp.exp(scale_col * (s_all - 1.0)) * live_row
    den = jnp.sum(w, axis=1, keepdims=True)
    w_b = w.astype(jnp.bfloat16)
    num = jnp.zeros((width, feat), jnp.float32)
    den_full = jnp.zeros((width, feat), jnp.float32)
    for h in range(count):
        part = jnp.dot(w_b[h * width:(h + 1) * width], values, preferred_element_type=jnp.float32)
        num = jnp.where(lane_head == h, part, num)
        den_full = jnp.where(lane_head == h, den[h * width:(h + 1) * width], den_full)
    out_ref[0] = (num / den_full).astype(out_ref.dtype)


def attend(query_stack, own_kv, recv_kv, slot_of, live, scales):
    nblocks, stacked, feat = query_stack.shape
    count = scales.shape[0]
    width = stacked // count
    slots = slot_of.shape[0] // nblocks
    grid_spec = pltpu.PrefetchScalarGridSpec(
        num_scalar_prefetch=2,
        grid=(nblocks,),
        in_specs=[
            pl.BlockSpec(memory_space=pltpu.SMEM),
            pl.BlockSpec((1, stacked, feat), lambda b, slot_of, live: (b, 0, 0)),
            pl.BlockSpec((nblocks, width, 2 * feat), lambda b, slot_of, live: (0, 0, 0)),
            pl.BlockSpec(memory_space=pl.ANY),
        ],
        out_specs=pl.BlockSpec((1, width, feat), lambda b, slot_of, live: (b, 0, 0)),
        scratch_shapes=[
            pltpu.VMEM((nblocks * slots, width, 2 * feat), recv_kv.dtype),
            pltpu.SemaphoreType.DMA((nblocks * slots,)),
        ],
    )
    return pl.pallas_call(
        functools.partial(attend_kernel, count=count, slots=slots),
        grid_spec=grid_spec,
        out_shape=jax.ShapeDtypeStruct((nblocks, width, feat), jnp.bfloat16),
        compiler_params=pltpu.CompilerParams(vmem_limit_bytes=48 * 1024 * 1024),
    )(slot_of, live, scales, query_stack, own_kv, recv_kv)


def gather_kernel(pick_ref, src_ref, out_ref):
    g = pl.program_id(0)
    group = out_ref.shape[0]
    for i in range(group):
        out_ref[i] = src_ref[pick_ref[g * group + i]]


def gather_blocks(blocks, pick):
    nblocks, r, l = blocks.shape
    tiles = pick.shape[0]
    group = 32
    grid_spec = pltpu.PrefetchScalarGridSpec(
        num_scalar_prefetch=1,
        grid=(tiles // group,),
        in_specs=[pl.BlockSpec((nblocks, r, l), lambda g, pick: (0, 0, 0))],
        out_specs=pl.BlockSpec((group, r, l), lambda g, pick: (g, 0, 0)),
    )
    return pl.pallas_call(
        gather_kernel,
        grid_spec=grid_spec,
        out_shape=jax.ShapeDtypeStruct((tiles, r, l), blocks.dtype),
    )(pick, blocks)


def project_kernel(slot_ref, recv_ref, w_ref, out_ref, rows_scr, sems, *, hd):
    y = pl.program_id(0)
    pairs = sems.shape[0]
    quarter = recv_ref.shape[1]

    def piece_copy(p):
        return pltpu.make_async_copy(
            recv_ref.at[slot_ref[p]], rows_scr.at[pl.ds(p * quarter, quarter)], sems.at[p]
        )

    @pl.when(y == 0)
    def _():
        for p in range(pairs):
            piece_copy(p).start()
        for p in range(pairs):
            piece_copy(p).wait()

    kv = jnp.dot(rows_scr[...], w_ref[...], preferred_element_type=jnp.float32)
    feat = kv.shape[1] // 2
    keys = kv[:, :feat]
    lane = lax.broadcasted_iota(jnp.int32, (1, feat), 1)
    sq = keys * keys
    scale = jnp.zeros(keys.shape, jnp.float32)
    for h in range(feat // hd):
        inside = (lane >= h * hd) & (lane < (h + 1) * hd)
        total = jnp.sum(jnp.where(inside, sq, 0.0), axis=1, keepdims=True)
        scale = jnp.where(inside, lax.rsqrt(total + 1e-06), scale)
    out_ref[0, :, :feat] = (keys * scale).astype(out_ref.dtype)
    out_ref[0, :, feat:] = kv[:, feat:].astype(out_ref.dtype)


def project_all(recv, slot_of, w_kv, heads, hd):
    tiles, quarter, model = recv.shape
    pairs = slot_of.shape[0]
    n = pairs * quarter
    cols = w_kv.shape[1] // heads
    grid_spec = pltpu.PrefetchScalarGridSpec(
        num_scalar_prefetch=1,
        grid=(heads,),
        in_specs=[
            pl.BlockSpec(memory_space=pl.ANY),
            pl.BlockSpec((model, cols), lambda y, slot_of: (0, y)),
        ],
        out_specs=pl.BlockSpec((1, n, cols), lambda y, slot_of: (y, 0, 0)),
        scratch_shapes=[
            pltpu.VMEM((n, model), recv.dtype),
            pltpu.SemaphoreType.DMA((pairs,)),
        ],
    )
    return pl.pallas_call(
        functools.partial(project_kernel, hd=hd),
        grid_spec=grid_spec,
        out_shape=jax.ShapeDtypeStruct((heads, n, cols), jnp.bfloat16),
    )(slot_of, recv, w_kv)


def body(feats, w_query, w_key, w_value, w_out, head_scale, nbr_owner, nbr_local, slot_valid):
    rows = feats.shape[0]
    feat = w_query.shape[1]
    count = head_scale.shape[0]
    nblocks, slots = nbr_owner.shape
    width = rows // nblocks
    devices = lax.axis_size("nodes")
    capacity = max(2, min(nblocks // 2, 3 * nblocks * slots // (2 * devices)))
    tile_count = devices * capacity
    query_n = unit_rows(jnp.dot(feats, w_query, preferred_element_type=jnp.float32), count)
    key_n = unit_rows(jnp.dot(feats, w_key, preferred_element_type=jnp.float32), count)
    value_b = jnp.dot(feats, w_value, preferred_element_type=jnp.float32).astype(jnp.bfloat16)
    query_blocks = query_n.reshape(nblocks, width, feat)
    head_of = jnp.arange(feat, dtype=jnp.int32) // (feat // count)
    query_stack = jnp.concatenate(
        [jnp.where(head_of[None, None, :] == h, query_blocks, 0) for h in range(count)], axis=1
    )
    own_kv = jnp.concatenate([key_n, value_b], axis=1).reshape(nblocks, width, 2 * feat)
    owners = nbr_owner.reshape(-1)
    owner_hot = (owners[:, None] == jnp.arange(devices, dtype=jnp.int32)[None, :]).astype(jnp.int32)
    rank = jnp.sum(jnp.cumsum(owner_hot, axis=0) * owner_hot, axis=1) - 1
    target = owners * capacity + rank
    place = (target[:, None] == jnp.arange(tile_count, dtype=jnp.int32)[None, :]).astype(jnp.int32)
    valid = (slot_valid.reshape(-1) > 0).astype(jnp.int32)
    wanted = jnp.where(valid > 0, nbr_local.reshape(-1), -1)
    request = jnp.sum(place * (wanted[:, None] + 1), axis=0) - 1
    asked = lax.all_to_all(
        request.reshape(devices, capacity), "nodes", split_axis=0, concat_axis=0, tiled=True
    ).reshape(-1)
    heads = lax.axis_size("heads")
    me = lax.axis_index("heads")
    quarter = width // heads
    model = feats.shape[1]
    feats_parts = feats.reshape(nblocks * heads, quarter, model)
    pick = jnp.clip(asked, 0, nblocks - 1).astype(jnp.int32) * heads + me
    payload = gather_blocks(feats_parts, pick)
    w_out, w_key_b, w_value_b, payload = lax.optimization_barrier((w_out, w_key, w_value, payload))
    w_out_t = lax.all_gather(w_out.T, "heads", axis=1, tiled=True)
    w_key_all = lax.all_gather(w_key_b, "heads", axis=1, tiled=True).reshape(model, heads, feat)
    w_value_all = lax.all_gather(w_value_b, "heads", axis=1, tiled=True).reshape(model, heads, feat)
    w_kv_all = jnp.stack([w_key_all, w_value_all], axis=2).reshape(model, heads * 2 * feat)
    recv = lax.all_to_all(
        payload.reshape(devices, capacity * quarter, model),
        "nodes",
        split_axis=0,
        concat_axis=0,
        tiled=True,
    ).reshape(tile_count, quarter, model)
    recv, w_out_t, w_kv_all = lax.optimization_barrier((recv, w_out_t, w_kv_all))
    slot_of = jnp.clip(target, 0, tile_count - 1).astype(jnp.int32)
    pairs = slot_of.shape[0]
    send = project_all(recv, slot_of, w_kv_all, heads, feat // count).reshape(
        heads, pairs, quarter, 2 * feat
    )
    got = lax.all_to_all(send, "heads", 0, 0, tiled=True)
    pair_kv = jnp.transpose(got, (1, 0, 2, 3)).reshape(pairs, width, 2 * feat)
    pair_ids = jnp.arange(pairs, dtype=jnp.int32)
    attn_t = attend(query_stack, own_kv, pair_kv, pair_ids, valid, head_scale)
    attn = attn_t.reshape(rows, feat)
    heads = lax.axis_size("heads")
    me = lax.axis_index("heads")

    def out_part(piece, source):
        w_part = lax.dynamic_slice(w_out_t, (me * feat, source * feat), (feat, feat))
        return lax.dot_general(
            piece, w_part, (((1,), (1,)), ((), ())), preferred_element_type=jnp.float32
        )

    mixed = out_part(attn, me)
    for k in range(1, heads):
        piece = lax.ppermute(attn, "heads", [(j, (j + k) % heads) for j in range(heads)])
        mixed = mixed + out_part(piece, (me - k) % heads)
    return mixed.astype(jnp.bfloat16)


def solution(mesh):
    placed = (
        P("nodes", None),
        P(None, "heads"),
        P(None, "heads"),
        P(None, "heads"),
        P("heads", None),
        P("heads"),
        P("nodes", None),
        P("nodes", None),
        P("nodes", None),
    )
    return jax.shard_map(
        body, mesh=mesh, in_specs=placed, out_specs=P("nodes", "heads"), check_vma=False
    )
```

```python
import functools

import jax
import jax.numpy as jnp
from jax import lax
from jax.experimental import pallas as pl
from jax.experimental.pallas import tpu as pltpu
from jax.sharding import PartitionSpec as P


def unit_rows(values, count):
    shaped = values.reshape(values.shape[0], count, -1)
    total = jnp.sum(shaped * shaped, axis=-1, keepdims=True)
    return (shaped * lax.rsqrt(total + 1e-06)).astype(jnp.bfloat16).reshape(values.shape)


def attend_kernel(slot_ref, live_ref, scale_ref, q_ref, own_ref, recv_ref, out_ref, buf, sems, *, count, slots):
    b = pl.program_id(0)
    pairs = buf.shape[0]
    stacked, feat = q_ref.shape[1], q_ref.shape[2]
    width = stacked // count
    hd = feat // count

    def pair_copy(p):
        return pltpu.make_async_copy(recv_ref.at[slot_ref[p]], buf.at[p], sems.at[p])

    @pl.when(b == 0)
    def _():
        for p in range(pairs):
            pair_copy(p).start()

    for s in range(slots):
        pair_copy(b * slots + s).wait()
    lane_head = lax.broadcasted_iota(jnp.int32, (width, feat), 1) // hd
    stack_rows = lax.broadcasted_iota(jnp.int32, (stacked, 1), 0)
    scale_col = jnp.zeros((stacked, 1), jnp.float32)
    for h in range(count):
        inside = (stack_rows >= h * width) & (stack_rows < (h + 1) * width)
        scale_col = jnp.where(inside, scale_ref[h], scale_col)
    key_lanes = lax.broadcasted_iota(jnp.int32, (1, (slots + 1) * width), 1)
    live_row = jnp.ones((1, (slots + 1) * width), jnp.float32)
    for s in range(slots):
        inside = (key_lanes >= (s + 1) * width) & (key_lanes < (s + 2) * width)
        live_row = jnp.where(inside, live_ref[b * slots + s].astype(jnp.float32), live_row)
    blocks = [own_ref[b]] + [buf[b * slots + s] for s in range(slots)]
    keys = jnp.concatenate([blk[:, :feat] for blk in blocks], axis=0)
    values = jnp.concatenate([blk[:, feat:] for blk in blocks], axis=0)
    s_all = lax.dot_general(
        q_ref[0], keys, (((1,), (1,)), ((), ())), preferred_element_type=jnp.float32
    )
    w = jnp.exp(scale_col * (s_all - 1.0)) * live_row
    den = jnp.sum(w, axis=1, keepdims=True)
    w_b = w.astype(jnp.bfloat16)
    num = jnp.zeros((width, feat), jnp.float32)
    den_full = jnp.zeros((width, feat), jnp.float32)
    for h in range(count):
        part = jnp.dot(w_b[h * width:(h + 1) * width], values, preferred_element_type=jnp.float32)
        num = jnp.where(lane_head == h, part, num)
        den_full = jnp.where(lane_head == h, den[h * width:(h + 1) * width], den_full)
    out_ref[0] = (num / den_full).astype(out_ref.dtype)


def attend(query_stack, own_kv, recv_kv, slot_of, live, scales):
    nblocks, stacked, feat = query_stack.shape
    count = scales.shape[0]
    width = stacked // count
    slots = slot_of.shape[0] // nblocks
    grid_spec = pltpu.PrefetchScalarGridSpec(
        num_scalar_prefetch=2,
        grid=(nblocks,),
        in_specs=[
            pl.BlockSpec(memory_space=pltpu.SMEM),
            pl.BlockSpec((1, stacked, feat), lambda b, slot_of, live: (b, 0, 0)),
            pl.BlockSpec((nblocks, width, 2 * feat), lambda b, slot_of, live: (0, 0, 0)),
            pl.BlockSpec(memory_space=pl.ANY),
        ],
        out_specs=pl.BlockSpec((1, width, feat), lambda b, slot_of, live: (b, 0, 0)),
        scratch_shapes=[
            pltpu.VMEM((nblocks * slots, width, 2 * feat), recv_kv.dtype),
            pltpu.SemaphoreType.DMA((nblocks * slots,)),
        ],
    )
    return pl.pallas_call(
        functools.partial(attend_kernel, count=count, slots=slots),
        grid_spec=grid_spec,
        out_shape=jax.ShapeDtypeStruct((nblocks, width, feat), jnp.bfloat16),
        compiler_params=pltpu.CompilerParams(vmem_limit_bytes=48 * 1024 * 1024),
    )(slot_of, live, scales, query_stack, own_kv, recv_kv)


def gather_kernel(pick_ref, src_ref, out_ref):
    g = pl.program_id(0)
    group = out_ref.shape[0]
    for i in range(group):
        out_ref[i] = src_ref[pick_ref[g * group + i]]


def gather_blocks(blocks, pick):
    nblocks, r, l = blocks.shape
    tiles = pick.shape[0]
    group = 32
    grid_spec = pltpu.PrefetchScalarGridSpec(
        num_scalar_prefetch=1,
        grid=(tiles // group,),
        in_specs=[pl.BlockSpec((nblocks, r, l), lambda g, pick: (0, 0, 0))],
        out_specs=pl.BlockSpec((group, r, l), lambda g, pick: (g, 0, 0)),
    )
    return pl.pallas_call(
        gather_kernel,
        grid_spec=grid_spec,
        out_shape=jax.ShapeDtypeStruct((tiles, r, l), blocks.dtype),
    )(pick, blocks)


def project_kernel(slot_ref, recv_ref, w_ref, out_ref, rows_scr, sems, *, hd):
    y = pl.program_id(0)
    pairs = sems.shape[0]
    quarter = recv_ref.shape[1]

    def piece_copy(p):
        return pltpu.make_async_copy(
            recv_ref.at[slot_ref[p]], rows_scr.at[pl.ds(p * quarter, quarter)], sems.at[p]
        )

    @pl.when(y == 0)
    def _():
        for p in range(pairs):
            piece_copy(p).start()
        for p in range(pairs):
            piece_copy(p).wait()

    kv = jnp.dot(rows_scr[...], w_ref[...], preferred_element_type=jnp.float32)
    feat = kv.shape[1] // 2
    keys = kv[:, :feat]
    lane = lax.broadcasted_iota(jnp.int32, (1, feat), 1)
    sq = keys * keys
    scale = jnp.zeros(keys.shape, jnp.float32)
    for h in range(feat // hd):
        inside = (lane >= h * hd) & (lane < (h + 1) * hd)
        total = jnp.sum(jnp.where(inside, sq, 0.0), axis=1, keepdims=True)
        scale = jnp.where(inside, lax.rsqrt(total + 1e-06), scale)
    out_ref[0, :, :feat] = (keys * scale).astype(out_ref.dtype)
    out_ref[0, :, feat:] = kv[:, feat:].astype(out_ref.dtype)


def project_all(recv, slot_of, w_kv, heads, hd):
    tiles, quarter, model = recv.shape
    pairs = slot_of.shape[0]
    n = pairs * quarter
    cols = w_kv.shape[1] // heads
    grid_spec = pltpu.PrefetchScalarGridSpec(
        num_scalar_prefetch=1,
        grid=(heads,),
        in_specs=[
            pl.BlockSpec(memory_space=pl.ANY),
            pl.BlockSpec((model, cols), lambda y, slot_of: (0, y)),
        ],
        out_specs=pl.BlockSpec((1, n, cols), lambda y, slot_of: (y, 0, 0)),
        scratch_shapes=[
            pltpu.VMEM((n, model), recv.dtype),
            pltpu.SemaphoreType.DMA((pairs,)),
        ],
    )
    return pl.pallas_call(
        functools.partial(project_kernel, hd=hd),
        grid_spec=grid_spec,
        out_shape=jax.ShapeDtypeStruct((heads, n, cols), jnp.bfloat16),
    )(slot_of, recv, w_kv)


def body(feats, w_query, w_key, w_value, w_out, head_scale, nbr_owner, nbr_local, slot_valid):
    rows = feats.shape[0]
    feat = w_query.shape[1]
    count = head_scale.shape[0]
    nblocks, slots = nbr_owner.shape
    width = rows // nblocks
    devices = lax.axis_size("nodes")
    capacity = max(2, min(nblocks // 2, 3 * nblocks * slots // (2 * devices)))
    tile_count = devices * capacity
    query_n = unit_rows(jnp.dot(feats, w_query, preferred_element_type=jnp.float32), count)
    key_n = unit_rows(jnp.dot(feats, w_key, preferred_element_type=jnp.float32), count)
    value_b = jnp.dot(feats, w_value, preferred_element_type=jnp.float32).astype(jnp.bfloat16)
    query_blocks = query_n.reshape(nblocks, width, feat)
    head_of = jnp.arange(feat, dtype=jnp.int32) // (feat // count)
    query_stack = jnp.concatenate(
        [jnp.where(head_of[None, None, :] == h, query_blocks, 0) for h in range(count)], axis=1
    )
    own_kv = jnp.concatenate([key_n, value_b], axis=1).reshape(nblocks, width, 2 * feat)
    owners = nbr_owner.reshape(-1)
    owner_hot = (owners[:, None] == jnp.arange(devices, dtype=jnp.int32)[None, :]).astype(jnp.int32)
    rank = jnp.sum(jnp.cumsum(owner_hot, axis=0) * owner_hot, axis=1) - 1
    target = owners * capacity + rank
    place = (target[:, None] == jnp.arange(tile_count, dtype=jnp.int32)[None, :]).astype(jnp.int32)
    valid = (slot_valid.reshape(-1) > 0).astype(jnp.int32)
    wanted = jnp.where(valid > 0, nbr_local.reshape(-1), -1)
    request = jnp.sum(place * (wanted[:, None] + 1), axis=0) - 1
    asked = lax.all_to_all(
        request.reshape(devices, capacity), "nodes", split_axis=0, concat_axis=0, tiled=True
    ).reshape(-1)
    heads = lax.axis_size("heads")
    me = lax.axis_index("heads")
    quarter = width // heads
    model = feats.shape[1]
    feats_parts = feats.reshape(nblocks * heads, quarter, model)
    pick = jnp.clip(asked, 0, nblocks - 1).astype(jnp.int32) * heads + me
    payload = gather_blocks(feats_parts, pick)
    w_out, w_key_b, w_value_b, payload = lax.optimization_barrier((w_out, w_key, w_value, payload))
    w_out_t = lax.all_gather(w_out.T, "heads", axis=1, tiled=True)
    w_key_all = lax.all_gather(w_key_b, "heads", axis=1, tiled=True).reshape(model, heads, feat)
    w_value_all = lax.all_gather(w_value_b, "heads", axis=1, tiled=True).reshape(model, heads, feat)
    w_kv_all = jnp.stack([w_key_all, w_value_all], axis=2).reshape(model, heads * 2 * feat)
    recv = lax.all_to_all(
        payload.reshape(devices, capacity * quarter, model),
        "nodes",
        split_axis=0,
        concat_axis=0,
        tiled=True,
    ).reshape(tile_count, quarter, model)
    recv, w_out_t, w_kv_all = lax.optimization_barrier((recv, w_out_t, w_kv_all))
    slot_of = jnp.clip(target, 0, tile_count - 1).astype(jnp.int32)
    pairs = slot_of.shape[0]
    send = project_all(recv, slot_of, w_kv_all, heads, feat // count).reshape(
        heads, pairs, quarter, 2 * feat
    )
    got = lax.all_to_all(send, "heads", 0, 0, tiled=True)
    pair_kv = jnp.transpose(got, (1, 0, 2, 3)).reshape(pairs, width, 2 * feat)
    pair_ids = jnp.arange(pairs, dtype=jnp.int32)
    heads_n = lax.axis_size("heads")
    me_h = lax.axis_index("heads")

    def out_part(piece, source):
        w_part = lax.dynamic_slice(w_out_t, (me_h * feat, source * feat), (feat, feat))
        return lax.dot_general(
            piece, w_part, (((1,), (1,)), ((), ())), preferred_element_type=jnp.float32
        )

    halves = 2
    per_half = nblocks // halves
    outs = []
    for part in range(halves):
        lo, hi = part * per_half, (part + 1) * per_half
        attn_half = attend(
            query_stack[lo:hi],
            own_kv[lo:hi],
            pair_kv,
            pair_ids[lo * slots:hi * slots],
            valid[lo * slots:hi * slots],
            head_scale,
        ).reshape(per_half * width, feat)
        mixed = out_part(attn_half, me_h)
        for k in range(1, heads_n):
            piece = lax.ppermute(attn_half, "heads", [(j, (j + k) % heads_n) for j in range(heads_n)])
            mixed = mixed + out_part(piece, (me_h - k) % heads_n)
        outs.append(mixed.astype(jnp.bfloat16))
    return jnp.concatenate(outs, axis=0)


def solution(mesh):
    placed = (
        P("nodes", None),
        P(None, "heads"),
        P(None, "heads"),
        P(None, "heads"),
        P("heads", None),
        P("heads"),
        P("nodes", None),
        P("nodes", None),
        P("nodes", None),
    )
    return jax.shard_map(
        body, mesh=mesh, in_specs=placed, out_specs=P("nodes", "heads"), check_vma=False
    )
```

```python
import functools

import jax
import jax.numpy as jnp
from jax import lax
from jax.experimental import pallas as pl
from jax.experimental.pallas import tpu as pltpu
from jax.sharding import PartitionSpec as P


def unit_rows(values, count):
    shaped = values.reshape(values.shape[0], count, -1)
    total = jnp.sum(shaped * shaped, axis=-1, keepdims=True)
    return (shaped * lax.rsqrt(total + 1e-06)).astype(jnp.bfloat16).reshape(values.shape)


def attend_kernel(slot_ref, live_ref, scale_ref, q_ref, own_ref, recv_ref, out_ref, buf, sems, *, count, slots):
    b = pl.program_id(0)
    pairs = buf.shape[0]
    stacked, feat = q_ref.shape[1], q_ref.shape[2]
    width = stacked // count
    hd = feat // count

    def pair_copy(p):
        return pltpu.make_async_copy(recv_ref.at[slot_ref[p]], buf.at[p], sems.at[p])

    @pl.when(b == 0)
    def _():
        for p in range(pairs):
            pair_copy(p).start()

    for s in range(slots):
        pair_copy(b * slots + s).wait()
    lane_head = lax.broadcasted_iota(jnp.int32, (width, feat), 1) // hd
    stack_rows = lax.broadcasted_iota(jnp.int32, (stacked, 1), 0)
    scale_col = jnp.zeros((stacked, 1), jnp.float32)
    for h in range(count):
        inside = (stack_rows >= h * width) & (stack_rows < (h + 1) * width)
        scale_col = jnp.where(inside, scale_ref[h], scale_col)
    key_lanes = lax.broadcasted_iota(jnp.int32, (1, (slots + 1) * width), 1)
    live_row = jnp.ones((1, (slots + 1) * width), jnp.float32)
    for s in range(slots):
        inside = (key_lanes >= (s + 1) * width) & (key_lanes < (s + 2) * width)
        live_row = jnp.where(inside, live_ref[b * slots + s].astype(jnp.float32), live_row)
    blocks = [own_ref[b]] + [buf[b * slots + s] for s in range(slots)]
    keys = jnp.concatenate([blk[:, :feat] for blk in blocks], axis=0)
    values = jnp.concatenate([blk[:, feat:] for blk in blocks], axis=0)
    s_all = lax.dot_general(
        q_ref[0], keys, (((1,), (1,)), ((), ())), preferred_element_type=jnp.float32
    )
    w = jnp.exp(scale_col * (s_all - 1.0)) * live_row
    den = jnp.sum(w, axis=1, keepdims=True)
    w_b = w.astype(jnp.bfloat16)
    num = jnp.zeros((width, feat), jnp.float32)
    den_full = jnp.zeros((width, feat), jnp.float32)
    for h in range(count):
        part = jnp.dot(w_b[h * width:(h + 1) * width], values, preferred_element_type=jnp.float32)
        num = jnp.where(lane_head == h, part, num)
        den_full = jnp.where(lane_head == h, den[h * width:(h + 1) * width], den_full)
    out_ref[0] = (num / den_full).astype(out_ref.dtype)


def attend(query_stack, own_kv, recv_kv, slot_of, live, scales):
    nblocks, stacked, feat = query_stack.shape
    count = scales.shape[0]
    width = stacked // count
    slots = slot_of.shape[0] // nblocks
    grid_spec = pltpu.PrefetchScalarGridSpec(
        num_scalar_prefetch=2,
        grid=(nblocks,),
        in_specs=[
            pl.BlockSpec(memory_space=pltpu.SMEM),
            pl.BlockSpec((1, stacked, feat), lambda b, slot_of, live: (b, 0, 0)),
            pl.BlockSpec((nblocks, width, 2 * feat), lambda b, slot_of, live: (0, 0, 0)),
            pl.BlockSpec(memory_space=pl.ANY),
        ],
        out_specs=pl.BlockSpec((1, width, feat), lambda b, slot_of, live: (b, 0, 0)),
        scratch_shapes=[
            pltpu.VMEM((nblocks * slots, width, 2 * feat), recv_kv.dtype),
            pltpu.SemaphoreType.DMA((nblocks * slots,)),
        ],
    )
    return pl.pallas_call(
        functools.partial(attend_kernel, count=count, slots=slots),
        grid_spec=grid_spec,
        out_shape=jax.ShapeDtypeStruct((nblocks, width, feat), jnp.bfloat16),
        compiler_params=pltpu.CompilerParams(vmem_limit_bytes=48 * 1024 * 1024),
    )(slot_of, live, scales, query_stack, own_kv, recv_kv)


def gather_kernel(pick_ref, src_ref, out_ref):
    g = pl.program_id(0)
    group = out_ref.shape[0]
    for i in range(group):
        out_ref[i] = src_ref[pick_ref[g * group + i]]


def gather_blocks(blocks, pick):
    nblocks, r, l = blocks.shape
    tiles = pick.shape[0]
    group = 64
    grid_spec = pltpu.PrefetchScalarGridSpec(
        num_scalar_prefetch=1,
        grid=(tiles // group,),
        in_specs=[pl.BlockSpec((nblocks, r, l), lambda g, pick: (0, 0, 0))],
        out_specs=pl.BlockSpec((group, r, l), lambda g, pick: (g, 0, 0)),
    )
    return pl.pallas_call(
        gather_kernel,
        grid_spec=grid_spec,
        out_shape=jax.ShapeDtypeStruct((tiles, r, l), blocks.dtype),
    )(pick, blocks)


def project_kernel(slot_ref, recv_ref, w_ref, out_ref, rows_scr, sems, *, hd):
    y = pl.program_id(0)
    pairs = sems.shape[0]
    quarter = recv_ref.shape[1]

    def piece_copy(p):
        return pltpu.make_async_copy(
            recv_ref.at[slot_ref[p]], rows_scr.at[pl.ds(p * quarter, quarter)], sems.at[p]
        )

    @pl.when(y == 0)
    def _():
        for p in range(pairs):
            piece_copy(p).start()
        for p in range(pairs):
            piece_copy(p).wait()

    kv = jnp.dot(rows_scr[...], w_ref[...], preferred_element_type=jnp.float32)
    feat = kv.shape[1] // 2
    keys = kv[:, :feat]
    lane = lax.broadcasted_iota(jnp.int32, (1, feat), 1)
    sq = keys * keys
    scale = jnp.zeros(keys.shape, jnp.float32)
    for h in range(feat // hd):
        inside = (lane >= h * hd) & (lane < (h + 1) * hd)
        total = jnp.sum(jnp.where(inside, sq, 0.0), axis=1, keepdims=True)
        scale = jnp.where(inside, lax.rsqrt(total + 1e-06), scale)
    out_ref[0, :, :feat] = (keys * scale).astype(out_ref.dtype)
    out_ref[0, :, feat:] = kv[:, feat:].astype(out_ref.dtype)


def project_all(recv, slot_of, w_kv, heads, hd):
    tiles, quarter, model = recv.shape
    pairs = slot_of.shape[0]
    n = pairs * quarter
    cols = w_kv.shape[1] // heads
    grid_spec = pltpu.PrefetchScalarGridSpec(
        num_scalar_prefetch=1,
        grid=(heads,),
        in_specs=[
            pl.BlockSpec(memory_space=pl.ANY),
            pl.BlockSpec((model, cols), lambda y, slot_of: (0, y)),
        ],
        out_specs=pl.BlockSpec((1, n, cols), lambda y, slot_of: (y, 0, 0)),
        scratch_shapes=[
            pltpu.VMEM((n, model), recv.dtype),
            pltpu.SemaphoreType.DMA((pairs,)),
        ],
    )
    return pl.pallas_call(
        functools.partial(project_kernel, hd=hd),
        grid_spec=grid_spec,
        out_shape=jax.ShapeDtypeStruct((heads, n, cols), jnp.bfloat16),
    )(slot_of, recv, w_kv)


def body(feats, w_query, w_key, w_value, w_out, head_scale, nbr_owner, nbr_local, slot_valid):
    rows = feats.shape[0]
    feat = w_query.shape[1]
    count = head_scale.shape[0]
    nblocks, slots = nbr_owner.shape
    width = rows // nblocks
    devices = lax.axis_size("nodes")
    capacity = max(2, min(nblocks // 2, 3 * nblocks * slots // (2 * devices)))
    tile_count = devices * capacity
    query_n = unit_rows(jnp.dot(feats, w_query, preferred_element_type=jnp.float32), count)
    key_n = unit_rows(jnp.dot(feats, w_key, preferred_element_type=jnp.float32), count)
    value_b = jnp.dot(feats, w_value, preferred_element_type=jnp.float32).astype(jnp.bfloat16)
    query_blocks = query_n.reshape(nblocks, width, feat)
    head_of = jnp.arange(feat, dtype=jnp.int32) // (feat // count)
    query_stack = jnp.concatenate(
        [jnp.where(head_of[None, None, :] == h, query_blocks, 0) for h in range(count)], axis=1
    )
    own_kv = jnp.concatenate([key_n, value_b], axis=1).reshape(nblocks, width, 2 * feat)
    owners = nbr_owner.reshape(-1)
    owner_hot = (owners[:, None] == jnp.arange(devices, dtype=jnp.int32)[None, :]).astype(jnp.int32)
    rank = jnp.sum(jnp.cumsum(owner_hot, axis=0) * owner_hot, axis=1) - 1
    target = owners * capacity + rank
    place = (target[:, None] == jnp.arange(tile_count, dtype=jnp.int32)[None, :]).astype(jnp.int32)
    valid = (slot_valid.reshape(-1) > 0).astype(jnp.int32)
    wanted = jnp.where(valid > 0, nbr_local.reshape(-1), -1)
    request = jnp.sum(place * (wanted[:, None] + 1), axis=0) - 1
    asked = lax.all_to_all(
        request.reshape(devices, capacity), "nodes", split_axis=0, concat_axis=0, tiled=True
    ).reshape(-1)
    heads = lax.axis_size("heads")
    me = lax.axis_index("heads")
    quarter = width // heads
    model = feats.shape[1]
    feats_parts = feats.reshape(nblocks * heads, quarter, model)
    pick = jnp.clip(asked, 0, nblocks - 1).astype(jnp.int32) * heads + me
    payload = gather_blocks(feats_parts, pick)
    w_out, w_key_b, w_value_b, payload = lax.optimization_barrier((w_out, w_key, w_value, payload))
    w_out_t = lax.all_gather(w_out.T, "heads", axis=1, tiled=True)
    w_key_all = lax.all_gather(w_key_b, "heads", axis=1, tiled=True).reshape(model, heads, feat)
    w_value_all = lax.all_gather(w_value_b, "heads", axis=1, tiled=True).reshape(model, heads, feat)
    w_kv_all = jnp.stack([w_key_all, w_value_all], axis=2).reshape(model, heads * 2 * feat)
    recv = lax.all_to_all(
        payload.reshape(devices, capacity * quarter, model),
        "nodes",
        split_axis=0,
        concat_axis=0,
        tiled=True,
    ).reshape(tile_count, quarter, model)
    recv, w_out_t, w_kv_all = lax.optimization_barrier((recv, w_out_t, w_kv_all))
    slot_of = jnp.clip(target, 0, tile_count - 1).astype(jnp.int32)
    pairs = slot_of.shape[0]
    send = project_all(recv, slot_of, w_kv_all, heads, feat // count).reshape(
        heads, pairs, quarter, 2 * feat
    )
    got = lax.all_to_all(send, "heads", 0, 0, tiled=True)
    pair_kv = jnp.transpose(got, (1, 0, 2, 3)).reshape(pairs, width, 2 * feat)
    pair_ids = jnp.arange(pairs, dtype=jnp.int32)
    heads_n = lax.axis_size("heads")
    me_h = lax.axis_index("heads")

    def out_part(piece, source):
        w_part = lax.dynamic_slice(w_out_t, (me_h * feat, source * feat), (feat, feat))
        return lax.dot_general(
            piece, w_part, (((1,), (1,)), ((), ())), preferred_element_type=jnp.float32
        )

    halves = 2
    per_half = nblocks // halves
    outs = []
    for part in range(halves):
        lo, hi = part * per_half, (part + 1) * per_half
        attn_half = attend(
            query_stack[lo:hi],
            own_kv[lo:hi],
            pair_kv,
            pair_ids[lo * slots:hi * slots],
            valid[lo * slots:hi * slots],
            head_scale,
        ).reshape(per_half * width, feat)
        mixed = out_part(attn_half, me_h)
        for k in range(1, heads_n):
            piece = lax.ppermute(attn_half, "heads", [(j, (j + k) % heads_n) for j in range(heads_n)])
            mixed = mixed + out_part(piece, (me_h - k) % heads_n)
        outs.append(mixed.astype(jnp.bfloat16))
    return jnp.concatenate(outs, axis=0)


def solution(mesh):
    placed = (
        P("nodes", None),
        P(None, "heads"),
        P(None, "heads"),
        P(None, "heads"),
        P("heads", None),
        P("heads"),
        P("nodes", None),
        P("nodes", None),
        P("nodes", None),
    )
    return jax.shard_map(
        body, mesh=mesh, in_specs=placed, out_specs=P("nodes", "heads"), check_vma=False
    )
```

```python
import functools

import jax
import jax.numpy as jnp
from jax import lax
from jax.experimental import pallas as pl
from jax.experimental.pallas import tpu as pltpu
from jax.sharding import PartitionSpec as P


def unit_rows(values, count):
    shaped = values.reshape(values.shape[0], count, -1)
    total = jnp.sum(shaped * shaped, axis=-1, keepdims=True)
    return (shaped * lax.rsqrt(total + 1e-06)).astype(jnp.bfloat16).reshape(values.shape)


def attend_kernel(slot_ref, live_ref, scale_ref, q_ref, own_ref, recv_ref, out_ref, buf, sems, *, count, slots):
    b = pl.program_id(0)
    pairs = buf.shape[0]
    stacked, feat = q_ref.shape[1], q_ref.shape[2]
    width = stacked // count
    hd = feat // count

    def pair_copy(p):
        return pltpu.make_async_copy(recv_ref.at[slot_ref[p]], buf.at[p], sems.at[p])

    @pl.when(b == 0)
    def _():
        for p in range(pairs):
            pair_copy(p).start()

    for s in range(slots):
        pair_copy(b * slots + s).wait()
    lane_head = lax.broadcasted_iota(jnp.int32, (width, feat), 1) // hd
    stack_rows = lax.broadcasted_iota(jnp.int32, (stacked, 1), 0)
    scale_col = jnp.zeros((stacked, 1), jnp.float32)
    for h in range(count):
        inside = (stack_rows >= h * width) & (stack_rows < (h + 1) * width)
        scale_col = jnp.where(inside, scale_ref[h], scale_col)
    key_lanes = lax.broadcasted_iota(jnp.int32, (1, (slots + 1) * width), 1)
    live_row = jnp.ones((1, (slots + 1) * width), jnp.float32)
    for s in range(slots):
        inside = (key_lanes >= (s + 1) * width) & (key_lanes < (s + 2) * width)
        live_row = jnp.where(inside, live_ref[b * slots + s].astype(jnp.float32), live_row)
    blocks = [own_ref[b]] + [buf[b * slots + s] for s in range(slots)]
    keys = jnp.concatenate([blk[:, :feat] for blk in blocks], axis=0)
    values = jnp.concatenate([blk[:, feat:] for blk in blocks], axis=0)
    s_all = lax.dot_general(
        q_ref[0], keys, (((1,), (1,)), ((), ())), preferred_element_type=jnp.float32
    )
    w = jnp.exp(scale_col * (s_all - 1.0)) * live_row
    den = jnp.sum(w, axis=1, keepdims=True)
    w_b = w.astype(jnp.bfloat16)
    num = jnp.zeros((width, feat), jnp.float32)
    den_full = jnp.zeros((width, feat), jnp.float32)
    for h in range(count):
        part = jnp.dot(w_b[h * width:(h + 1) * width], values, preferred_element_type=jnp.float32)
        num = jnp.where(lane_head == h, part, num)
        den_full = jnp.where(lane_head == h, den[h * width:(h + 1) * width], den_full)
    out_ref[0] = (num / den_full).astype(out_ref.dtype)


def attend(query_stack, own_kv, recv_kv, slot_of, live, scales):
    nblocks, stacked, feat = query_stack.shape
    count = scales.shape[0]
    width = stacked // count
    slots = slot_of.shape[0] // nblocks
    grid_spec = pltpu.PrefetchScalarGridSpec(
        num_scalar_prefetch=2,
        grid=(nblocks,),
        in_specs=[
            pl.BlockSpec(memory_space=pltpu.SMEM),
            pl.BlockSpec((1, stacked, feat), lambda b, slot_of, live: (b, 0, 0)),
            pl.BlockSpec((nblocks, width, 2 * feat), lambda b, slot_of, live: (0, 0, 0)),
            pl.BlockSpec(memory_space=pl.ANY),
        ],
        out_specs=pl.BlockSpec((1, width, feat), lambda b, slot_of, live: (b, 0, 0)),
        scratch_shapes=[
            pltpu.VMEM((nblocks * slots, width, 2 * feat), recv_kv.dtype),
            pltpu.SemaphoreType.DMA((nblocks * slots,)),
        ],
    )
    return pl.pallas_call(
        functools.partial(attend_kernel, count=count, slots=slots),
        grid_spec=grid_spec,
        out_shape=jax.ShapeDtypeStruct((nblocks, width, feat), jnp.bfloat16),
        compiler_params=pltpu.CompilerParams(vmem_limit_bytes=48 * 1024 * 1024),
    )(slot_of, live, scales, query_stack, own_kv, recv_kv)


def gather_kernel(pick_ref, src_ref, out_ref):
    g = pl.program_id(0)
    group = out_ref.shape[0]
    for i in range(group):
        out_ref[i] = src_ref[pick_ref[g * group + i]]


def gather_blocks(blocks, pick):
    nblocks, r, l = blocks.shape
    tiles = pick.shape[0]
    group = 64
    grid_spec = pltpu.PrefetchScalarGridSpec(
        num_scalar_prefetch=1,
        grid=(tiles // group,),
        in_specs=[pl.BlockSpec((nblocks, r, l), lambda g, pick: (0, 0, 0))],
        out_specs=pl.BlockSpec((group, r, l), lambda g, pick: (g, 0, 0)),
    )
    return pl.pallas_call(
        gather_kernel,
        grid_spec=grid_spec,
        out_shape=jax.ShapeDtypeStruct((tiles, r, l), blocks.dtype),
    )(pick, blocks)


def project_kernel(slot_ref, recv_ref, w_ref, out_ref, rows_scr, sems, *, hd):
    y = pl.program_id(0)
    pairs = sems.shape[0]
    quarter = recv_ref.shape[1]

    def piece_copy(p):
        return pltpu.make_async_copy(
            recv_ref.at[slot_ref[p]], rows_scr.at[pl.ds(p * quarter, quarter)], sems.at[p]
        )

    @pl.when(y == 0)
    def _():
        for p in range(pairs):
            piece_copy(p).start()
        for p in range(pairs):
            piece_copy(p).wait()

    kv = jnp.dot(rows_scr[...], w_ref[...], preferred_element_type=jnp.float32)
    feat = kv.shape[1] // 2
    keys = kv[:, :feat]
    lane = lax.broadcasted_iota(jnp.int32, (1, feat), 1)
    sq = keys * keys
    scale = jnp.zeros(keys.shape, jnp.float32)
    for h in range(feat // hd):
        inside = (lane >= h * hd) & (lane < (h + 1) * hd)
        total = jnp.sum(jnp.where(inside, sq, 0.0), axis=1, keepdims=True)
        scale = jnp.where(inside, lax.rsqrt(total + 1e-06), scale)
    out_ref[0, :, :feat] = (keys * scale).astype(out_ref.dtype)
    out_ref[0, :, feat:] = kv[:, feat:].astype(out_ref.dtype)


def project_all(recv, slot_of, w_kv, heads, hd):
    tiles, quarter, model = recv.shape
    pairs = slot_of.shape[0]
    n = pairs * quarter
    cols = w_kv.shape[1] // heads
    grid_spec = pltpu.PrefetchScalarGridSpec(
        num_scalar_prefetch=1,
        grid=(heads,),
        in_specs=[
            pl.BlockSpec(memory_space=pl.ANY),
            pl.BlockSpec((model, cols), lambda y, slot_of: (0, y)),
        ],
        out_specs=pl.BlockSpec((1, n, cols), lambda y, slot_of: (y, 0, 0)),
        scratch_shapes=[
            pltpu.VMEM((n, model), recv.dtype),
            pltpu.SemaphoreType.DMA((pairs,)),
        ],
    )
    return pl.pallas_call(
        functools.partial(project_kernel, hd=hd),
        grid_spec=grid_spec,
        out_shape=jax.ShapeDtypeStruct((heads, n, cols), jnp.bfloat16),
    )(slot_of, recv, w_kv)


def body(feats, w_query, w_key, w_value, w_out, head_scale, nbr_owner, nbr_local, slot_valid):
    rows = feats.shape[0]
    feat = w_query.shape[1]
    count = head_scale.shape[0]
    nblocks, slots = nbr_owner.shape
    width = rows // nblocks
    devices = lax.axis_size("nodes")
    capacity = max(2, min(nblocks // 2, 3 * nblocks * slots // (2 * devices)))
    tile_count = devices * capacity
    query_n = unit_rows(jnp.dot(feats, w_query, preferred_element_type=jnp.float32), count)
    key_n = unit_rows(jnp.dot(feats, w_key, preferred_element_type=jnp.float32), count)
    value_b = jnp.dot(feats, w_value, preferred_element_type=jnp.float32).astype(jnp.bfloat16)
    query_blocks = query_n.reshape(nblocks, width, feat)
    head_of = jnp.arange(feat, dtype=jnp.int32) // (feat // count)
    query_stack = jnp.concatenate(
        [jnp.where(head_of[None, None, :] == h, query_blocks, 0) for h in range(count)], axis=1
    )
    own_kv = jnp.concatenate([key_n, value_b], axis=1).reshape(nblocks, width, 2 * feat)
    owners = nbr_owner.reshape(-1)
    owner_hot = (owners[:, None] == jnp.arange(devices, dtype=jnp.int32)[None, :]).astype(jnp.int32)
    rank = jnp.sum(jnp.cumsum(owner_hot, axis=0) * owner_hot, axis=1) - 1
    target = owners * capacity + rank
    place = (target[:, None] == jnp.arange(tile_count, dtype=jnp.int32)[None, :]).astype(jnp.int32)
    valid = (slot_valid.reshape(-1) > 0).astype(jnp.int32)
    wanted = jnp.where(valid > 0, nbr_local.reshape(-1), -1)
    request = jnp.sum(place * (wanted[:, None] + 1), axis=0) - 1
    asked = lax.all_to_all(
        request.reshape(devices, capacity), "nodes", split_axis=0, concat_axis=0, tiled=True
    ).reshape(-1)
    heads = lax.axis_size("heads")
    me = lax.axis_index("heads")
    quarter = width // heads
    model = feats.shape[1]
    feats_parts = feats.reshape(nblocks * heads, quarter, model)
    pick = jnp.clip(asked, 0, nblocks - 1).astype(jnp.int32) * heads + me
    payload = gather_blocks(feats_parts, pick)
    w_out, w_key_b, w_value_b, payload = lax.optimization_barrier((w_out, w_key, w_value, payload))
    w_out_t = lax.all_gather(w_out.T, "heads", axis=1, tiled=True)
    w_key_all = lax.all_gather(w_key_b, "heads", axis=1, tiled=True).reshape(model, heads, feat)
    w_value_all = lax.all_gather(w_value_b, "heads", axis=1, tiled=True).reshape(model, heads, feat)
    w_kv_all = jnp.stack([w_key_all, w_value_all], axis=2).reshape(model, heads * 2 * feat)
    recv = lax.all_to_all(
        payload.reshape(devices, capacity * quarter, model),
        "nodes",
        split_axis=0,
        concat_axis=0,
        tiled=True,
    ).reshape(tile_count, quarter, model)
    recv, w_out_t, w_kv_all = lax.optimization_barrier((recv, w_out_t, w_kv_all))
    slot_of = jnp.clip(target, 0, tile_count - 1).astype(jnp.int32)
    pairs = slot_of.shape[0]
    send = project_all(recv, slot_of, w_kv_all, heads, feat // count).reshape(
        heads, pairs, quarter, 2 * feat
    )
    got = lax.all_to_all(send, "heads", 0, 0, tiled=True)
    pair_kv = jnp.transpose(got, (1, 0, 2, 3)).reshape(pairs, width, 2 * feat)
    pair_ids = jnp.arange(pairs, dtype=jnp.int32)
    heads_n = lax.axis_size("heads")
    me_h = lax.axis_index("heads")

    def out_part(piece, source):
        w_part = lax.dynamic_slice(w_out_t, (me_h * feat, source * feat), (feat, feat))
        return lax.dot_general(
            piece, w_part, (((1,), (1,)), ((), ())), preferred_element_type=jnp.float32
        )

    halves = 4
    per_half = nblocks // halves
    outs = []
    for part in range(halves):
        lo, hi = part * per_half, (part + 1) * per_half
        attn_half = attend(
            query_stack[lo:hi],
            own_kv[lo:hi],
            pair_kv,
            pair_ids[lo * slots:hi * slots],
            valid[lo * slots:hi * slots],
            head_scale,
        ).reshape(per_half * width, feat)
        mixed = out_part(attn_half, me_h)
        for k in range(1, heads_n):
            piece = lax.ppermute(attn_half, "heads", [(j, (j + k) % heads_n) for j in range(heads_n)])
            mixed = mixed + out_part(piece, (me_h - k) % heads_n)
        outs.append(mixed.astype(jnp.bfloat16))
    return jnp.concatenate(outs, axis=0)


def solution(mesh):
    placed = (
        P("nodes", None),
        P(None, "heads"),
        P(None, "heads"),
        P(None, "heads"),
        P("heads", None),
        P("heads"),
        P("nodes", None),
        P("nodes", None),
        P("nodes", None),
    )
    return jax.shard_map(
        body, mesh=mesh, in_specs=placed, out_specs=P("nodes", "heads"), check_vma=False
    )
```

```python
import functools

import jax
import jax.numpy as jnp
from jax import lax
from jax.experimental import pallas as pl
from jax.experimental.pallas import tpu as pltpu
from jax.sharding import PartitionSpec as P


def unit_rows(values, count):
    shaped = values.reshape(values.shape[0], count, -1)
    total = jnp.sum(shaped * shaped, axis=-1, keepdims=True)
    return (shaped * lax.rsqrt(total + 1e-06)).astype(jnp.bfloat16).reshape(values.shape)


def attend_kernel(slot_ref, live_ref, scale_ref, q_ref, own_ref, recv_ref, out_ref, buf, sems, *, count, slots):
    b = pl.program_id(0)
    pairs = buf.shape[0]
    stacked, feat = q_ref.shape[1], q_ref.shape[2]
    width = stacked // count
    hd = feat // count

    def pair_copy(p):
        return pltpu.make_async_copy(recv_ref.at[:, slot_ref[p]], buf.at[p], sems.at[p])

    @pl.when(b == 0)
    def _():
        for p in range(pairs):
            pair_copy(p).start()

    for s in range(slots):
        pair_copy(b * slots + s).wait()
    lane_head = lax.broadcasted_iota(jnp.int32, (width, feat), 1) // hd
    stack_rows = lax.broadcasted_iota(jnp.int32, (stacked, 1), 0)
    scale_col = jnp.zeros((stacked, 1), jnp.float32)
    for h in range(count):
        inside = (stack_rows >= h * width) & (stack_rows < (h + 1) * width)
        scale_col = jnp.where(inside, scale_ref[h], scale_col)
    key_lanes = lax.broadcasted_iota(jnp.int32, (1, (slots + 1) * width), 1)
    live_row = jnp.ones((1, (slots + 1) * width), jnp.float32)
    for s in range(slots):
        inside = (key_lanes >= (s + 1) * width) & (key_lanes < (s + 2) * width)
        live_row = jnp.where(inside, live_ref[b * slots + s].astype(jnp.float32), live_row)
    blocks = [own_ref[b]] + [buf[b * slots + s].reshape(width, 2 * feat) for s in range(slots)]
    keys = jnp.concatenate([blk[:, :feat] for blk in blocks], axis=0)
    values = jnp.concatenate([blk[:, feat:] for blk in blocks], axis=0)
    s_all = lax.dot_general(
        q_ref[0], keys, (((1,), (1,)), ((), ())), preferred_element_type=jnp.float32
    )
    w = jnp.exp(scale_col * (s_all - 1.0)) * live_row
    den = jnp.sum(w, axis=1, keepdims=True)
    w_b = w.astype(jnp.bfloat16)
    num = jnp.zeros((width, feat), jnp.float32)
    den_full = jnp.zeros((width, feat), jnp.float32)
    for h in range(count):
        part = jnp.dot(w_b[h * width:(h + 1) * width], values, preferred_element_type=jnp.float32)
        num = jnp.where(lane_head == h, part, num)
        den_full = jnp.where(lane_head == h, den[h * width:(h + 1) * width], den_full)
    out_ref[0] = (num / den_full).astype(out_ref.dtype)


def attend(query_stack, own_kv, recv_kv, slot_of, live, scales):
    nblocks, stacked, feat = query_stack.shape
    count = scales.shape[0]
    width = stacked // count
    slots = slot_of.shape[0] // nblocks
    grid_spec = pltpu.PrefetchScalarGridSpec(
        num_scalar_prefetch=2,
        grid=(nblocks,),
        in_specs=[
            pl.BlockSpec(memory_space=pltpu.SMEM),
            pl.BlockSpec((1, stacked, feat), lambda b, slot_of, live: (b, 0, 0)),
            pl.BlockSpec((nblocks, width, 2 * feat), lambda b, slot_of, live: (0, 0, 0)),
            pl.BlockSpec(memory_space=pl.ANY),
        ],
        out_specs=pl.BlockSpec((1, width, feat), lambda b, slot_of, live: (b, 0, 0)),
        scratch_shapes=[
            pltpu.VMEM((nblocks * slots,) + recv_kv.shape[:1] + recv_kv.shape[2:], recv_kv.dtype),
            pltpu.SemaphoreType.DMA((nblocks * slots,)),
        ],
    )
    return pl.pallas_call(
        functools.partial(attend_kernel, count=count, slots=slots),
        grid_spec=grid_spec,
        out_shape=jax.ShapeDtypeStruct((nblocks, width, feat), jnp.bfloat16),
        compiler_params=pltpu.CompilerParams(vmem_limit_bytes=48 * 1024 * 1024),
    )(slot_of, live, scales, query_stack, own_kv, recv_kv)


def gather_kernel(pick_ref, src_ref, out_ref):
    g = pl.program_id(0)
    group = out_ref.shape[0]
    for i in range(group):
        out_ref[i] = src_ref[pick_ref[g * group + i]]


def gather_blocks(blocks, pick):
    nblocks, r, l = blocks.shape
    tiles = pick.shape[0]
    group = 64
    grid_spec = pltpu.PrefetchScalarGridSpec(
        num_scalar_prefetch=1,
        grid=(tiles // group,),
        in_specs=[pl.BlockSpec((nblocks, r, l), lambda g, pick: (0, 0, 0))],
        out_specs=pl.BlockSpec((group, r, l), lambda g, pick: (g, 0, 0)),
    )
    return pl.pallas_call(
        gather_kernel,
        grid_spec=grid_spec,
        out_shape=jax.ShapeDtypeStruct((tiles, r, l), blocks.dtype),
    )(pick, blocks)


def project_kernel(slot_ref, recv_ref, w_ref, out_ref, rows_scr, sems, *, hd):
    y = pl.program_id(0)
    pairs = sems.shape[0]
    quarter = recv_ref.shape[1]

    def piece_copy(p):
        return pltpu.make_async_copy(
            recv_ref.at[slot_ref[p]], rows_scr.at[pl.ds(p * quarter, quarter)], sems.at[p]
        )

    @pl.when(y == 0)
    def _():
        for p in range(pairs):
            piece_copy(p).start()
        for p in range(pairs):
            piece_copy(p).wait()

    kv = jnp.dot(rows_scr[...], w_ref[...], preferred_element_type=jnp.float32)
    feat = kv.shape[1] // 2
    keys = kv[:, :feat]
    lane = lax.broadcasted_iota(jnp.int32, (1, feat), 1)
    sq = keys * keys
    scale = jnp.zeros(keys.shape, jnp.float32)
    for h in range(feat // hd):
        inside = (lane >= h * hd) & (lane < (h + 1) * hd)
        total = jnp.sum(jnp.where(inside, sq, 0.0), axis=1, keepdims=True)
        scale = jnp.where(inside, lax.rsqrt(total + 1e-06), scale)
    out_ref[0, :, :feat] = (keys * scale).astype(out_ref.dtype)
    out_ref[0, :, feat:] = kv[:, feat:].astype(out_ref.dtype)


def project_all(recv, slot_of, w_kv, heads, hd):
    tiles, quarter, model = recv.shape
    pairs = slot_of.shape[0]
    n = pairs * quarter
    cols = w_kv.shape[1] // heads
    grid_spec = pltpu.PrefetchScalarGridSpec(
        num_scalar_prefetch=1,
        grid=(heads,),
        in_specs=[
            pl.BlockSpec(memory_space=pl.ANY),
            pl.BlockSpec((model, cols), lambda y, slot_of: (0, y)),
        ],
        out_specs=pl.BlockSpec((1, n, cols), lambda y, slot_of: (y, 0, 0)),
        scratch_shapes=[
            pltpu.VMEM((n, model), recv.dtype),
            pltpu.SemaphoreType.DMA((pairs,)),
        ],
    )
    return pl.pallas_call(
        functools.partial(project_kernel, hd=hd),
        grid_spec=grid_spec,
        out_shape=jax.ShapeDtypeStruct((heads, n, cols), jnp.bfloat16),
    )(slot_of, recv, w_kv)


def body(feats, w_query, w_key, w_value, w_out, head_scale, nbr_owner, nbr_local, slot_valid):
    rows = feats.shape[0]
    feat = w_query.shape[1]
    count = head_scale.shape[0]
    nblocks, slots = nbr_owner.shape
    width = rows // nblocks
    devices = lax.axis_size("nodes")
    capacity = max(2, min(nblocks // 2, 3 * nblocks * slots // (2 * devices)))
    tile_count = devices * capacity
    query_n = unit_rows(jnp.dot(feats, w_query, preferred_element_type=jnp.float32), count)
    key_n = unit_rows(jnp.dot(feats, w_key, preferred_element_type=jnp.float32), count)
    value_b = jnp.dot(feats, w_value, preferred_element_type=jnp.float32).astype(jnp.bfloat16)
    query_blocks = query_n.reshape(nblocks, width, feat)
    head_of = jnp.arange(feat, dtype=jnp.int32) // (feat // count)
    query_stack = jnp.concatenate(
        [jnp.where(head_of[None, None, :] == h, query_blocks, 0) for h in range(count)], axis=1
    )
    own_kv = jnp.concatenate([key_n, value_b], axis=1).reshape(nblocks, width, 2 * feat)
    owners = nbr_owner.reshape(-1)
    owner_hot = (owners[:, None] == jnp.arange(devices, dtype=jnp.int32)[None, :]).astype(jnp.int32)
    rank = jnp.sum(jnp.cumsum(owner_hot, axis=0) * owner_hot, axis=1) - 1
    target = owners * capacity + rank
    place = (target[:, None] == jnp.arange(tile_count, dtype=jnp.int32)[None, :]).astype(jnp.int32)
    valid = (slot_valid.reshape(-1) > 0).astype(jnp.int32)
    wanted = jnp.where(valid > 0, nbr_local.reshape(-1), -1)
    request = jnp.sum(place * (wanted[:, None] + 1), axis=0) - 1
    asked = lax.all_to_all(
        request.reshape(devices, capacity), "nodes", split_axis=0, concat_axis=0, tiled=True
    ).reshape(-1)
    heads = lax.axis_size("heads")
    me = lax.axis_index("heads")
    quarter = width // heads
    model = feats.shape[1]
    feats_parts = feats.reshape(nblocks * heads, quarter, model)
    pick = jnp.clip(asked, 0, nblocks - 1).astype(jnp.int32) * heads + me
    payload = gather_blocks(feats_parts, pick)
    w_out, w_key_b, w_value_b, payload = lax.optimization_barrier((w_out, w_key, w_value, payload))
    w_out_t = lax.all_gather(w_out.T, "heads", axis=1, tiled=True)
    w_key_all = lax.all_gather(w_key_b, "heads", axis=1, tiled=True).reshape(model, heads, feat)
    w_value_all = lax.all_gather(w_value_b, "heads", axis=1, tiled=True).reshape(model, heads, feat)
    w_kv_all = jnp.stack([w_key_all, w_value_all], axis=2).reshape(model, heads * 2 * feat)
    recv = lax.all_to_all(
        payload.reshape(devices, capacity * quarter, model),
        "nodes",
        split_axis=0,
        concat_axis=0,
        tiled=True,
    ).reshape(tile_count, quarter, model)
    recv, w_out_t, w_kv_all = lax.optimization_barrier((recv, w_out_t, w_kv_all))
    slot_of = jnp.clip(target, 0, tile_count - 1).astype(jnp.int32)
    pairs = slot_of.shape[0]
    send = project_all(recv, slot_of, w_kv_all, heads, feat // count).reshape(
        heads, pairs, quarter, 2 * feat
    )
    got = lax.all_to_all(send, "heads", 0, 0, tiled=True)
    pair_kv = got
    pair_ids = jnp.arange(pairs, dtype=jnp.int32)
    heads_n = lax.axis_size("heads")
    me_h = lax.axis_index("heads")

    def out_part(piece, source):
        w_part = lax.dynamic_slice(w_out_t, (me_h * feat, source * feat), (feat, feat))
        return lax.dot_general(
            piece, w_part, (((1,), (1,)), ((), ())), preferred_element_type=jnp.float32
        )

    halves = 2
    per_half = nblocks // halves
    outs = []
    for part in range(halves):
        lo, hi = part * per_half, (part + 1) * per_half
        attn_half = attend(
            query_stack[lo:hi],
            own_kv[lo:hi],
            pair_kv,
            pair_ids[lo * slots:hi * slots],
            valid[lo * slots:hi * slots],
            head_scale,
        ).reshape(per_half * width, feat)
        mixed = out_part(attn_half, me_h)
        for k in range(1, heads_n):
            piece = lax.ppermute(attn_half, "heads", [(j, (j + k) % heads_n) for j in range(heads_n)])
            mixed = mixed + out_part(piece, (me_h - k) % heads_n)
        outs.append(mixed.astype(jnp.bfloat16))
    return jnp.concatenate(outs, axis=0)


def solution(mesh):
    placed = (
        P("nodes", None),
        P(None, "heads"),
        P(None, "heads"),
        P(None, "heads"),
        P("heads", None),
        P("heads"),
        P("nodes", None),
        P("nodes", None),
        P("nodes", None),
    )
    return jax.shard_map(
        body, mesh=mesh, in_specs=placed, out_specs=P("nodes", "heads"), check_vma=False
    )
```

```python
import functools

import jax
import jax.numpy as jnp
from jax import lax
from jax.experimental import pallas as pl
from jax.experimental.pallas import tpu as pltpu
from jax.sharding import PartitionSpec as P


def unit_rows(values, count):
    shaped = values.reshape(values.shape[0], count, -1)
    total = jnp.sum(shaped * shaped, axis=-1, keepdims=True)
    return (shaped * lax.rsqrt(total + 1e-06)).astype(jnp.bfloat16).reshape(values.shape)


def attend_kernel(slot_ref, live_ref, scale_ref, q_ref, own_ref, recv_ref, out_ref, buf, sems, *, count, slots):
    b = pl.program_id(0)
    pairs = buf.shape[0]
    stacked, feat = q_ref.shape[1], q_ref.shape[2]
    width = stacked // count
    hd = feat // count

    def pair_copy(p):
        return pltpu.make_async_copy(recv_ref.at[:, slot_ref[p]], buf.at[p], sems.at[p])

    @pl.when(b == 0)
    def _():
        for p in range(pairs):
            pair_copy(p).start()

    for s in range(slots):
        pair_copy(b * slots + s).wait()
    lane_head = lax.broadcasted_iota(jnp.int32, (width, feat), 1) // hd
    stack_rows = lax.broadcasted_iota(jnp.int32, (stacked, 1), 0)
    scale_col = jnp.zeros((stacked, 1), jnp.float32)
    for h in range(count):
        inside = (stack_rows >= h * width) & (stack_rows < (h + 1) * width)
        scale_col = jnp.where(inside, scale_ref[h], scale_col)
    key_lanes = lax.broadcasted_iota(jnp.int32, (1, (slots + 1) * width), 1)
    live_row = jnp.ones((1, (slots + 1) * width), jnp.float32)
    for s in range(slots):
        inside = (key_lanes >= (s + 1) * width) & (key_lanes < (s + 2) * width)
        live_row = jnp.where(inside, live_ref[b * slots + s].astype(jnp.float32), live_row)
    blocks = [own_ref[b]] + [buf[b * slots + s].reshape(width, 2 * feat) for s in range(slots)]
    keys = jnp.concatenate([blk[:, :feat] for blk in blocks], axis=0)
    values = jnp.concatenate([blk[:, feat:] for blk in blocks], axis=0)
    s_all = lax.dot_general(
        q_ref[0], keys, (((1,), (1,)), ((), ())), preferred_element_type=jnp.float32
    )
    w = jnp.exp(scale_col * (s_all - 1.0)) * live_row
    den = jnp.sum(w, axis=1, keepdims=True)
    w_b = w.astype(jnp.bfloat16)
    num = jnp.zeros((width, feat), jnp.float32)
    den_full = jnp.zeros((width, feat), jnp.float32)
    for h in range(count):
        part = jnp.dot(w_b[h * width:(h + 1) * width], values, preferred_element_type=jnp.float32)
        num = jnp.where(lane_head == h, part, num)
        den_full = jnp.where(lane_head == h, den[h * width:(h + 1) * width], den_full)
    out_ref[0] = (num / den_full).astype(out_ref.dtype)


def attend(query_stack, own_kv, recv_kv, slot_of, live, scales):
    nblocks, stacked, feat = query_stack.shape
    count = scales.shape[0]
    width = stacked // count
    slots = slot_of.shape[0] // nblocks
    grid_spec = pltpu.PrefetchScalarGridSpec(
        num_scalar_prefetch=2,
        grid=(nblocks,),
        in_specs=[
            pl.BlockSpec(memory_space=pltpu.SMEM),
            pl.BlockSpec((1, stacked, feat), lambda b, slot_of, live: (b, 0, 0)),
            pl.BlockSpec((nblocks, width, 2 * feat), lambda b, slot_of, live: (0, 0, 0)),
            pl.BlockSpec(memory_space=pl.ANY),
        ],
        out_specs=pl.BlockSpec((1, width, feat), lambda b, slot_of, live: (b, 0, 0)),
        scratch_shapes=[
            pltpu.VMEM((nblocks * slots,) + recv_kv.shape[:1] + recv_kv.shape[2:], recv_kv.dtype),
            pltpu.SemaphoreType.DMA((nblocks * slots,)),
        ],
    )
    return pl.pallas_call(
        functools.partial(attend_kernel, count=count, slots=slots),
        grid_spec=grid_spec,
        out_shape=jax.ShapeDtypeStruct((nblocks, width, feat), jnp.bfloat16),
        compiler_params=pltpu.CompilerParams(vmem_limit_bytes=48 * 1024 * 1024),
    )(slot_of, live, scales, query_stack, own_kv, recv_kv)


def gather_kernel(pick_ref, src_ref, out_ref):
    g = pl.program_id(0)
    group = out_ref.shape[0]
    for i in range(group):
        out_ref[i] = src_ref[pick_ref[g * group + i]]


def gather_blocks(blocks, pick):
    nblocks, r, l = blocks.shape
    tiles = pick.shape[0]
    group = 128
    grid_spec = pltpu.PrefetchScalarGridSpec(
        num_scalar_prefetch=1,
        grid=(tiles // group,),
        in_specs=[pl.BlockSpec((nblocks, r, l), lambda g, pick: (0, 0, 0))],
        out_specs=pl.BlockSpec((group, r, l), lambda g, pick: (g, 0, 0)),
    )
    return pl.pallas_call(
        gather_kernel,
        grid_spec=grid_spec,
        out_shape=jax.ShapeDtypeStruct((tiles, r, l), blocks.dtype),
    )(pick, blocks)


def project_kernel(slot_ref, recv_ref, w_ref, out_ref, rows_scr, sems, *, hd):
    y = pl.program_id(0)
    pairs = sems.shape[0]
    quarter = recv_ref.shape[1]

    def piece_copy(p):
        return pltpu.make_async_copy(
            recv_ref.at[slot_ref[p]], rows_scr.at[pl.ds(p * quarter, quarter)], sems.at[p]
        )

    @pl.when(y == 0)
    def _():
        for p in range(pairs):
            piece_copy(p).start()
        for p in range(pairs):
            piece_copy(p).wait()

    kv = jnp.dot(rows_scr[...], w_ref[...], preferred_element_type=jnp.float32)
    feat = kv.shape[1] // 2
    keys = kv[:, :feat]
    lane = lax.broadcasted_iota(jnp.int32, (1, feat), 1)
    sq = keys * keys
    scale = jnp.zeros(keys.shape, jnp.float32)
    for h in range(feat // hd):
        inside = (lane >= h * hd) & (lane < (h + 1) * hd)
        total = jnp.sum(jnp.where(inside, sq, 0.0), axis=1, keepdims=True)
        scale = jnp.where(inside, lax.rsqrt(total + 1e-06), scale)
    out_ref[0, :, :feat] = (keys * scale).astype(out_ref.dtype)
    out_ref[0, :, feat:] = kv[:, feat:].astype(out_ref.dtype)


def project_all(recv, slot_of, w_kv, heads, hd):
    tiles, quarter, model = recv.shape
    pairs = slot_of.shape[0]
    n = pairs * quarter
    cols = w_kv.shape[1] // heads
    grid_spec = pltpu.PrefetchScalarGridSpec(
        num_scalar_prefetch=1,
        grid=(heads,),
        in_specs=[
            pl.BlockSpec(memory_space=pl.ANY),
            pl.BlockSpec((model, cols), lambda y, slot_of: (0, y)),
        ],
        out_specs=pl.BlockSpec((1, n, cols), lambda y, slot_of: (y, 0, 0)),
        scratch_shapes=[
            pltpu.VMEM((n, model), recv.dtype),
            pltpu.SemaphoreType.DMA((pairs,)),
        ],
    )
    return pl.pallas_call(
        functools.partial(project_kernel, hd=hd),
        grid_spec=grid_spec,
        out_shape=jax.ShapeDtypeStruct((heads, n, cols), jnp.bfloat16),
    )(slot_of, recv, w_kv)


def body(feats, w_query, w_key, w_value, w_out, head_scale, nbr_owner, nbr_local, slot_valid):
    rows = feats.shape[0]
    feat = w_query.shape[1]
    count = head_scale.shape[0]
    nblocks, slots = nbr_owner.shape
    width = rows // nblocks
    devices = lax.axis_size("nodes")
    capacity = max(2, min(nblocks // 2, 3 * nblocks * slots // (2 * devices)))
    tile_count = devices * capacity
    query_n = unit_rows(jnp.dot(feats, w_query, preferred_element_type=jnp.float32), count)
    key_n = unit_rows(jnp.dot(feats, w_key, preferred_element_type=jnp.float32), count)
    value_b = jnp.dot(feats, w_value, preferred_element_type=jnp.float32).astype(jnp.bfloat16)
    query_blocks = query_n.reshape(nblocks, width, feat)
    head_of = jnp.arange(feat, dtype=jnp.int32) // (feat // count)
    query_stack = jnp.concatenate(
        [jnp.where(head_of[None, None, :] == h, query_blocks, 0) for h in range(count)], axis=1
    )
    own_kv = jnp.concatenate([key_n, value_b], axis=1).reshape(nblocks, width, 2 * feat)
    owners = nbr_owner.reshape(-1)
    owner_hot = (owners[:, None] == jnp.arange(devices, dtype=jnp.int32)[None, :]).astype(jnp.int32)
    rank = jnp.sum(jnp.cumsum(owner_hot, axis=0) * owner_hot, axis=1) - 1
    target = owners * capacity + rank
    place = (target[:, None] == jnp.arange(tile_count, dtype=jnp.int32)[None, :]).astype(jnp.int32)
    valid = (slot_valid.reshape(-1) > 0).astype(jnp.int32)
    wanted = jnp.where(valid > 0, nbr_local.reshape(-1), -1)
    request = jnp.sum(place * (wanted[:, None] + 1), axis=0) - 1
    asked = lax.all_to_all(
        request.reshape(devices, capacity), "nodes", split_axis=0, concat_axis=0, tiled=True
    ).reshape(-1)
    heads = lax.axis_size("heads")
    me = lax.axis_index("heads")
    quarter = width // heads
    model = feats.shape[1]
    feats_parts = feats.reshape(nblocks * heads, quarter, model)
    pick = jnp.clip(asked, 0, nblocks - 1).astype(jnp.int32) * heads + me
    payload = gather_blocks(feats_parts, pick)
    w_out, w_key_b, w_value_b, payload = lax.optimization_barrier((w_out, w_key, w_value, payload))
    w_out_t = lax.all_gather(w_out.T, "heads", axis=1, tiled=True)
    w_key_all = lax.all_gather(w_key_b, "heads", axis=1, tiled=True).reshape(model, heads, feat)
    w_value_all = lax.all_gather(w_value_b, "heads", axis=1, tiled=True).reshape(model, heads, feat)
    w_kv_all = jnp.stack([w_key_all, w_value_all], axis=2).reshape(model, heads * 2 * feat)
    recv = lax.all_to_all(
        payload.reshape(devices, capacity * quarter, model),
        "nodes",
        split_axis=0,
        concat_axis=0,
        tiled=True,
    ).reshape(tile_count, quarter, model)
    recv, w_out_t, w_kv_all = lax.optimization_barrier((recv, w_out_t, w_kv_all))
    slot_of = jnp.clip(target, 0, tile_count - 1).astype(jnp.int32)
    pairs = slot_of.shape[0]
    send = project_all(recv, slot_of, w_kv_all, heads, feat // count).reshape(
        heads, pairs, quarter, 2 * feat
    )
    got = lax.all_to_all(send, "heads", 0, 0, tiled=True)
    pair_kv = got
    pair_ids = jnp.arange(pairs, dtype=jnp.int32)
    heads_n = lax.axis_size("heads")
    me_h = lax.axis_index("heads")

    def out_part(piece, source):
        w_part = lax.dynamic_slice(w_out_t, (me_h * feat, source * feat), (feat, feat))
        return lax.dot_general(
            piece, w_part, (((1,), (1,)), ((), ())), preferred_element_type=jnp.float32
        )

    halves = 2
    per_half = nblocks // halves
    outs = []
    for part in range(halves):
        lo, hi = part * per_half, (part + 1) * per_half
        attn_half = attend(
            query_stack[lo:hi],
            own_kv[lo:hi],
            pair_kv,
            pair_ids[lo * slots:hi * slots],
            valid[lo * slots:hi * slots],
            head_scale,
        ).reshape(per_half * width, feat)
        mixed = out_part(attn_half, me_h)
        for k in range(1, heads_n):
            piece = lax.ppermute(attn_half, "heads", [(j, (j + k) % heads_n) for j in range(heads_n)])
            mixed = mixed + out_part(piece, (me_h - k) % heads_n)
        outs.append(mixed.astype(jnp.bfloat16))
    return jnp.concatenate(outs, axis=0)


def solution(mesh):
    placed = (
        P("nodes", None),
        P(None, "heads"),
        P(None, "heads"),
        P(None, "heads"),
        P("heads", None),
        P("heads"),
        P("nodes", None),
        P("nodes", None),
        P("nodes", None),
    )
    return jax.shard_map(
        body, mesh=mesh, in_specs=placed, out_specs=P("nodes", "heads"), check_vma=False
    )
```

```python
import functools

import jax
import jax.numpy as jnp
from jax import lax
from jax.experimental import pallas as pl
from jax.experimental.pallas import tpu as pltpu
from jax.sharding import PartitionSpec as P


def unit_rows(values, count):
    shaped = values.reshape(values.shape[0], count, -1)
    total = jnp.sum(shaped * shaped, axis=-1, keepdims=True)
    return (shaped * lax.rsqrt(total + 1e-06)).astype(jnp.bfloat16).reshape(values.shape)


def attend_kernel(slot_ref, live_ref, scale_ref, q_ref, own_ref, recv_ref, out_ref, buf, sems, *, count, slots):
    b = pl.program_id(0)
    pairs = buf.shape[0]
    stacked, feat = q_ref.shape[1], q_ref.shape[2]
    width = stacked // count
    hd = feat // count

    def pair_copy(p):
        return pltpu.make_async_copy(recv_ref.at[:, slot_ref[p]], buf.at[p], sems.at[p])

    @pl.when(b == 0)
    def _():
        for p in range(pairs):
            pair_copy(p).start()

    for s in range(slots):
        pair_copy(b * slots + s).wait()
    lane_head = lax.broadcasted_iota(jnp.int32, (width, feat), 1) // hd
    stack_rows = lax.broadcasted_iota(jnp.int32, (stacked, 1), 0)
    scale_col = jnp.zeros((stacked, 1), jnp.float32)
    for h in range(count):
        inside = (stack_rows >= h * width) & (stack_rows < (h + 1) * width)
        scale_col = jnp.where(inside, scale_ref[h], scale_col)
    key_lanes = lax.broadcasted_iota(jnp.int32, (1, (slots + 1) * width), 1)
    live_row = jnp.ones((1, (slots + 1) * width), jnp.float32)
    for s in range(slots):
        inside = (key_lanes >= (s + 1) * width) & (key_lanes < (s + 2) * width)
        live_row = jnp.where(inside, live_ref[b * slots + s].astype(jnp.float32), live_row)
    blocks = [own_ref[b]] + [buf[b * slots + s].reshape(width, 2 * feat) for s in range(slots)]
    keys = jnp.concatenate([blk[:, :feat] for blk in blocks], axis=0)
    values = jnp.concatenate([blk[:, feat:] for blk in blocks], axis=0)
    s_all = lax.dot_general(
        q_ref[0], keys, (((1,), (1,)), ((), ())), preferred_element_type=jnp.float32
    )
    w = jnp.exp(scale_col * (s_all - 1.0)) * live_row
    den = jnp.sum(w, axis=1, keepdims=True)
    w_b = w.astype(jnp.bfloat16)
    num = jnp.zeros((width, feat), jnp.float32)
    den_full = jnp.zeros((width, feat), jnp.float32)
    for h in range(count):
        part = jnp.dot(w_b[h * width:(h + 1) * width], values, preferred_element_type=jnp.float32)
        num = jnp.where(lane_head == h, part, num)
        den_full = jnp.where(lane_head == h, den[h * width:(h + 1) * width], den_full)
    out_ref[0] = (num / den_full).astype(out_ref.dtype)


def attend(query_stack, own_kv, recv_kv, slot_of, live, scales):
    nblocks, stacked, feat = query_stack.shape
    count = scales.shape[0]
    width = stacked // count
    slots = slot_of.shape[0] // nblocks
    grid_spec = pltpu.PrefetchScalarGridSpec(
        num_scalar_prefetch=2,
        grid=(nblocks,),
        in_specs=[
            pl.BlockSpec(memory_space=pltpu.SMEM),
            pl.BlockSpec((1, stacked, feat), lambda b, slot_of, live: (b, 0, 0)),
            pl.BlockSpec((nblocks, width, 2 * feat), lambda b, slot_of, live: (0, 0, 0)),
            pl.BlockSpec(memory_space=pl.ANY),
        ],
        out_specs=pl.BlockSpec((1, width, feat), lambda b, slot_of, live: (b, 0, 0)),
        scratch_shapes=[
            pltpu.VMEM((nblocks * slots,) + recv_kv.shape[:1] + recv_kv.shape[2:], recv_kv.dtype),
            pltpu.SemaphoreType.DMA((nblocks * slots,)),
        ],
    )
    return pl.pallas_call(
        functools.partial(attend_kernel, count=count, slots=slots),
        grid_spec=grid_spec,
        out_shape=jax.ShapeDtypeStruct((nblocks, width, feat), jnp.bfloat16),
        compiler_params=pltpu.CompilerParams(vmem_limit_bytes=48 * 1024 * 1024),
    )(slot_of, live, scales, query_stack, own_kv, recv_kv)


def gather_kernel(pick_ref, src_ref, out_ref):
    g = pl.program_id(0)
    group = out_ref.shape[0]
    for i in range(group):
        out_ref[i] = src_ref[pick_ref[g * group + i]]


def gather_blocks(blocks, pick):
    nblocks, r, l = blocks.shape
    tiles = pick.shape[0]
    group = 128
    grid_spec = pltpu.PrefetchScalarGridSpec(
        num_scalar_prefetch=1,
        grid=(tiles // group,),
        in_specs=[pl.BlockSpec((nblocks, r, l), lambda g, pick: (0, 0, 0))],
        out_specs=pl.BlockSpec((group, r, l), lambda g, pick: (g, 0, 0)),
    )
    return pl.pallas_call(
        gather_kernel,
        grid_spec=grid_spec,
        out_shape=jax.ShapeDtypeStruct((tiles, r, l), blocks.dtype),
    )(pick, blocks)


def project_kernel(slot_ref, recv_ref, w_ref, out_ref, rows_scr, sems, *, hd):
    pairs = sems.shape[0]
    quarter = recv_ref.shape[1]
    planes = out_ref.shape[0]
    cols = out_ref.shape[2]

    def piece_copy(p):
        return pltpu.make_async_copy(
            recv_ref.at[slot_ref[p]], rows_scr.at[pl.ds(p * quarter, quarter)], sems.at[p]
        )

    for p in range(pairs):
        piece_copy(p).start()
    for p in range(pairs):
        piece_copy(p).wait()
    rows = rows_scr[...]
    feat = cols // 2
    lane = lax.broadcasted_iota(jnp.int32, (1, feat), 1)
    for y in range(planes):
        kv = jnp.dot(rows, w_ref[:, y * cols:(y + 1) * cols], preferred_element_type=jnp.float32)
        keys = kv[:, :feat]
        sq = keys * keys
        scale = jnp.zeros(keys.shape, jnp.float32)
        for h in range(feat // hd):
            inside = (lane >= h * hd) & (lane < (h + 1) * hd)
            total = jnp.sum(jnp.where(inside, sq, 0.0), axis=1, keepdims=True)
            scale = jnp.where(inside, lax.rsqrt(total + 1e-06), scale)
        out_ref[y, :, :feat] = (keys * scale).astype(out_ref.dtype)
        out_ref[y, :, feat:] = kv[:, feat:].astype(out_ref.dtype)


def project_all(recv, slot_of, w_kv, heads, hd):
    tiles, quarter, model = recv.shape
    pairs = slot_of.shape[0]
    n = pairs * quarter
    cols = w_kv.shape[1] // heads
    grid_spec = pltpu.PrefetchScalarGridSpec(
        num_scalar_prefetch=1,
        grid=(1,),
        in_specs=[
            pl.BlockSpec(memory_space=pl.ANY),
            pl.BlockSpec((model, heads * cols), lambda i, slot_of: (0, 0)),
        ],
        out_specs=pl.BlockSpec((heads, n, cols), lambda i, slot_of: (0, 0, 0)),
        scratch_shapes=[
            pltpu.VMEM((n, model), recv.dtype),
            pltpu.SemaphoreType.DMA((pairs,)),
        ],
    )
    return pl.pallas_call(
        functools.partial(project_kernel, hd=hd),
        grid_spec=grid_spec,
        out_shape=jax.ShapeDtypeStruct((heads, n, cols), jnp.bfloat16),
    )(slot_of, recv, w_kv)


def body(feats, w_query, w_key, w_value, w_out, head_scale, nbr_owner, nbr_local, slot_valid):
    rows = feats.shape[0]
    feat = w_query.shape[1]
    count = head_scale.shape[0]
    nblocks, slots = nbr_owner.shape
    width = rows // nblocks
    devices = lax.axis_size("nodes")
    capacity = max(2, min(nblocks // 2, 3 * nblocks * slots // (2 * devices)))
    tile_count = devices * capacity
    query_n = unit_rows(jnp.dot(feats, w_query, preferred_element_type=jnp.float32), count)
    key_n = unit_rows(jnp.dot(feats, w_key, preferred_element_type=jnp.float32), count)
    value_b = jnp.dot(feats, w_value, preferred_element_type=jnp.float32).astype(jnp.bfloat16)
    query_blocks = query_n.reshape(nblocks, width, feat)
    head_of = jnp.arange(feat, dtype=jnp.int32) // (feat // count)
    query_stack = jnp.concatenate(
        [jnp.where(head_of[None, None, :] == h, query_blocks, 0) for h in range(count)], axis=1
    )
    own_kv = jnp.concatenate([key_n, value_b], axis=1).reshape(nblocks, width, 2 * feat)
    owners = nbr_owner.reshape(-1)
    owner_hot = (owners[:, None] == jnp.arange(devices, dtype=jnp.int32)[None, :]).astype(jnp.int32)
    rank = jnp.sum(jnp.cumsum(owner_hot, axis=0) * owner_hot, axis=1) - 1
    target = owners * capacity + rank
    place = (target[:, None] == jnp.arange(tile_count, dtype=jnp.int32)[None, :]).astype(jnp.int32)
    valid = (slot_valid.reshape(-1) > 0).astype(jnp.int32)
    wanted = jnp.where(valid > 0, nbr_local.reshape(-1), -1)
    request = jnp.sum(place * (wanted[:, None] + 1), axis=0) - 1
    asked = lax.all_to_all(
        request.reshape(devices, capacity), "nodes", split_axis=0, concat_axis=0, tiled=True
    ).reshape(-1)
    heads = lax.axis_size("heads")
    me = lax.axis_index("heads")
    quarter = width // heads
    model = feats.shape[1]
    feats_parts = feats.reshape(nblocks * heads, quarter, model)
    pick = jnp.clip(asked, 0, nblocks - 1).astype(jnp.int32) * heads + me
    payload = gather_blocks(feats_parts, pick)
    w_out, w_key_b, w_value_b, payload = lax.optimization_barrier((w_out, w_key, w_value, payload))
    w_out_t = lax.all_gather(w_out.T, "heads", axis=1, tiled=True)
    w_key_all = lax.all_gather(w_key_b, "heads", axis=1, tiled=True).reshape(model, heads, feat)
    w_value_all = lax.all_gather(w_value_b, "heads", axis=1, tiled=True).reshape(model, heads, feat)
    w_kv_all = jnp.stack([w_key_all, w_value_all], axis=2).reshape(model, heads * 2 * feat)
    recv = lax.all_to_all(
        payload.reshape(devices, capacity * quarter, model),
        "nodes",
        split_axis=0,
        concat_axis=0,
        tiled=True,
    ).reshape(tile_count, quarter, model)
    recv, w_out_t, w_kv_all = lax.optimization_barrier((recv, w_out_t, w_kv_all))
    slot_of = jnp.clip(target, 0, tile_count - 1).astype(jnp.int32)
    pairs = slot_of.shape[0]
    send = project_all(recv, slot_of, w_kv_all, heads, feat // count).reshape(
        heads, pairs, quarter, 2 * feat
    )
    got = lax.all_to_all(send, "heads", 0, 0, tiled=True)
    pair_kv = got
    pair_ids = jnp.arange(pairs, dtype=jnp.int32)
    heads_n = lax.axis_size("heads")
    me_h = lax.axis_index("heads")

    def out_part(piece, source):
        w_part = lax.dynamic_slice(w_out_t, (me_h * feat, source * feat), (feat, feat))
        return lax.dot_general(
            piece, w_part, (((1,), (1,)), ((), ())), preferred_element_type=jnp.float32
        )

    halves = 2
    per_half = nblocks // halves
    outs = []
    for part in range(halves):
        lo, hi = part * per_half, (part + 1) * per_half
        attn_half = attend(
            query_stack[lo:hi],
            own_kv[lo:hi],
            pair_kv,
            pair_ids[lo * slots:hi * slots],
            valid[lo * slots:hi * slots],
            head_scale,
        ).reshape(per_half * width, feat)
        mixed = out_part(attn_half, me_h)
        for k in range(1, heads_n):
            piece = lax.ppermute(attn_half, "heads", [(j, (j + k) % heads_n) for j in range(heads_n)])
            mixed = mixed + out_part(piece, (me_h - k) % heads_n)
        outs.append(mixed.astype(jnp.bfloat16))
    return jnp.concatenate(outs, axis=0)


def solution(mesh):
    placed = (
        P("nodes", None),
        P(None, "heads"),
        P(None, "heads"),
        P(None, "heads"),
        P("heads", None),
        P("heads"),
        P("nodes", None),
        P("nodes", None),
        P("nodes", None),
    )
    return jax.shard_map(
        body, mesh=mesh, in_specs=placed, out_specs=P("nodes", "heads"), check_vma=False
    )
```

```python
import functools

import jax
import jax.numpy as jnp
from jax import lax
from jax.experimental import pallas as pl
from jax.experimental.pallas import tpu as pltpu
from jax.sharding import PartitionSpec as P


def unit_rows(values, count):
    shaped = values.reshape(values.shape[0], count, -1)
    total = jnp.sum(shaped * shaped, axis=-1, keepdims=True)
    return (shaped * lax.rsqrt(total + 1e-06)).astype(jnp.bfloat16).reshape(values.shape)


def attend_kernel(slot_ref, live_ref, scale_ref, q_ref, own_ref, recv_ref, out_ref, buf, sems, *, count, slots):
    b = pl.program_id(0)
    pairs = buf.shape[0]
    stacked, feat = q_ref.shape[1], q_ref.shape[2]
    width = stacked // count
    hd = feat // count

    def pair_copy(p):
        return pltpu.make_async_copy(recv_ref.at[:, slot_ref[p]], buf.at[p], sems.at[p])

    @pl.when(b == 0)
    def _():
        for p in range(pairs):
            pair_copy(p).start()

    for s in range(slots):
        pair_copy(b * slots + s).wait()
    lane_head = lax.broadcasted_iota(jnp.int32, (width, feat), 1) // hd
    stack_rows = lax.broadcasted_iota(jnp.int32, (stacked, 1), 0)
    scale_col = jnp.zeros((stacked, 1), jnp.float32)
    for h in range(count):
        inside = (stack_rows >= h * width) & (stack_rows < (h + 1) * width)
        scale_col = jnp.where(inside, scale_ref[h], scale_col)
    key_lanes = lax.broadcasted_iota(jnp.int32, (1, (slots + 1) * width), 1)
    live_row = jnp.ones((1, (slots + 1) * width), jnp.float32)
    for s in range(slots):
        inside = (key_lanes >= (s + 1) * width) & (key_lanes < (s + 2) * width)
        live_row = jnp.where(inside, live_ref[b * slots + s].astype(jnp.float32), live_row)
    blocks = [own_ref[b]] + [buf[b * slots + s].reshape(width, 2 * feat) for s in range(slots)]
    keys = jnp.concatenate([blk[:, :feat] for blk in blocks], axis=0)
    values = jnp.concatenate([blk[:, feat:] for blk in blocks], axis=0)
    s_all = lax.dot_general(
        q_ref[0], keys, (((1,), (1,)), ((), ())), preferred_element_type=jnp.float32
    )
    w = jnp.exp(scale_col * (s_all - 1.0)) * live_row
    den = jnp.sum(w, axis=1, keepdims=True)
    w_b = w.astype(jnp.bfloat16)
    num = jnp.zeros((width, feat), jnp.float32)
    den_full = jnp.zeros((width, feat), jnp.float32)
    for h in range(count):
        part = jnp.dot(w_b[h * width:(h + 1) * width], values, preferred_element_type=jnp.float32)
        num = jnp.where(lane_head == h, part, num)
        den_full = jnp.where(lane_head == h, den[h * width:(h + 1) * width], den_full)
    out_ref[0] = (num / den_full).astype(out_ref.dtype)


def attend(query_stack, own_kv, recv_kv, slot_of, live, scales):
    nblocks, stacked, feat = query_stack.shape
    count = scales.shape[0]
    width = stacked // count
    slots = slot_of.shape[0] // nblocks
    grid_spec = pltpu.PrefetchScalarGridSpec(
        num_scalar_prefetch=2,
        grid=(nblocks,),
        in_specs=[
            pl.BlockSpec(memory_space=pltpu.SMEM),
            pl.BlockSpec((1, stacked, feat), lambda b, slot_of, live: (b, 0, 0)),
            pl.BlockSpec((nblocks, width, 2 * feat), lambda b, slot_of, live: (0, 0, 0)),
            pl.BlockSpec(memory_space=pl.ANY),
        ],
        out_specs=pl.BlockSpec((1, width, feat), lambda b, slot_of, live: (b, 0, 0)),
        scratch_shapes=[
            pltpu.VMEM((nblocks * slots,) + recv_kv.shape[:1] + recv_kv.shape[2:], recv_kv.dtype),
            pltpu.SemaphoreType.DMA((nblocks * slots,)),
        ],
    )
    return pl.pallas_call(
        functools.partial(attend_kernel, count=count, slots=slots),
        grid_spec=grid_spec,
        out_shape=jax.ShapeDtypeStruct((nblocks, width, feat), jnp.bfloat16),
        compiler_params=pltpu.CompilerParams(vmem_limit_bytes=48 * 1024 * 1024),
    )(slot_of, live, scales, query_stack, own_kv, recv_kv)


def gather_kernel(pick_ref, src_ref, out_ref):
    g = pl.program_id(0)
    group = out_ref.shape[0]
    for i in range(group):
        out_ref[i] = src_ref[pick_ref[g * group + i]]


def gather_blocks(blocks, pick):
    nblocks, r, l = blocks.shape
    tiles = pick.shape[0]
    group = 128
    grid_spec = pltpu.PrefetchScalarGridSpec(
        num_scalar_prefetch=1,
        grid=(tiles // group,),
        in_specs=[pl.BlockSpec((nblocks, r, l), lambda g, pick: (0, 0, 0))],
        out_specs=pl.BlockSpec((group, r, l), lambda g, pick: (g, 0, 0)),
    )
    return pl.pallas_call(
        gather_kernel,
        grid_spec=grid_spec,
        out_shape=jax.ShapeDtypeStruct((tiles, r, l), blocks.dtype),
    )(pick, blocks)


def project_kernel(slot_ref, recv_ref, w_ref, out_ref, rows_scr, sems, *, hd):
    y = pl.program_id(0)
    pairs = sems.shape[0]
    quarter = recv_ref.shape[1]

    def piece_copy(p):
        return pltpu.make_async_copy(
            recv_ref.at[slot_ref[p]], rows_scr.at[pl.ds(p * quarter, quarter)], sems.at[p]
        )

    @pl.when(y == 0)
    def _():
        for p in range(pairs):
            piece_copy(p).start()
        for p in range(pairs):
            piece_copy(p).wait()

    kv = jnp.dot(rows_scr[...], w_ref[...], preferred_element_type=jnp.float32)
    feat = kv.shape[1] // 2
    keys = kv[:, :feat]
    lane = lax.broadcasted_iota(jnp.int32, (1, feat), 1)
    sq = keys * keys
    scale = jnp.zeros(keys.shape, jnp.float32)
    for h in range(feat // hd):
        inside = (lane >= h * hd) & (lane < (h + 1) * hd)
        total = jnp.sum(jnp.where(inside, sq, 0.0), axis=1, keepdims=True)
        scale = jnp.where(inside, lax.rsqrt(total + 1e-06), scale)
    out_ref[0, :, :feat] = (keys * scale).astype(out_ref.dtype)
    out_ref[0, :, feat:] = kv[:, feat:].astype(out_ref.dtype)


def project_all(recv, slot_of, w_kv, heads, hd):
    tiles, quarter, model = recv.shape
    pairs = slot_of.shape[0]
    n = pairs * quarter
    cols = w_kv.shape[1] // heads
    grid_spec = pltpu.PrefetchScalarGridSpec(
        num_scalar_prefetch=1,
        grid=(heads,),
        in_specs=[
            pl.BlockSpec(memory_space=pl.ANY),
            pl.BlockSpec((model, cols), lambda y, slot_of: (0, y)),
        ],
        out_specs=pl.BlockSpec((1, n, cols), lambda y, slot_of: (y, 0, 0)),
        scratch_shapes=[
            pltpu.VMEM((n, model), recv.dtype),
            pltpu.SemaphoreType.DMA((pairs,)),
        ],
    )
    return pl.pallas_call(
        functools.partial(project_kernel, hd=hd),
        grid_spec=grid_spec,
        out_shape=jax.ShapeDtypeStruct((heads, n, cols), jnp.bfloat16),
    )(slot_of, recv, w_kv)


def body(feats, w_query, w_key, w_value, w_out, head_scale, nbr_owner, nbr_local, slot_valid):
    rows = feats.shape[0]
    feat = w_query.shape[1]
    count = head_scale.shape[0]
    nblocks, slots = nbr_owner.shape
    width = rows // nblocks
    devices = lax.axis_size("nodes")
    capacity = max(2, min(nblocks // 2, 3 * nblocks * slots // (2 * devices)))
    tile_count = devices * capacity
    query_n = unit_rows(jnp.dot(feats, w_query, preferred_element_type=jnp.float32), count)
    key_n = unit_rows(jnp.dot(feats, w_key, preferred_element_type=jnp.float32), count)
    value_b = jnp.dot(feats, w_value, preferred_element_type=jnp.float32).astype(jnp.bfloat16)
    query_blocks = query_n.reshape(nblocks, width, feat)
    head_of = jnp.arange(feat, dtype=jnp.int32) // (feat // count)
    query_stack = jnp.concatenate(
        [jnp.where(head_of[None, None, :] == h, query_blocks, 0) for h in range(count)], axis=1
    )
    own_kv = jnp.concatenate([key_n, value_b], axis=1).reshape(nblocks, width, 2 * feat)
    owners = nbr_owner.reshape(-1)
    owner_hot = (owners[:, None] == jnp.arange(devices, dtype=jnp.int32)[None, :]).astype(jnp.int32)
    rank = jnp.sum(jnp.cumsum(owner_hot, axis=0) * owner_hot, axis=1) - 1
    target = owners * capacity + rank
    place = (target[:, None] == jnp.arange(tile_count, dtype=jnp.int32)[None, :]).astype(jnp.int32)
    valid = (slot_valid.reshape(-1) > 0).astype(jnp.int32)
    wanted = jnp.where(valid > 0, nbr_local.reshape(-1), -1)
    request = jnp.sum(place * (wanted[:, None] + 1), axis=0) - 1
    asked = lax.all_to_all(
        request.reshape(devices, capacity), "nodes", split_axis=0, concat_axis=0, tiled=True
    ).reshape(-1)
    heads = lax.axis_size("heads")
    me = lax.axis_index("heads")
    quarter = width // heads
    model = feats.shape[1]
    feats_parts = feats.reshape(nblocks * heads, quarter, model)
    pick = jnp.clip(asked, 0, nblocks - 1).astype(jnp.int32) * heads + me
    payload = gather_blocks(feats_parts, pick)
    w_out, w_key_b, w_value_b, payload = lax.optimization_barrier((w_out, w_key, w_value, payload))
    w_out_t = lax.all_gather(w_out.T, "heads", axis=1, tiled=True)
    w_key_all = lax.all_gather(w_key_b, "heads", axis=1, tiled=True).reshape(model, heads, feat)
    w_value_all = lax.all_gather(w_value_b, "heads", axis=1, tiled=True).reshape(model, heads, feat)
    w_kv_all = jnp.stack([w_key_all, w_value_all], axis=2).reshape(model, heads * 2 * feat)
    recv = lax.all_to_all(
        payload.reshape(devices, capacity * quarter, model),
        "nodes",
        split_axis=0,
        concat_axis=0,
        tiled=True,
    ).reshape(tile_count, quarter, model)
    recv, w_out_t, w_kv_all = lax.optimization_barrier((recv, w_out_t, w_kv_all))
    slot_of = jnp.clip(target, 0, tile_count - 1).astype(jnp.int32)
    pairs = slot_of.shape[0]
    send = project_all(recv, slot_of, w_kv_all, heads, feat // count).reshape(
        heads, pairs, quarter, 2 * feat
    )
    me_plane = lax.axis_index("heads")
    received = [lax.dynamic_index_in_dim(send, me_plane, 0, keepdims=False)]
    for k in range(1, heads):
        outgoing = lax.dynamic_index_in_dim(send, (me_plane + k) % heads, 0, keepdims=False)
        received.append(
            lax.ppermute(outgoing, "heads", [(j, (j + k) % heads) for j in range(heads)])
        )
    got = jnp.stack(received, axis=0)
    pair_kv = got
    pair_ids = jnp.arange(pairs, dtype=jnp.int32)
    heads_n = lax.axis_size("heads")
    me_h = lax.axis_index("heads")

    def out_part(piece, source):
        w_part = lax.dynamic_slice(w_out_t, (me_h * feat, source * feat), (feat, feat))
        return lax.dot_general(
            piece, w_part, (((1,), (1,)), ((), ())), preferred_element_type=jnp.float32
        )

    halves = 2
    per_half = nblocks // halves
    outs = []
    for part in range(halves):
        lo, hi = part * per_half, (part + 1) * per_half
        attn_half = attend(
            query_stack[lo:hi],
            own_kv[lo:hi],
            pair_kv,
            pair_ids[lo * slots:hi * slots],
            valid[lo * slots:hi * slots],
            head_scale,
        ).reshape(per_half * width, feat)
        mixed = out_part(attn_half, me_h)
        for k in range(1, heads_n):
            piece = lax.ppermute(attn_half, "heads", [(j, (j + k) % heads_n) for j in range(heads_n)])
            mixed = mixed + out_part(piece, (me_h - k) % heads_n)
        outs.append(mixed.astype(jnp.bfloat16))
    return jnp.concatenate(outs, axis=0)


def solution(mesh):
    placed = (
        P("nodes", None),
        P(None, "heads"),
        P(None, "heads"),
        P(None, "heads"),
        P("heads", None),
        P("heads"),
        P("nodes", None),
        P("nodes", None),
        P("nodes", None),
    )
    return jax.shard_map(
        body, mesh=mesh, in_specs=placed, out_specs=P("nodes", "heads"), check_vma=False
    )
```

```python
import functools

import jax
import jax.numpy as jnp
from jax import lax
from jax.experimental import pallas as pl
from jax.experimental.pallas import tpu as pltpu
from jax.sharding import PartitionSpec as P


def unit_rows(values, count):
    shaped = values.reshape(values.shape[0], count, -1)
    total = jnp.sum(shaped * shaped, axis=-1, keepdims=True)
    return (shaped * lax.rsqrt(total + 1e-06)).astype(jnp.bfloat16).reshape(values.shape)


def attend_kernel(slot_ref, live_ref, scale_ref, q_ref, own_ref, recv_ref, out_ref, buf, sems, *, count, slots):
    b = pl.program_id(0)
    pairs = buf.shape[0]
    stacked, feat = q_ref.shape[1], q_ref.shape[2]
    width = stacked // count
    hd = feat // count

    def pair_copy(p):
        return pltpu.make_async_copy(recv_ref.at[:, slot_ref[p]], buf.at[p], sems.at[p])

    @pl.when(b == 0)
    def _():
        for p in range(pairs):
            pair_copy(p).start()

    for s in range(slots):
        pair_copy(b * slots + s).wait()
    lane_head = lax.broadcasted_iota(jnp.int32, (width, feat), 1) // hd
    stack_rows = lax.broadcasted_iota(jnp.int32, (stacked, 1), 0)
    scale_col = jnp.zeros((stacked, 1), jnp.float32)
    for h in range(count):
        inside = (stack_rows >= h * width) & (stack_rows < (h + 1) * width)
        scale_col = jnp.where(inside, scale_ref[h], scale_col)
    key_lanes = lax.broadcasted_iota(jnp.int32, (1, (slots + 1) * width), 1)
    live_row = jnp.ones((1, (slots + 1) * width), jnp.float32)
    for s in range(slots):
        inside = (key_lanes >= (s + 1) * width) & (key_lanes < (s + 2) * width)
        live_row = jnp.where(inside, live_ref[b * slots + s].astype(jnp.float32), live_row)
    blocks = [own_ref[b]] + [buf[b * slots + s].reshape(width, 2 * feat) for s in range(slots)]
    keys = jnp.concatenate([blk[:, :feat] for blk in blocks], axis=0)
    values = jnp.concatenate([blk[:, feat:] for blk in blocks], axis=0)
    s_all = lax.dot_general(
        q_ref[0], keys, (((1,), (1,)), ((), ())), preferred_element_type=jnp.float32
    )
    w = jnp.exp(scale_col * (s_all - 1.0)) * live_row
    den = jnp.sum(w, axis=1, keepdims=True)
    w_b = w.astype(jnp.bfloat16)
    num = jnp.zeros((width, feat), jnp.float32)
    den_full = jnp.zeros((width, feat), jnp.float32)
    for h in range(count):
        part = jnp.dot(w_b[h * width:(h + 1) * width], values, preferred_element_type=jnp.float32)
        num = jnp.where(lane_head == h, part, num)
        den_full = jnp.where(lane_head == h, den[h * width:(h + 1) * width], den_full)
    out_ref[0] = (num / den_full).astype(out_ref.dtype)


def attend(query_stack, own_kv, recv_kv, slot_of, live, scales):
    nblocks, stacked, feat = query_stack.shape
    count = scales.shape[0]
    width = stacked // count
    slots = slot_of.shape[0] // nblocks
    grid_spec = pltpu.PrefetchScalarGridSpec(
        num_scalar_prefetch=2,
        grid=(nblocks,),
        in_specs=[
            pl.BlockSpec(memory_space=pltpu.SMEM),
            pl.BlockSpec((1, stacked, feat), lambda b, slot_of, live: (b, 0, 0)),
            pl.BlockSpec((nblocks, width, 2 * feat), lambda b, slot_of, live: (0, 0, 0)),
            pl.BlockSpec(memory_space=pl.ANY),
        ],
        out_specs=pl.BlockSpec((1, width, feat), lambda b, slot_of, live: (b, 0, 0)),
        scratch_shapes=[
            pltpu.VMEM((nblocks * slots,) + recv_kv.shape[:1] + recv_kv.shape[2:], recv_kv.dtype),
            pltpu.SemaphoreType.DMA((nblocks * slots,)),
        ],
    )
    return pl.pallas_call(
        functools.partial(attend_kernel, count=count, slots=slots),
        grid_spec=grid_spec,
        out_shape=jax.ShapeDtypeStruct((nblocks, width, feat), jnp.bfloat16),
        compiler_params=pltpu.CompilerParams(vmem_limit_bytes=48 * 1024 * 1024),
    )(slot_of, live, scales, query_stack, own_kv, recv_kv)


def gather_kernel(pick_ref, src_ref, out_ref):
    g = pl.program_id(0)
    group = out_ref.shape[0]
    for i in range(group):
        out_ref[i] = src_ref[pick_ref[g * group + i]]


def gather_blocks(blocks, pick):
    nblocks, r, l = blocks.shape
    tiles = pick.shape[0]
    group = 128
    grid_spec = pltpu.PrefetchScalarGridSpec(
        num_scalar_prefetch=1,
        grid=(tiles // group,),
        in_specs=[pl.BlockSpec((nblocks, r, l), lambda g, pick: (0, 0, 0))],
        out_specs=pl.BlockSpec((group, r, l), lambda g, pick: (g, 0, 0)),
    )
    return pl.pallas_call(
        gather_kernel,
        grid_spec=grid_spec,
        out_shape=jax.ShapeDtypeStruct((tiles, r, l), blocks.dtype),
    )(pick, blocks)


def project_kernel(slot_ref, recv_ref, w_ref, out_ref, rows_scr, sems, *, hd):
    y = pl.program_id(0)
    pairs = sems.shape[0]
    quarter = recv_ref.shape[1]

    def piece_copy(p):
        return pltpu.make_async_copy(
            recv_ref.at[slot_ref[p]], rows_scr.at[pl.ds(p * quarter, quarter)], sems.at[p]
        )

    @pl.when(y == 0)
    def _():
        for p in range(pairs):
            piece_copy(p).start()
        for p in range(pairs):
            piece_copy(p).wait()

    kv = jnp.dot(rows_scr[...], w_ref[...], preferred_element_type=jnp.float32)
    feat = kv.shape[1] // 2
    keys = kv[:, :feat]
    lane = lax.broadcasted_iota(jnp.int32, (1, feat), 1)
    sq = keys * keys
    scale = jnp.zeros(keys.shape, jnp.float32)
    for h in range(feat // hd):
        inside = (lane >= h * hd) & (lane < (h + 1) * hd)
        total = jnp.sum(jnp.where(inside, sq, 0.0), axis=1, keepdims=True)
        scale = jnp.where(inside, lax.rsqrt(total + 1e-06), scale)
    out_ref[0, :, :feat] = (keys * scale).astype(out_ref.dtype)
    out_ref[0, :, feat:] = kv[:, feat:].astype(out_ref.dtype)


def project_all(recv, slot_of, w_kv, heads, hd):
    tiles, quarter, model = recv.shape
    pairs = slot_of.shape[0]
    n = pairs * quarter
    cols = w_kv.shape[1] // heads
    grid_spec = pltpu.PrefetchScalarGridSpec(
        num_scalar_prefetch=1,
        grid=(heads,),
        in_specs=[
            pl.BlockSpec(memory_space=pl.ANY),
            pl.BlockSpec((model, cols), lambda y, slot_of: (0, y)),
        ],
        out_specs=pl.BlockSpec((1, n, cols), lambda y, slot_of: (y, 0, 0)),
        scratch_shapes=[
            pltpu.VMEM((n, model), recv.dtype),
            pltpu.SemaphoreType.DMA((pairs,)),
        ],
    )
    return pl.pallas_call(
        functools.partial(project_kernel, hd=hd),
        grid_spec=grid_spec,
        out_shape=jax.ShapeDtypeStruct((heads, n, cols), jnp.bfloat16),
    )(slot_of, recv, w_kv)


def body(feats, w_query, w_key, w_value, w_out, head_scale, nbr_owner, nbr_local, slot_valid):
    rows = feats.shape[0]
    feat = w_query.shape[1]
    count = head_scale.shape[0]
    nblocks, slots = nbr_owner.shape
    width = rows // nblocks
    devices = lax.axis_size("nodes")
    capacity = max(2, min(nblocks // 2, 3 * nblocks * slots // (2 * devices)))
    tile_count = devices * capacity
    query_n = unit_rows(jnp.dot(feats, w_query, preferred_element_type=jnp.float32), count)
    key_n = unit_rows(jnp.dot(feats, w_key, preferred_element_type=jnp.float32), count)
    value_b = jnp.dot(feats, w_value, preferred_element_type=jnp.float32).astype(jnp.bfloat16)
    query_blocks = query_n.reshape(nblocks, width, feat)
    head_of = jnp.arange(feat, dtype=jnp.int32) // (feat // count)
    query_stack = jnp.concatenate(
        [jnp.where(head_of[None, None, :] == h, query_blocks, 0) for h in range(count)], axis=1
    )
    own_kv = jnp.concatenate([key_n, value_b], axis=1).reshape(nblocks, width, 2 * feat)
    owners = nbr_owner.reshape(-1)
    owner_hot = (owners[:, None] == jnp.arange(devices, dtype=jnp.int32)[None, :]).astype(jnp.int32)
    rank = jnp.sum(jnp.cumsum(owner_hot, axis=0) * owner_hot, axis=1) - 1
    target = owners * capacity + rank
    place = (target[:, None] == jnp.arange(tile_count, dtype=jnp.int32)[None, :]).astype(jnp.int32)
    valid = (slot_valid.reshape(-1) > 0).astype(jnp.int32)
    wanted = jnp.where(valid > 0, nbr_local.reshape(-1), -1)
    request = jnp.sum(place * (wanted[:, None] + 1), axis=0) - 1
    asked = lax.all_to_all(
        request.reshape(devices, capacity), "nodes", split_axis=0, concat_axis=0, tiled=True
    ).reshape(-1)
    heads = lax.axis_size("heads")
    me = lax.axis_index("heads")
    quarter = width // heads
    model = feats.shape[1]
    feats_parts = feats.reshape(nblocks * heads, quarter, model)
    pick = jnp.clip(asked, 0, nblocks - 1).astype(jnp.int32) * heads + me
    payload = gather_blocks(feats_parts, pick)
    w_out, w_key_b, w_value_b, payload = lax.optimization_barrier((w_out, w_key, w_value, payload))
    w_out_t = lax.all_gather(w_out.T, "heads", axis=1, tiled=True)
    w_key_all = lax.all_gather(w_key_b, "heads", axis=1, tiled=True).reshape(model, heads, feat)
    w_value_all = lax.all_gather(w_value_b, "heads", axis=1, tiled=True).reshape(model, heads, feat)
    w_kv_all = jnp.stack([w_key_all, w_value_all], axis=2).reshape(model, heads * 2 * feat)
    recv = lax.all_to_all(
        payload.reshape(devices, capacity * quarter, model),
        "nodes",
        split_axis=0,
        concat_axis=0,
        tiled=True,
    ).reshape(tile_count, quarter, model)
    recv, w_out_t, w_kv_all = lax.optimization_barrier((recv, w_out_t, w_kv_all))
    slot_of = jnp.clip(target, 0, tile_count - 1).astype(jnp.int32)
    pairs = slot_of.shape[0]
    send = project_all(recv, slot_of, w_kv_all, heads, feat // count).reshape(
        heads, pairs, quarter, 2 * feat
    )
    got = lax.all_to_all(send, "heads", 0, 0, tiled=True)
    pair_kv = got
    pair_ids = jnp.arange(pairs, dtype=jnp.int32)
    heads_n = lax.axis_size("heads")
    me_h = lax.axis_index("heads")

    def out_part(piece, source):
        w_part = lax.dynamic_slice(w_out_t, (me_h * feat, source * feat), (feat, feat))
        return lax.dot_general(
            piece, w_part, (((1,), (1,)), ((), ())), preferred_element_type=jnp.float32
        )

    first = (nblocks * 5) // 8
    outs = []
    for lo, hi in ((0, first), (first, nblocks)):
        per_half = hi - lo
        attn_half = attend(
            query_stack[lo:hi],
            own_kv[lo:hi],
            pair_kv,
            pair_ids[lo * slots:hi * slots],
            valid[lo * slots:hi * slots],
            head_scale,
        ).reshape(per_half * width, feat)
        mixed = out_part(attn_half, me_h)
        for k in range(1, heads_n):
            piece = lax.ppermute(attn_half, "heads", [(j, (j + k) % heads_n) for j in range(heads_n)])
            mixed = mixed + out_part(piece, (me_h - k) % heads_n)
        outs.append(mixed.astype(jnp.bfloat16))
    return jnp.concatenate(outs, axis=0)


def solution(mesh):
    placed = (
        P("nodes", None),
        P(None, "heads"),
        P(None, "heads"),
        P(None, "heads"),
        P("heads", None),
        P("heads"),
        P("nodes", None),
        P("nodes", None),
        P("nodes", None),
    )
    return jax.shard_map(
        body, mesh=mesh, in_specs=placed, out_specs=P("nodes", "heads"), check_vma=False
    )
```
